128 devices in a mesh: dom: 128 (over x, z, y, core).
Axes of the slice: x: 4, y: 4, z: 4, core: 2. Of those that a mesh axis runs over, the one named last changes fastest.
Arguments:
- loads: float32 [4, 3, 8192, 2, 128], P(None, None, 'dom'), may hold values from -6 to 6
- modal_disp: float32 [4, 3, 8192, 2, 128], P(None, None, 'dom'), may hold values from -6 to 6
- material: int32 [8192, 2, 128], P('dom'), may hold values from 0 to 7
- moduli: float32 [8], replicated, may hold values from 0.05 to 0.4
- part_device: int32 [128], replicated, may hold values from 0 to 127, as said below
- partners: int32 [2, 128], replicated, may hold values from 0 to 127, as said below
- low_bound: float32 [1], replicated, may hold values from 0.02 to 0.3
- high_bound: float32 [1], replicated, may hold values from 1.5 to 2.5
Outputs:
- displacement: float32 [4, 3, 8192, 2, 128], P(None, None, 'dom')
- residual: float32 [4, 3, 8192, 2, 128], P(None, None, 'dom')
The draws below stay inside these ranges and needn't reach their ends.
Inputs may be any that keep to these rules, and one draw needn't show every extreme that they name: `part_device`: each device is named once. `partners`: round 0 pairs the devices of partitions 2i and 2i+1, round 1 those of partitions 2i+1 and 2i+2, partitions as given by part_device; a device without a partner in a round is its own partner.
All inputs are finite; a program needn't handle non-finite values.
Results may differ from the reference program's by a relative error of at most 0.00002.
Values sent between devices are 32-bit elements; how exact they have to be, the bound alone decides.
No kernel may reach another device: no remote copies, remote signals or barrier semaphores. Data moves between devices by JAX's collectives and lax.ppermute only.
A program may use at most 128 MiB of HBM per device.

```python
import math
import jax
import jax.numpy as jnp
from jax import lax

CX = 64
NY = 2
NZ = 128
SAMPLES = 4
MATERIALS = 8
NX = 8192
N_DOM = 128


def shared_order(key):
    return jax.random.permutation(jax.random.fold_in(key, 11), N_DOM).astype(jnp.int32)


def draw_part_device(key, part):
    return shared_order(key)


def draw_partners(key, part):
    order = shared_order(key)
    ids = jnp.arange(N_DOM, dtype=jnp.int32)
    place = jnp.zeros((N_DOM,), jnp.int32).at[order].set(ids)
    rounds_out = []
    for which in (0, 1):
        upper = place % 2 == which
        mate = jnp.where(upper, place + 1, place - 1)
        inside = (mate >= 0) & (mate < N_DOM)
        mate_dev = order[jnp.clip(mate, 0, N_DOM - 1)]
        rounds_out.append(jnp.where(inside, mate_dev, ids))
    return jnp.stack(rounds_out, axis=0).astype(jnp.int32)


def plant(values, stream_key, smallest, high):
    extent = values.shape
    spot = [jax.random.randint(jax.random.fold_in(stream_key, axis), (), 0, extent[axis]) for axis in range(len(extent))]
    values = values.at[tuple(spot)].set(smallest)
    longest = extent.index(max(extent))
    spot[longest] = (spot[longest] + 1) % extent[longest]
    return values.at[tuple(spot)].set(high)


def level_of(own_key, shape, shards, least, high):
    def one(dim, shards_of):
        draws = jax.random.uniform(jax.random.fold_in(jax.random.fold_in(own_key, 6), dim), (shards_of,), jnp.float32, least / len(shards), high / len(shards))
        return jnp.repeat(jnp.exp(draws), shape[dim] // shards_of).reshape((-1,) + (1,) * (len(shape) - dim - 1))

    level = one(*shards[0])
    for cut in shards[1:]:
        level = level * one(*cut)
    return level


def gaussian(key, dims, scale, limit, cuts=(), kind=jnp.bfloat16):
    values = jax.random.normal(key, dims, jnp.float32) * scale
    if len(cuts) > 0:
        values = level_of(key, dims, cuts, -0.22, 0.18) * values
    return jnp.clip(values, min=-limit, max=limit).astype(kind)


def setup_inputs(seed: int = 0) -> dict:
    key_of = jax.random.split(jax.random.key(seed), 9)
    loads = gaussian(key_of[0], (SAMPLES, 3, NX, NY, NZ), 1.0, 6.0, ((2, 128),), jnp.float32)
    modal_disp = gaussian(key_of[1], (SAMPLES, 3, NX, NY, NZ), 1.0, 6.0, ((2, 128),), jnp.float32)
    material = plant(jax.random.randint(key_of[2], (NX, NY, NZ), 0, MATERIALS), jax.random.fold_in(key_of[2], 1), 0, MATERIALS - 1).astype(jnp.int32)
    moduli = jnp.clip(jnp.exp(jax.random.uniform(key_of[3], (MATERIALS,), jnp.float32, math.log(0.05), math.log(0.4))), 0.05, 0.4)
    part_device = draw_part_device(jax.random.fold_in(key_of[8], 71), 0)
    partners = draw_partners(jax.random.fold_in(key_of[8], 71), 0)
    low_bound = jnp.clip(jax.random.uniform(key_of[6], (1,), jnp.float32, 0.02, 0.3), 0.02, 0.3)
    high_bound = jnp.clip(jax.random.uniform(key_of[7], (1,), jnp.float32, 1.5, 2.5), 1.5, 2.5)
    return dict(loads=loads, modal_disp=modal_disp, material=material, moduli=moduli, part_device=part_device, partners=partners, low_bound=low_bound, high_bound=high_bound)


GAMMA = 0.2
BETA = 0.5
EDGE_WEIGHTS = (0.0, 1.0, 0.5, 0.25)
OFFSETS = [(a, b, c) for a in (-1, 0, 1) for b in (-1, 0, 1) for c in (-1, 0, 1) if (a, b, c) != (0, 0, 0)]


def shift_cells(array, axis, step):
    if step == 0:
        return array
    length = array.shape[axis]
    zero = jnp.zeros_like(lax.slice_in_dim(array, 0, 1, axis=axis))
    if step > 0:
        return jnp.concatenate([lax.slice_in_dim(array, 1, length, axis=axis), zero], axis=axis)
    return jnp.concatenate([zero, lax.slice_in_dim(array, 0, length - 1, axis=axis)], axis=axis)


def neighbour(extended, off_x, off_y, off_z, depth):
    rank_all = extended.ndim
    rows = lax.slice_in_dim(extended, 1 + off_x, 1 + off_x + depth, axis=rank_all - 3)
    return shift_cells(shift_cells(rows, rank_all - 2, off_y), rank_all - 1, off_z)


def diagonal_of(mod_ext, depth):
    centre = neighbour(mod_ext, 0, 0, 0, depth)
    comps = [GAMMA * centre, GAMMA * centre, GAMMA * centre]
    for offset in OFFSETS:
        norm_sq = offset[0] * offset[0] + offset[1] * offset[1] + offset[2] * offset[2]
        edge = EDGE_WEIGHTS[norm_sq] * 0.5 * (centre + neighbour(mod_ext, offset[0], offset[1], offset[2], depth))
        for comp in range(3):
            comps[comp] = comps[comp] + edge * (1.0 + BETA * offset[comp] * offset[comp] / norm_sq)
    return jnp.stack(comps, axis=0)


def stiffness(field_ext, mod_ext, depth):
    centre_mod = neighbour(mod_ext, 0, 0, 0, depth)
    centre = neighbour(field_ext, 0, 0, 0, depth)
    comps = [GAMMA * centre_mod * centre[:, comp] for comp in range(3)]
    for offset in OFFSETS:
        norm_sq = offset[0] * offset[0] + offset[1] * offset[1] + offset[2] * offset[2]
        edge = EDGE_WEIGHTS[norm_sq] * 0.5 * (centre_mod + neighbour(mod_ext, offset[0], offset[1], offset[2], depth))
        delta = centre - neighbour(field_ext, offset[0], offset[1], offset[2], depth)
        project = None
        for comp in range(3):
            if offset[comp] != 0:
                term = offset[comp] * delta[:, comp]
                project = term if project is None else project + term
        project = project / norm_sq
        for comp in range(3):
            if offset[comp] != 0:
                comps[comp] = comps[comp] + edge * (delta[:, comp] + BETA * offset[comp] * project)
            else:
                comps[comp] = comps[comp] + edge * delta[:, comp]
    return jnp.stack(comps, axis=1)


def lookup_modulus(material, moduli):
    modulus = jnp.zeros(material.shape, jnp.float32)
    for index in range(MATERIALS):
        modulus = modulus + jnp.where(material == index, moduli[index], jnp.float32(0.0))
    return modulus


def reference(loads, modal_disp, material, moduli, part_device, partners, low_bound, high_bound):
    count = part_device.shape[0]
    ids = jnp.arange(count, dtype=jnp.int32)
    place = jnp.zeros((count,), jnp.int32).at[part_device].set(ids)
    up_dev = partners[place % 2, ids]
    low_dev = partners[1 - place % 2, ids]
    up_on = (up_dev != ids).astype(jnp.float32)[:, None, None]
    low_on = (low_dev != ids).astype(jnp.float32)[:, None, None]

    def extend(array):
        lead = array.shape[:-3]
        blocks = array.reshape(lead + (count, CX, NY, NZ))
        first = blocks[..., 0, :, :]
        last = blocks[..., CX - 1, :, :]
        below = jnp.take(last, low_dev, axis=-3) * low_on
        above = jnp.take(first, up_dev, axis=-3) * up_on
        return jnp.concatenate([below[..., None, :, :], blocks, above[..., None, :, :]], axis=-3)

    modulus = lookup_modulus(material, moduli)
    mod_ext = extend(modulus)
    jacobi = diagonal_of(mod_ext, CX).reshape((3, NX, NY, NZ))

    def apply(field):
        field_ext = jnp.moveaxis(extend(field), 2, 0)

        def one_block(pair):
            return stiffness(pair[0], pair[1], CX)

        out = lax.map(one_block, (field_ext, mod_ext))
        return jnp.moveaxis(out, 0, 2).reshape(field.shape)

    theta = (high_bound[0] + low_bound[0]) / 2.0
    half = (high_bound[0] - low_bound[0]) / 2.0
    sigma = theta / half
    rho0 = 1.0 / sigma
    rho1 = 1.0 / (2.0 * sigma - rho0)
    start = loads - apply(modal_disp)
    step0 = start / (theta * jacobi)
    residual1 = start - apply(step0)
    step1 = rho1 * rho0 * step0 + (2.0 * rho1 / half) * residual1 / jacobi
    displacement = (modal_disp + step0) + step1
    residual = residual1 - apply(step1)
    return displacement, residual
```

```python
import jax
import jax.numpy as jnp
from jax import lax
from jax.sharding import Mesh, PartitionSpec as P

MATERIALS = 8


GAMMA = 0.2
BETA = 0.5
EDGE_WEIGHTS = (0.0, 1.0, 0.5, 0.25)
OFFSETS = [
    (a, b, c) for a in (-1, 0, 1) for b in (-1, 0, 1) for c in (-1, 0, 1) if (a, b, c) != (0, 0, 0)
]


def shift_cells(array, axis, step):
    if step == 0:
        return array
    length = array.shape[axis]
    zero = jnp.zeros_like(lax.slice_in_dim(array, 0, 1, axis=axis))
    if step > 0:
        return jnp.concatenate([lax.slice_in_dim(array, 1, length, axis=axis), zero], axis=axis)
    return jnp.concatenate([zero, lax.slice_in_dim(array, 0, length - 1, axis=axis)], axis=axis)


def neighbour(extended, off_x, off_y, off_z, depth):
    rank_all = extended.ndim
    rows = lax.slice_in_dim(extended, 1 + off_x, 1 + off_x + depth, axis=rank_all - 3)
    return shift_cells(shift_cells(rows, rank_all - 2, off_y), rank_all - 1, off_z)


def diagonal_of(mod_ext, depth):
    centre = neighbour(mod_ext, 0, 0, 0, depth)
    comps = [GAMMA * centre, GAMMA * centre, GAMMA * centre]
    for offset in OFFSETS:
        norm_sq = offset[0] * offset[0] + offset[1] * offset[1] + offset[2] * offset[2]
        edge = (
            EDGE_WEIGHTS[norm_sq]
            * 0.5
            * (centre + neighbour(mod_ext, offset[0], offset[1], offset[2], depth))
        )
        for comp in range(3):
            comps[comp] = comps[comp] + edge * (1.0 + BETA * offset[comp] * offset[comp] / norm_sq)
    return jnp.stack(comps, axis=0)


def stiffness(field_ext, mod_ext, depth):
    centre_mod = neighbour(mod_ext, 0, 0, 0, depth)
    centre = neighbour(field_ext, 0, 0, 0, depth)
    comps = [GAMMA * centre_mod * centre[:, comp] for comp in range(3)]
    for offset in OFFSETS:
        norm_sq = offset[0] * offset[0] + offset[1] * offset[1] + offset[2] * offset[2]
        edge = (
            EDGE_WEIGHTS[norm_sq]
            * 0.5
            * (centre_mod + neighbour(mod_ext, offset[0], offset[1], offset[2], depth))
        )
        delta = centre - neighbour(field_ext, offset[0], offset[1], offset[2], depth)
        project = None
        for comp in range(3):
            if offset[comp] != 0:
                term = offset[comp] * delta[:, comp]
                project = term if project is None else project + term
        project = project / norm_sq
        for comp in range(3):
            if offset[comp] != 0:
                comps[comp] = comps[comp] + edge * (delta[:, comp] + BETA * offset[comp] * project)
            else:
                comps[comp] = comps[comp] + edge * delta[:, comp]
    return jnp.stack(comps, axis=1)


def lookup_modulus(material, moduli):
    modulus = jnp.zeros(material.shape, jnp.float32)
    for index in range(MATERIALS):
        modulus = modulus + jnp.where(material == index, moduli[index], jnp.float32(0.0))
    return modulus


GROUP = 8


def neighbour_devices(part_device, partners):
    count = part_device.shape[0]
    ids = jnp.arange(count, dtype=jnp.int32)
    place = jnp.zeros((count,), jnp.int32).at[part_device].set(ids)
    parity = place % 2
    up_dev = partners[parity, ids]
    low_dev = partners[1 - parity, ids]
    return up_dev, low_dev


def exchange(first, last, up_dev, low_dev):
    col = lax.axis_index("col")
    grp = lax.axis_index("grp")
    me = col * GROUP + grp
    cols = up_dev.shape[0] // GROUP
    pack = jnp.stack([first, last], axis=0)[None]
    held = lax.all_gather(pack, "grp", axis=0, tiled=True)
    targets = jnp.arange(cols, dtype=jnp.int32) * GROUP + grp
    t_up = up_dev[targets]
    t_low = low_dev[targets]
    up_here = (t_up // GROUP) == col
    low_here = (t_low // GROUP) == col
    from_up = held[t_up % GROUP, 0]
    from_low = held[t_low % GROUP, 1]
    shape = (cols,) + (1,) * (from_up.ndim - 1)
    from_up = jnp.where(up_here.reshape(shape), from_up, jnp.float32(0.0))
    from_low = jnp.where(low_here.reshape(shape), from_low, jnp.float32(0.0))
    slots = jnp.stack([from_up, from_low], axis=1)
    got = lax.all_to_all(slots, "col", 0, 0, tiled=True)
    my_up = up_dev[me]
    my_low = low_dev[me]
    above = got[my_up // GROUP, 0]
    below = got[my_low // GROUP, 1]
    above = jnp.where(my_up != me, above, jnp.float32(0.0))
    below = jnp.where(my_low != me, below, jnp.float32(0.0))
    return below, above


def on_device(loads, modal_disp, material, moduli, part_device, partners, low_bound, high_bound):
    up_dev, low_dev = neighbour_devices(part_device, partners)
    depth = loads.shape[2]
    modulus = lookup_modulus(material, moduli)
    plane = loads.shape[:2] + loads.shape[3:]
    plane_size = 1
    for size in plane:
        plane_size *= size

    def ext_field(field, below, above):
        return jnp.concatenate([below[:, :, None], field, above[:, :, None]], axis=2)

    first = jnp.concatenate([modal_disp[:, :, 0].reshape(-1), modulus[0].reshape(-1)])
    last = jnp.concatenate([modal_disp[:, :, depth - 1].reshape(-1), modulus[depth - 1].reshape(-1)])
    below, above = exchange(first, last, up_dev, low_dev)
    below_mod = below[plane_size:].reshape(modulus.shape[1:])
    above_mod = above[plane_size:].reshape(modulus.shape[1:])
    mod_ext = jnp.concatenate([below_mod[None], modulus, above_mod[None]], axis=0)
    first_ext = ext_field(
        modal_disp, below[:plane_size].reshape(plane), above[:plane_size].reshape(plane)
    )
    jacobi = diagonal_of(mod_ext, depth)

    def apply(field):
        below, above = exchange(field[:, :, 0], field[:, :, depth - 1], up_dev, low_dev)
        return stiffness(ext_field(field, below, above), mod_ext, depth)

    theta = (high_bound[0] + low_bound[0]) / 2.0
    half = (high_bound[0] - low_bound[0]) / 2.0
    sigma = theta / half
    rho0 = 1.0 / sigma
    rho1 = 1.0 / (2.0 * sigma - rho0)
    start = loads - stiffness(first_ext, mod_ext, depth)
    step0 = start / (theta * jacobi)
    residual1 = start - apply(step0)
    step1 = rho1 * rho0 * step0 + 2.0 * rho1 / half * residual1 / jacobi
    displacement = modal_disp + step0 + step1
    residual = residual1 - apply(step1)
    return (displacement, residual)


def solution(mesh):
    devices = mesh.devices.reshape(-1)
    grid = Mesh(devices.reshape(devices.size // GROUP, GROUP), ("col", "grp"))
    slab = ("col", "grp")
    in_specs = (
        P(None, None, slab, None, None),
        P(None, None, slab, None, None),
        P(slab, None, None),
        P(),
        P(),
        P(),
        P(),
        P(),
    )
    out_specs = (P(None, None, slab, None, None), P(None, None, slab, None, None))
    return jax.shard_map(
        on_device, mesh=grid, in_specs=in_specs, out_specs=out_specs, check_vma=False
    )
```

```python
import jax
import jax.numpy as jnp
from jax import lax
from jax.sharding import Mesh, PartitionSpec as P

MATERIALS = 8
GROUP = 8

GAMMA = 0.2
BETA = 0.5
EDGE_WEIGHTS = (0.0, 1.0, 0.5, 0.25)
OFFSETS = [
    (a, b, c) for a in (-1, 0, 1) for b in (-1, 0, 1) for c in (-1, 0, 1) if (a, b, c) != (0, 0, 0)
]


def shift_lanes(array, step, width, off_z):
    if step == 0:
        return array
    length = array.shape[-1]
    zero = jnp.zeros(array.shape[:-1] + (abs(step),), array.dtype)
    if step > 0:
        moved = jnp.concatenate([array[..., step:], zero], axis=-1)
    else:
        moved = jnp.concatenate([zero, array[..., : length + step]], axis=-1)
    if off_z == 0:
        return moved
    z = lax.broadcasted_iota(jnp.int32, (length,), 0) % width
    inside = (z + off_z >= 0) & (z + off_z < width)
    return jnp.where(inside, moved, jnp.float32(0.0))


def neighbour(extended, off_x, off_y, off_z, depth, width):
    rows = lax.slice_in_dim(extended, 1 + off_x, 1 + off_x + depth, axis=extended.ndim - 2)
    return shift_lanes(rows, off_y * width + off_z, width, off_z)


def edges_of(mod_ext, depth, width):
    centre = neighbour(mod_ext, 0, 0, 0, depth, width)
    edges = []
    for offset in OFFSETS:
        norm_sq = offset[0] * offset[0] + offset[1] * offset[1] + offset[2] * offset[2]
        edges.append(
            EDGE_WEIGHTS[norm_sq]
            * 0.5
            * (centre + neighbour(mod_ext, offset[0], offset[1], offset[2], depth, width))
        )
    return centre, edges


def diagonal_of(centre, edges):
    comps = [GAMMA * centre, GAMMA * centre, GAMMA * centre]
    for offset, edge in zip(OFFSETS, edges):
        norm_sq = offset[0] * offset[0] + offset[1] * offset[1] + offset[2] * offset[2]
        for comp in range(3):
            comps[comp] = comps[comp] + edge * (1.0 + BETA * offset[comp] * offset[comp] / norm_sq)
    return jnp.stack(comps, axis=0)


def stiffness(field_ext, centre_mod, edges, depth, width):
    centre = neighbour(field_ext, 0, 0, 0, depth, width)
    comps = [GAMMA * centre_mod * centre[:, comp] for comp in range(3)]
    for offset, edge in zip(OFFSETS, edges):
        norm_sq = offset[0] * offset[0] + offset[1] * offset[1] + offset[2] * offset[2]
        delta = centre - neighbour(field_ext, offset[0], offset[1], offset[2], depth, width)
        project = None
        for comp in range(3):
            if offset[comp] != 0:
                term = offset[comp] * delta[:, comp]
                project = term if project is None else project + term
        project = project / norm_sq
        for comp in range(3):
            if offset[comp] != 0:
                comps[comp] = comps[comp] + edge * (delta[:, comp] + BETA * offset[comp] * project)
            else:
                comps[comp] = comps[comp] + edge * delta[:, comp]
    return jnp.stack(comps, axis=1)


def lookup_modulus(material, moduli):
    modulus = jnp.zeros(material.shape, jnp.float32)
    for index in range(MATERIALS):
        modulus = modulus + jnp.where(material == index, moduli[index], jnp.float32(0.0))
    return modulus


def neighbour_devices(part_device, partners):
    count = part_device.shape[0]
    ids = jnp.arange(count, dtype=jnp.int32)
    place = jnp.zeros((count,), jnp.int32).at[part_device].set(ids)
    parity = place % 2
    up_dev = partners[parity, ids]
    low_dev = partners[1 - parity, ids]
    return up_dev, low_dev


def exchange(first, last, up_dev, low_dev):
    col = lax.axis_index("col")
    grp = lax.axis_index("grp")
    me = col * GROUP + grp
    cols = up_dev.shape[0] // GROUP
    pack = jnp.stack([first, last], axis=0)[None]
    held = lax.all_gather(pack, "grp", axis=0, tiled=True)
    targets = jnp.arange(cols, dtype=jnp.int32) * GROUP + grp
    t_up = up_dev[targets]
    t_low = low_dev[targets]
    up_here = (t_up // GROUP) == col
    low_here = (t_low // GROUP) == col
    from_up = held[t_up % GROUP, 0]
    from_low = held[t_low % GROUP, 1]
    shape = (cols,) + (1,) * (from_up.ndim - 1)
    from_up = jnp.where(up_here.reshape(shape), from_up, jnp.float32(0.0))
    from_low = jnp.where(low_here.reshape(shape), from_low, jnp.float32(0.0))
    slots = jnp.stack([from_up, from_low], axis=1)
    got = lax.all_to_all(slots, "col", 0, 0, tiled=True)
    my_up = up_dev[me]
    my_low = low_dev[me]
    above = got[my_up // GROUP, 0]
    below = got[my_low // GROUP, 1]
    above = jnp.where(my_up != me, above, jnp.float32(0.0))
    below = jnp.where(my_low != me, below, jnp.float32(0.0))
    return below, above


def on_device(loads, modal_disp, material, moduli, part_device, partners, low_bound, high_bound):
    up_dev, low_dev = neighbour_devices(part_device, partners)
    samples, _, depth, rows_y, width = loads.shape
    lanes = rows_y * width
    flat = (samples, 3, depth, lanes)
    loads = loads.reshape(flat)
    modal_disp = modal_disp.reshape(flat)
    modulus = lookup_modulus(material, moduli).reshape(depth, lanes)
    plane_size = samples * 3 * lanes

    def ext_field(field, below, above):
        return jnp.concatenate([below[:, :, None], field, above[:, :, None]], axis=2)

    first = jnp.concatenate([modal_disp[:, :, 0].reshape(-1), modulus[0]])
    last = jnp.concatenate([modal_disp[:, :, depth - 1].reshape(-1), modulus[depth - 1]])
    below, above = exchange(first, last, up_dev, low_dev)
    mod_ext = jnp.concatenate([below[None, plane_size:], modulus, above[None, plane_size:]], axis=0)
    first_ext = ext_field(
        modal_disp,
        below[:plane_size].reshape(samples, 3, lanes),
        above[:plane_size].reshape(samples, 3, lanes),
    )
    centre_mod, edges = edges_of(mod_ext, depth, width)
    jacobi = diagonal_of(centre_mod, edges)

    def apply(field):
        below, above = exchange(field[:, :, 0], field[:, :, depth - 1], up_dev, low_dev)
        return stiffness(ext_field(field, below, above), centre_mod, edges, depth, width)

    theta = (high_bound[0] + low_bound[0]) / 2.0
    half = (high_bound[0] - low_bound[0]) / 2.0
    sigma = theta / half
    rho0 = 1.0 / sigma
    rho1 = 1.0 / (2.0 * sigma - rho0)
    start = loads - stiffness(first_ext, centre_mod, edges, depth, width)
    step0 = start / (theta * jacobi)
    residual1 = start - apply(step0)
    step1 = rho1 * rho0 * step0 + 2.0 * rho1 / half * residual1 / jacobi
    displacement = modal_disp + step0 + step1
    residual = residual1 - apply(step1)
    out_shape = (samples, 3, depth, rows_y, width)
    return (displacement.reshape(out_shape), residual.reshape(out_shape))


def solution(mesh):
    devices = mesh.devices.reshape(-1)
    grid = Mesh(devices.reshape(devices.size // GROUP, GROUP), ("col", "grp"))
    slab = ("col", "grp")
    in_specs = (
        P(None, None, slab, None, None),
        P(None, None, slab, None, None),
        P(slab, None, None),
        P(),
        P(),
        P(),
        P(),
        P(),
    )
    out_specs = (P(None, None, slab, None, None), P(None, None, slab, None, None))
    return jax.shard_map(
        on_device, mesh=grid, in_specs=in_specs, out_specs=out_specs, check_vma=False
    )
```

```python
import jax
import jax.numpy as jnp
from jax import lax
from jax.experimental import pallas as pl
from jax.experimental.pallas import tpu as pltpu
from jax.sharding import Mesh, PartitionSpec as P

MATERIALS = 8
GROUP = 8
PAD = 8

GAMMA = 0.2
BETA = 0.5
EDGE_WEIGHTS = (0.0, 1.0, 0.5, 0.25)
OFFSETS = [
    (a, b, c) for a in (-1, 0, 1) for b in (-1, 0, 1) for c in (-1, 0, 1) if (a, b, c) != (0, 0, 0)
]


def shift_cells(array, axis, step):
    if step == 0:
        return array
    length = array.shape[axis]
    zero = jnp.zeros_like(lax.slice_in_dim(array, 0, 1, axis=axis))
    if step > 0:
        return jnp.concatenate([lax.slice_in_dim(array, 1, length, axis=axis), zero], axis=axis)
    return jnp.concatenate([zero, lax.slice_in_dim(array, 0, length - 1, axis=axis)], axis=axis)


def mod_neighbour(mod_ext, off_x, off_y, off_z, depth):
    rows = lax.slice_in_dim(mod_ext, 1 + off_x, 1 + off_x + depth, axis=1)
    return shift_cells(shift_cells(rows, 0, off_y), 2, off_z)


def edges_of(mod_ext, depth):
    centre = mod_neighbour(mod_ext, 0, 0, 0, depth)
    edges = []
    for offset in OFFSETS:
        norm_sq = offset[0] * offset[0] + offset[1] * offset[1] + offset[2] * offset[2]
        edges.append(
            EDGE_WEIGHTS[norm_sq]
            * 0.5
            * (centre + mod_neighbour(mod_ext, offset[0], offset[1], offset[2], depth))
        )
    return centre, edges


def diagonal_of(centre, edges):
    comps = [GAMMA * centre, GAMMA * centre, GAMMA * centre]
    for offset, edge in zip(OFFSETS, edges):
        norm_sq = offset[0] * offset[0] + offset[1] * offset[1] + offset[2] * offset[2]
        for comp in range(3):
            comps[comp] = comps[comp] + edge * (1.0 + BETA * offset[comp] * offset[comp] / norm_sq)
    return jnp.stack(comps, axis=0)


def stencil_kernel(field_ref, edge_ref, cm_ref, out_ref):
    samples, _, rows_y, padded, width = field_ref.shape
    depth = padded - 2 * PAD
    chunks = depth // 8
    sub = lax.broadcasted_iota(jnp.int32, (8, width), 0)
    lane = lax.broadcasted_iota(jnp.int32, (8, width), 1)

    def body(it, carry):
        s = it // chunks
        r = pl.multiple_of((it % chunks) * 8, 8)

        def rows(c, y, off):
            return field_ref[s, c, y, pl.ds(r + off, 8), :]

        centre = [[rows(c, y, PAD) for y in range(rows_y)] for c in range(3)]
        acc = [
            [GAMMA * cm_ref[y, pl.ds(r, 8), :] * centre[c][y] for y in range(rows_y)]
            for c in range(3)
        ]
        index = 0
        for off_x in (-1, 0, 1):
            if off_x == 0:
                shifted_x = centre
            elif off_x < 0:
                shifted_x = [
                    [
                        jnp.where(
                            sub == 0,
                            pltpu.roll(rows(c, y, PAD - 8), 1, 0),
                            pltpu.roll(centre[c][y], 1, 0),
                        )
                        for y in range(rows_y)
                    ]
                    for c in range(3)
                ]
            else:
                shifted_x = [
                    [
                        jnp.where(
                            sub == 7,
                            pltpu.roll(rows(c, y, PAD + 8), 7, 0),
                            pltpu.roll(centre[c][y], 7, 0),
                        )
                        for y in range(rows_y)
                    ]
                    for c in range(3)
                ]
            shifted = {}
            for off_z in (-1, 0, 1):
                if off_z == 0:
                    shifted[off_z] = shifted_x
                elif off_z < 0:
                    shifted[off_z] = [
                        [
                            jnp.where(lane == 0, jnp.float32(0.0), pltpu.roll(v, 1, 1))
                            for v in per_c
                        ]
                        for per_c in shifted_x
                    ]
                else:
                    shifted[off_z] = [
                        [
                            jnp.where(lane == width - 1, jnp.float32(0.0), pltpu.roll(v, width - 1, 1))
                            for v in per_c
                        ]
                        for per_c in shifted_x
                    ]
            for off_y in (-1, 0, 1):
                for off_z in (-1, 0, 1):
                    if (off_x, off_y, off_z) == (0, 0, 0):
                        continue
                    offset = (off_x, off_y, off_z)
                    norm_sq = off_x * off_x + off_y * off_y + off_z * off_z
                    for y in range(rows_y):
                        edge = edge_ref[index, y, pl.ds(r, 8), :]
                        source = y + off_y
                        if 0 <= source < rows_y:
                            delta = [centre[c][y] - shifted[off_z][c][source] for c in range(3)]
                        else:
                            delta = [centre[c][y] for c in range(3)]
                        project = None
                        for c in range(3):
                            if offset[c] > 0:
                                project = delta[c] if project is None else project + delta[c]
                            elif offset[c] < 0:
                                project = -delta[c] if project is None else project - delta[c]
                        if norm_sq == 2:
                            project = project * 0.5
                        elif norm_sq == 3:
                            project = project * (1.0 / 3.0)
                        for c in range(3):
                            if offset[c] != 0:
                                acc[c][y] = acc[c][y] + edge * (delta[c] + BETA * offset[c] * project)
                            else:
                                acc[c][y] = acc[c][y] + edge * delta[c]
                    index += 1
        for c in range(3):
            for y in range(rows_y):
                out_ref[s, c, y, pl.ds(r, 8), :] = acc[c][y]
        return carry

    lax.fori_loop(0, samples * chunks, body, 0)


def stiffness(field, below, above, edges, centre_mod):
    samples, _, rows_y, depth, width = field.shape
    zeros = jnp.zeros((samples, 3, rows_y, PAD - 1, width), jnp.float32)
    padded = jnp.concatenate([zeros, below[:, :, :, None], field, above[:, :, :, None], zeros], axis=3)
    vmem = pl.BlockSpec(memory_space=pltpu.VMEM)
    size = samples * 3 * rows_y * depth * width
    return pl.pallas_call(
        stencil_kernel,
        out_shape=jax.ShapeDtypeStruct(field.shape, jnp.float32),
        in_specs=[vmem, vmem, vmem],
        out_specs=vmem,
        cost_estimate=pl.CostEstimate(flops=26 * 20 * size, bytes_accessed=4 * (2 * size + 28 * size // samples // 3), transcendentals=0),
    )(padded, edges, centre_mod)


def lookup_modulus(material, moduli):
    modulus = jnp.zeros(material.shape, jnp.float32)
    for index in range(MATERIALS):
        modulus = modulus + jnp.where(material == index, moduli[index], jnp.float32(0.0))
    return modulus


def neighbour_devices(part_device, partners):
    count = part_device.shape[0]
    ids = jnp.arange(count, dtype=jnp.int32)
    place = jnp.zeros((count,), jnp.int32).at[part_device].set(ids)
    parity = place % 2
    up_dev = partners[parity, ids]
    low_dev = partners[1 - parity, ids]
    return up_dev, low_dev


def exchange(first, last, up_dev, low_dev):
    col = lax.axis_index("col")
    grp = lax.axis_index("grp")
    me = col * GROUP + grp
    cols = up_dev.shape[0] // GROUP
    pack = jnp.stack([first, last], axis=0)[None]
    held = lax.all_gather(pack, "grp", axis=0, tiled=True)
    targets = jnp.arange(cols, dtype=jnp.int32) * GROUP + grp
    t_up = up_dev[targets]
    t_low = low_dev[targets]
    up_here = (t_up // GROUP) == col
    low_here = (t_low // GROUP) == col
    from_up = held[t_up % GROUP, 0]
    from_low = held[t_low % GROUP, 1]
    shape = (cols,) + (1,) * (from_up.ndim - 1)
    from_up = jnp.where(up_here.reshape(shape), from_up, jnp.float32(0.0))
    from_low = jnp.where(low_here.reshape(shape), from_low, jnp.float32(0.0))
    slots = jnp.stack([from_up, from_low], axis=1)
    got = lax.all_to_all(slots, "col", 0, 0, tiled=True)
    my_up = up_dev[me]
    my_low = low_dev[me]
    above = got[my_up // GROUP, 0]
    below = got[my_low // GROUP, 1]
    above = jnp.where(my_up != me, above, jnp.float32(0.0))
    below = jnp.where(my_low != me, below, jnp.float32(0.0))
    return below, above


def on_device(loads, modal_disp, material, moduli, part_device, partners, low_bound, high_bound):
    up_dev, low_dev = neighbour_devices(part_device, partners)
    samples, _, depth, rows_y, width = loads.shape
    loads = jnp.transpose(loads, (0, 1, 3, 2, 4))
    modal_disp = jnp.transpose(modal_disp, (0, 1, 3, 2, 4))
    modulus = jnp.transpose(lookup_modulus(material, moduli), (1, 0, 2))
    plane = (samples, 3, rows_y, width)
    plane_size = samples * 3 * rows_y * width

    first = jnp.concatenate([modal_disp[:, :, :, 0].reshape(-1), modulus[:, 0].reshape(-1)])
    last = jnp.concatenate([modal_disp[:, :, :, depth - 1].reshape(-1), modulus[:, depth - 1].reshape(-1)])
    below, above = exchange(first, last, up_dev, low_dev)
    mod_ext = jnp.concatenate(
        [
            below[plane_size:].reshape(rows_y, 1, width),
            modulus,
            above[plane_size:].reshape(rows_y, 1, width),
        ],
        axis=1,
    )
    centre_mod, edges = edges_of(mod_ext, depth)
    jacobi = diagonal_of(centre_mod, edges)
    edges = jnp.stack(edges, axis=0)

    def apply(field):
        below, above = exchange(field[:, :, :, 0], field[:, :, :, depth - 1], up_dev, low_dev)
        return stiffness(field, below, above, edges, centre_mod)

    theta = (high_bound[0] + low_bound[0]) / 2.0
    half = (high_bound[0] - low_bound[0]) / 2.0
    sigma = theta / half
    rho0 = 1.0 / sigma
    rho1 = 1.0 / (2.0 * sigma - rho0)
    first_k = stiffness(
        modal_disp,
        below[:plane_size].reshape(plane),
        above[:plane_size].reshape(plane),
        edges,
        centre_mod,
    )
    start = loads - first_k
    step0 = start / (theta * jacobi)
    residual1 = start - apply(step0)
    step1 = rho1 * rho0 * step0 + 2.0 * rho1 / half * residual1 / jacobi
    displacement = modal_disp + step0 + step1
    residual = residual1 - apply(step1)
    return (
        jnp.transpose(displacement, (0, 1, 3, 2, 4)),
        jnp.transpose(residual, (0, 1, 3, 2, 4)),
    )


def solution(mesh):
    devices = mesh.devices.reshape(-1)
    grid = Mesh(devices.reshape(devices.size // GROUP, GROUP), ("col", "grp"))
    slab = ("col", "grp")
    in_specs = (
        P(None, None, slab, None, None),
        P(None, None, slab, None, None),
        P(slab, None, None),
        P(),
        P(),
        P(),
        P(),
        P(),
    )
    out_specs = (P(None, None, slab, None, None), P(None, None, slab, None, None))
    return jax.shard_map(
        on_device, mesh=grid, in_specs=in_specs, out_specs=out_specs, check_vma=False
    )
```

```python
import jax
import jax.numpy as jnp
from jax import lax
from jax.experimental import pallas as pl
from jax.experimental.pallas import tpu as pltpu
from jax.sharding import Mesh, PartitionSpec as P

MATERIALS = 8
GROUP = 8

GAMMA = 0.2
BETA = 0.5
EDGE_WEIGHTS = (0.0, 1.0, 0.5, 0.25)
OFFSETS = [
    (a, b, c) for a in (-1, 0, 1) for b in (-1, 0, 1) for c in (-1, 0, 1) if (a, b, c) != (0, 0, 0)
]


def shift_cells(array, axis, step):
    if step == 0:
        return array
    length = array.shape[axis]
    zero = jnp.zeros_like(lax.slice_in_dim(array, 0, 1, axis=axis))
    if step > 0:
        return jnp.concatenate([lax.slice_in_dim(array, 1, length, axis=axis), zero], axis=axis)
    return jnp.concatenate([zero, lax.slice_in_dim(array, 0, length - 1, axis=axis)], axis=axis)


def mod_neighbour(mod_ext, off_x, off_y, off_z, depth):
    rows = lax.slice_in_dim(mod_ext, 1 + off_x, 1 + off_x + depth, axis=1)
    return shift_cells(shift_cells(rows, 0, off_y), 2, off_z)


def edges_of(mod_ext, depth):
    centre = mod_neighbour(mod_ext, 0, 0, 0, depth)
    edges = []
    for offset in OFFSETS:
        norm_sq = offset[0] * offset[0] + offset[1] * offset[1] + offset[2] * offset[2]
        edges.append(
            EDGE_WEIGHTS[norm_sq]
            * 0.5
            * (centre + mod_neighbour(mod_ext, offset[0], offset[1], offset[2], depth))
        )
    return centre, edges


def diagonal_of(centre, edges):
    comps = [GAMMA * centre, GAMMA * centre, GAMMA * centre]
    for offset, edge in zip(OFFSETS, edges):
        norm_sq = offset[0] * offset[0] + offset[1] * offset[1] + offset[2] * offset[2]
        for comp in range(3):
            comps[comp] = comps[comp] + edge * (1.0 + BETA * offset[comp] * offset[comp] / norm_sq)
    return jnp.stack(comps, axis=0)


def edges_kernel(mod_ref, below_ref, above_ref, edge_ref, centre_ref, diag_ref):
    rows_y, depth, width = mod_ref.shape
    chunks = depth // 8
    sub = lax.broadcasted_iota(jnp.int32, (8, width), 0)
    lane = lax.broadcasted_iota(jnp.int32, (8, width), 1)

    def body(it, carry):
        r = pl.multiple_of(it * 8, 8)
        centre = [mod_ref[y, pl.ds(r, 8), :] for y in range(rows_y)]
        prev = [
            jnp.where(it == 0, below_ref[y], mod_ref[y, pl.ds(jnp.maximum(r - 8, 0), 8), :])
            for y in range(rows_y)
        ]
        nxt = [
            jnp.where(
                it == chunks - 1, above_ref[y], mod_ref[y, pl.ds(jnp.minimum(r + 8, depth - 8), 8), :]
            )
            for y in range(rows_y)
        ]
        comps = [[GAMMA * centre[y] for y in range(rows_y)] for c in range(3)]
        index = 0
        for off_x in (-1, 0, 1):
            if off_x == 0:
                shifted_x = centre
            elif off_x < 0:
                shifted_x = [
                    jnp.where(sub == 0, pltpu.roll(prev[y], 1, 0), pltpu.roll(centre[y], 1, 0))
                    for y in range(rows_y)
                ]
            else:
                shifted_x = [
                    jnp.where(sub == 7, pltpu.roll(nxt[y], 7, 0), pltpu.roll(centre[y], 7, 0))
                    for y in range(rows_y)
                ]
            shifted = {0: shifted_x}
            shifted[-1] = [jnp.where(lane == 0, jnp.float32(0.0), pltpu.roll(v, 1, 1)) for v in shifted_x]
            shifted[1] = [
                jnp.where(lane == width - 1, jnp.float32(0.0), pltpu.roll(v, width - 1, 1))
                for v in shifted_x
            ]
            for off_y in (-1, 0, 1):
                for off_z in (-1, 0, 1):
                    if (off_x, off_y, off_z) == (0, 0, 0):
                        continue
                    offset = (off_x, off_y, off_z)
                    norm_sq = off_x * off_x + off_y * off_y + off_z * off_z
                    for y in range(rows_y):
                        source = y + off_y
                        if 0 <= source < rows_y:
                            other = shifted[off_z][source]
                        else:
                            other = jnp.zeros_like(centre[y])
                        edge = EDGE_WEIGHTS[norm_sq] * 0.5 * (centre[y] + other)
                        edge_ref[index, y, pl.ds(r, 8), :] = edge
                        for c in range(3):
                            comps[c][y] = comps[c][y] + edge * (
                                1.0 + BETA * offset[c] * offset[c] / norm_sq
                            )
                    index += 1
        for y in range(rows_y):
            centre_ref[y, pl.ds(r, 8), :] = centre[y]
            for c in range(3):
                diag_ref[c, y, pl.ds(r, 8), :] = comps[c][y]
        return carry

    lax.fori_loop(0, chunks, body, 0)


def edges_and_diagonal(modulus, below, above):
    rows_y, depth, width = modulus.shape
    vmem = pl.BlockSpec(memory_space=pltpu.VMEM)
    halo_below = jnp.broadcast_to(below[:, None], (rows_y, 8, width))
    halo_above = jnp.broadcast_to(above[:, None], (rows_y, 8, width))
    return pl.pallas_call(
        edges_kernel,
        out_shape=(
            jax.ShapeDtypeStruct((len(OFFSETS), rows_y, depth, width), jnp.float32),
            jax.ShapeDtypeStruct((rows_y, depth, width), jnp.float32),
            jax.ShapeDtypeStruct((3, rows_y, depth, width), jnp.float32),
        ),
        in_specs=[vmem, vmem, vmem],
        out_specs=(vmem, vmem, vmem),
    )(modulus, halo_below, halo_above)


def stencil_kernel(field_ref, below_ref, above_ref, edge_ref, cm_ref, out_ref):
    samples, _, rows_y, depth, width = field_ref.shape
    chunks = depth // 8
    sub = lax.broadcasted_iota(jnp.int32, (8, width), 0)
    lane = lax.broadcasted_iota(jnp.int32, (8, width), 1)

    def body(it, carry):
        s = it // chunks
        r = pl.multiple_of((it % chunks) * 8, 8)

        first = (it % chunks) == 0
        last = (it % chunks) == chunks - 1

        def rows(c, y, off):
            if off == 0:
                return field_ref[s, c, y, pl.ds(r, 8), :]
            if off < 0:
                return jnp.where(
                    first, below_ref[s, c, y], field_ref[s, c, y, pl.ds(jnp.maximum(r - 8, 0), 8), :]
                )
            return jnp.where(
                last, above_ref[s, c, y], field_ref[s, c, y, pl.ds(jnp.minimum(r + 8, depth - 8), 8), :]
            )

        centre = [[rows(c, y, 0) for y in range(rows_y)] for c in range(3)]
        acc = [
            [GAMMA * cm_ref[y, pl.ds(r, 8), :] * centre[c][y] for y in range(rows_y)]
            for c in range(3)
        ]
        index = 0
        for off_x in (-1, 0, 1):
            if off_x == 0:
                shifted_x = centre
            elif off_x < 0:
                shifted_x = [
                    [
                        jnp.where(
                            sub == 0,
                            pltpu.roll(rows(c, y, -1), 1, 0),
                            pltpu.roll(centre[c][y], 1, 0),
                        )
                        for y in range(rows_y)
                    ]
                    for c in range(3)
                ]
            else:
                shifted_x = [
                    [
                        jnp.where(
                            sub == 7,
                            pltpu.roll(rows(c, y, 1), 7, 0),
                            pltpu.roll(centre[c][y], 7, 0),
                        )
                        for y in range(rows_y)
                    ]
                    for c in range(3)
                ]
            shifted = {}
            for off_z in (-1, 0, 1):
                if off_z == 0:
                    shifted[off_z] = shifted_x
                elif off_z < 0:
                    shifted[off_z] = [
                        [
                            jnp.where(lane == 0, jnp.float32(0.0), pltpu.roll(v, 1, 1))
                            for v in per_c
                        ]
                        for per_c in shifted_x
                    ]
                else:
                    shifted[off_z] = [
                        [
                            jnp.where(lane == width - 1, jnp.float32(0.0), pltpu.roll(v, width - 1, 1))
                            for v in per_c
                        ]
                        for per_c in shifted_x
                    ]
            for off_y in (-1, 0, 1):
                for off_z in (-1, 0, 1):
                    if (off_x, off_y, off_z) == (0, 0, 0):
                        continue
                    offset = (off_x, off_y, off_z)
                    norm_sq = off_x * off_x + off_y * off_y + off_z * off_z
                    for y in range(rows_y):
                        edge = edge_ref[index, y, pl.ds(r, 8), :]
                        source = y + off_y
                        if 0 <= source < rows_y:
                            delta = [centre[c][y] - shifted[off_z][c][source] for c in range(3)]
                        else:
                            delta = [centre[c][y] for c in range(3)]
                        project = None
                        for c in range(3):
                            if offset[c] > 0:
                                project = delta[c] if project is None else project + delta[c]
                            elif offset[c] < 0:
                                project = -delta[c] if project is None else project - delta[c]
                        if norm_sq == 2:
                            project = project * 0.5
                        elif norm_sq == 3:
                            project = project * (1.0 / 3.0)
                        for c in range(3):
                            if offset[c] != 0:
                                acc[c][y] = acc[c][y] + edge * (delta[c] + BETA * offset[c] * project)
                            else:
                                acc[c][y] = acc[c][y] + edge * delta[c]
                    index += 1
        for c in range(3):
            for y in range(rows_y):
                out_ref[s, c, y, pl.ds(r, 8), :] = acc[c][y]
        return carry

    lax.fori_loop(0, samples * chunks, body, 0)


def stiffness(field, below, above, edges, centre_mod):
    samples, _, rows_y, depth, width = field.shape
    halo_shape = (samples, 3, rows_y, 8, width)
    halo_below = jnp.broadcast_to(below[:, :, :, None], halo_shape)
    halo_above = jnp.broadcast_to(above[:, :, :, None], halo_shape)
    vmem = pl.BlockSpec(memory_space=pltpu.VMEM)
    size = samples * 3 * rows_y * depth * width
    return pl.pallas_call(
        stencil_kernel,
        out_shape=jax.ShapeDtypeStruct(field.shape, jnp.float32),
        in_specs=[vmem] * 5,
        out_specs=vmem,
        cost_estimate=pl.CostEstimate(flops=26 * 20 * size, bytes_accessed=4 * (2 * size + 28 * size // samples // 3), transcendentals=0),
    )(field, halo_below, halo_above, edges, centre_mod)


def lookup_modulus(material, moduli):
    modulus = jnp.zeros(material.shape, jnp.float32)
    for index in range(MATERIALS):
        modulus = modulus + jnp.where(material == index, moduli[index], jnp.float32(0.0))
    return modulus


def neighbour_devices(part_device, partners):
    count = part_device.shape[0]
    ids = jnp.arange(count, dtype=jnp.int32)
    place = jnp.zeros((count,), jnp.int32).at[part_device].set(ids)
    parity = place % 2
    up_dev = partners[parity, ids]
    low_dev = partners[1 - parity, ids]
    return up_dev, low_dev


def exchange(first, last, up_dev, low_dev):
    col = lax.axis_index("col")
    grp = lax.axis_index("grp")
    me = col * GROUP + grp
    cols = up_dev.shape[0] // GROUP
    pack = jnp.stack([first, last], axis=0)[None]
    held = lax.all_gather(pack, "grp", axis=0, tiled=True)
    targets = jnp.arange(cols, dtype=jnp.int32) * GROUP + grp
    t_up = up_dev[targets]
    t_low = low_dev[targets]
    up_here = (t_up // GROUP) == col
    low_here = (t_low // GROUP) == col
    from_up = held[t_up % GROUP, 0]
    from_low = held[t_low % GROUP, 1]
    shape = (cols,) + (1,) * (from_up.ndim - 1)
    from_up = jnp.where(up_here.reshape(shape), from_up, jnp.float32(0.0))
    from_low = jnp.where(low_here.reshape(shape), from_low, jnp.float32(0.0))
    slots = jnp.stack([from_up, from_low], axis=1)
    got = lax.all_to_all(slots, "col", 0, 0, tiled=True)
    my_up = up_dev[me]
    my_low = low_dev[me]
    above = got[my_up // GROUP, 0]
    below = got[my_low // GROUP, 1]
    above = jnp.where(my_up != me, above, jnp.float32(0.0))
    below = jnp.where(my_low != me, below, jnp.float32(0.0))
    return below, above


def on_device(loads, modal_disp, material, moduli, part_device, partners, low_bound, high_bound):
    up_dev, low_dev = neighbour_devices(part_device, partners)
    samples, _, depth, rows_y, width = loads.shape
    loads = jnp.transpose(loads, (0, 1, 3, 2, 4))
    modal_disp = jnp.transpose(modal_disp, (0, 1, 3, 2, 4))
    modulus = jnp.transpose(lookup_modulus(material, moduli), (1, 0, 2))
    plane = (samples, 3, rows_y, width)
    plane_size = samples * 3 * rows_y * width

    first = jnp.concatenate([modal_disp[:, :, :, 0].reshape(-1), modulus[:, 0].reshape(-1)])
    last = jnp.concatenate([modal_disp[:, :, :, depth - 1].reshape(-1), modulus[:, depth - 1].reshape(-1)])
    below, above = exchange(first, last, up_dev, low_dev)
    edges, centre_mod, jacobi = edges_and_diagonal(
        modulus,
        below[plane_size:].reshape(rows_y, width),
        above[plane_size:].reshape(rows_y, width),
    )

    def apply(field):
        below, above = exchange(field[:, :, :, 0], field[:, :, :, depth - 1], up_dev, low_dev)
        return stiffness(field, below, above, edges, centre_mod)

    theta = (high_bound[0] + low_bound[0]) / 2.0
    half = (high_bound[0] - low_bound[0]) / 2.0
    sigma = theta / half
    rho0 = 1.0 / sigma
    rho1 = 1.0 / (2.0 * sigma - rho0)
    first_k = stiffness(
        modal_disp,
        below[:plane_size].reshape(plane),
        above[:plane_size].reshape(plane),
        edges,
        centre_mod,
    )
    start = loads - first_k
    step0 = start / (theta * jacobi)
    residual1 = start - apply(step0)
    step1 = rho1 * rho0 * step0 + 2.0 * rho1 / half * residual1 / jacobi
    displacement = modal_disp + step0 + step1
    residual = residual1 - apply(step1)
    return (
        jnp.transpose(displacement, (0, 1, 3, 2, 4)),
        jnp.transpose(residual, (0, 1, 3, 2, 4)),
    )


def solution(mesh):
    devices = mesh.devices.reshape(-1)
    grid = Mesh(devices.reshape(devices.size // GROUP, GROUP), ("col", "grp"))
    slab = ("col", "grp")
    in_specs = (
        P(None, None, slab, None, None),
        P(None, None, slab, None, None),
        P(slab, None, None),
        P(),
        P(),
        P(),
        P(),
        P(),
    )
    out_specs = (P(None, None, slab, None, None), P(None, None, slab, None, None))
    return jax.shard_map(
        on_device, mesh=grid, in_specs=in_specs, out_specs=out_specs, check_vma=False
    )
```

```python
import jax
import jax.numpy as jnp
from jax import lax
from jax.experimental import pallas as pl
from jax.experimental.pallas import tpu as pltpu
from jax.sharding import Mesh, PartitionSpec as P

MATERIALS = 8
GROUP = 8

GAMMA = 0.2
BETA = 0.5
EDGE_WEIGHTS = (0.0, 1.0, 0.5, 0.25)
OFFSETS = [
    (a, b, c) for a in (-1, 0, 1) for b in (-1, 0, 1) for c in (-1, 0, 1) if (a, b, c) != (0, 0, 0)
]


def shift_cells(array, axis, step):
    if step == 0:
        return array
    length = array.shape[axis]
    zero = jnp.zeros_like(lax.slice_in_dim(array, 0, 1, axis=axis))
    if step > 0:
        return jnp.concatenate([lax.slice_in_dim(array, 1, length, axis=axis), zero], axis=axis)
    return jnp.concatenate([zero, lax.slice_in_dim(array, 0, length - 1, axis=axis)], axis=axis)


def mod_neighbour(mod_ext, off_x, off_y, off_z, depth):
    rows = lax.slice_in_dim(mod_ext, 1 + off_x, 1 + off_x + depth, axis=1)
    return shift_cells(shift_cells(rows, 0, off_y), 2, off_z)


def edges_of(mod_ext, depth):
    centre = mod_neighbour(mod_ext, 0, 0, 0, depth)
    edges = []
    for offset in OFFSETS:
        norm_sq = offset[0] * offset[0] + offset[1] * offset[1] + offset[2] * offset[2]
        edges.append(
            EDGE_WEIGHTS[norm_sq]
            * 0.5
            * (centre + mod_neighbour(mod_ext, offset[0], offset[1], offset[2], depth))
        )
    return centre, edges


def diagonal_of(centre, edges):
    comps = [GAMMA * centre, GAMMA * centre, GAMMA * centre]
    for offset, edge in zip(OFFSETS, edges):
        norm_sq = offset[0] * offset[0] + offset[1] * offset[1] + offset[2] * offset[2]
        for comp in range(3):
            comps[comp] = comps[comp] + edge * (1.0 + BETA * offset[comp] * offset[comp] / norm_sq)
    return jnp.stack(comps, axis=0)


def edges_kernel(mod_ref, below_ref, above_ref, edge_ref, centre_ref, diag_ref):
    rows_y, depth, width = mod_ref.shape
    chunks = depth // 8
    sub = lax.broadcasted_iota(jnp.int32, (8, width), 0)
    lane = lax.broadcasted_iota(jnp.int32, (8, width), 1)

    def body(it, carry):
        r = pl.multiple_of(it * 8, 8)
        centre = [mod_ref[y, pl.ds(r, 8), :] for y in range(rows_y)]
        prev = [
            jnp.where(it == 0, below_ref[y], mod_ref[y, pl.ds(jnp.maximum(r - 8, 0), 8), :])
            for y in range(rows_y)
        ]
        nxt = [
            jnp.where(
                it == chunks - 1, above_ref[y], mod_ref[y, pl.ds(jnp.minimum(r + 8, depth - 8), 8), :]
            )
            for y in range(rows_y)
        ]
        comps = [[GAMMA * centre[y] for y in range(rows_y)] for c in range(3)]
        index = 0
        for off_x in (-1, 0, 1):
            if off_x == 0:
                shifted_x = centre
            elif off_x < 0:
                shifted_x = [
                    jnp.where(sub == 0, pltpu.roll(prev[y], 1, 0), pltpu.roll(centre[y], 1, 0))
                    for y in range(rows_y)
                ]
            else:
                shifted_x = [
                    jnp.where(sub == 7, pltpu.roll(nxt[y], 7, 0), pltpu.roll(centre[y], 7, 0))
                    for y in range(rows_y)
                ]
            shifted = {0: shifted_x}
            shifted[-1] = [jnp.where(lane == 0, jnp.float32(0.0), pltpu.roll(v, 1, 1)) for v in shifted_x]
            shifted[1] = [
                jnp.where(lane == width - 1, jnp.float32(0.0), pltpu.roll(v, width - 1, 1))
                for v in shifted_x
            ]
            for off_y in (-1, 0, 1):
                for off_z in (-1, 0, 1):
                    if (off_x, off_y, off_z) == (0, 0, 0):
                        continue
                    offset = (off_x, off_y, off_z)
                    norm_sq = off_x * off_x + off_y * off_y + off_z * off_z
                    for y in range(rows_y):
                        source = y + off_y
                        if 0 <= source < rows_y:
                            other = shifted[off_z][source]
                        else:
                            other = jnp.zeros_like(centre[y])
                        edge = EDGE_WEIGHTS[norm_sq] * 0.5 * (centre[y] + other)
                        edge_ref[index, y, pl.ds(r, 8), :] = edge
                        for c in range(3):
                            comps[c][y] = comps[c][y] + edge * (
                                1.0 + BETA * offset[c] * offset[c] / norm_sq
                            )
                    index += 1
        for y in range(rows_y):
            centre_ref[y, pl.ds(r, 8), :] = centre[y]
            for c in range(3):
                diag_ref[c, y, pl.ds(r, 8), :] = comps[c][y]
        return carry

    lax.fori_loop(0, chunks, body, 0)


def edges_and_diagonal(modulus, below, above):
    rows_y, depth, width = modulus.shape
    vmem = pl.BlockSpec(memory_space=pltpu.VMEM)
    halo_below = jnp.broadcast_to(below[:, None], (rows_y, 8, width))
    halo_above = jnp.broadcast_to(above[:, None], (rows_y, 8, width))
    return pl.pallas_call(
        edges_kernel,
        out_shape=(
            jax.ShapeDtypeStruct((len(OFFSETS), rows_y, depth, width), jnp.float32),
            jax.ShapeDtypeStruct((rows_y, depth, width), jnp.float32),
            jax.ShapeDtypeStruct((3, rows_y, depth, width), jnp.float32),
        ),
        in_specs=[vmem, vmem, vmem],
        out_specs=(vmem, vmem, vmem),
    )(modulus, halo_below, halo_above)


def stencil_kernel(field_ref, below_ref, above_ref, edge_ref, cm_ref, out_ref):
    samples, _, rows_y, depth, width = field_ref.shape
    chunks = depth // 8
    sub = lax.broadcasted_iota(jnp.int32, (8, width), 0)
    lane = lax.broadcasted_iota(jnp.int32, (8, width), 1)

    def body(it, carry):
        s = it // chunks
        r = pl.multiple_of((it % chunks) * 8, 8)

        first = (it % chunks) == 0
        last = (it % chunks) == chunks - 1

        def rows(c, y, off):
            if off == 0:
                return field_ref[s, c, y, pl.ds(r, 8), :]
            if off < 0:
                return jnp.where(
                    first, below_ref[s, c, y], field_ref[s, c, y, pl.ds(jnp.maximum(r - 8, 0), 8), :]
                )
            return jnp.where(
                last, above_ref[s, c, y], field_ref[s, c, y, pl.ds(jnp.minimum(r + 8, depth - 8), 8), :]
            )

        centre = [[rows(c, y, 0) for y in range(rows_y)] for c in range(3)]
        acc = [
            [GAMMA * cm_ref[y, pl.ds(r, 8), :] * centre[c][y] for y in range(rows_y)]
            for c in range(3)
        ]
        index = 0
        for off_x in (-1, 0, 1):
            if off_x == 0:
                shifted_x = centre
            elif off_x < 0:
                shifted_x = [
                    [
                        jnp.where(
                            sub == 0,
                            pltpu.roll(rows(c, y, -1), 1, 0),
                            pltpu.roll(centre[c][y], 1, 0),
                        )
                        for y in range(rows_y)
                    ]
                    for c in range(3)
                ]
            else:
                shifted_x = [
                    [
                        jnp.where(
                            sub == 7,
                            pltpu.roll(rows(c, y, 1), 7, 0),
                            pltpu.roll(centre[c][y], 7, 0),
                        )
                        for y in range(rows_y)
                    ]
                    for c in range(3)
                ]
            shifted = {}
            for off_z in (-1, 0, 1):
                if off_z == 0:
                    shifted[off_z] = shifted_x
                elif off_z < 0:
                    shifted[off_z] = [
                        [
                            jnp.where(lane == 0, jnp.float32(0.0), pltpu.roll(v, 1, 1))
                            for v in per_c
                        ]
                        for per_c in shifted_x
                    ]
                else:
                    shifted[off_z] = [
                        [
                            jnp.where(lane == width - 1, jnp.float32(0.0), pltpu.roll(v, width - 1, 1))
                            for v in per_c
                        ]
                        for per_c in shifted_x
                    ]
            for off_y in (-1, 0, 1):
                for off_z in (-1, 0, 1):
                    if (off_x, off_y, off_z) == (0, 0, 0):
                        continue
                    offset = (off_x, off_y, off_z)
                    norm_sq = off_x * off_x + off_y * off_y + off_z * off_z
                    for y in range(rows_y):
                        edge = edge_ref[index, y, pl.ds(r, 8), :]
                        source = y + off_y
                        if 0 <= source < rows_y:
                            delta = [centre[c][y] - shifted[off_z][c][source] for c in range(3)]
                        else:
                            delta = [centre[c][y] for c in range(3)]
                        project = None
                        for c in range(3):
                            if offset[c] > 0:
                                project = delta[c] if project is None else project + delta[c]
                            elif offset[c] < 0:
                                project = -delta[c] if project is None else project - delta[c]
                        if norm_sq == 2:
                            project = project * 0.5
                        elif norm_sq == 3:
                            project = project * (1.0 / 3.0)
                        for c in range(3):
                            if offset[c] != 0:
                                acc[c][y] = acc[c][y] + edge * (delta[c] + BETA * offset[c] * project)
                            else:
                                acc[c][y] = acc[c][y] + edge * delta[c]
                    index += 1
        for c in range(3):
            for y in range(rows_y):
                out_ref[s, c, y, pl.ds(r, 8), :] = acc[c][y]
        return carry

    lax.fori_loop(0, samples * chunks, body, 0)


def stiffness(field, below, above, edges, centre_mod):
    samples, _, rows_y, depth, width = field.shape
    halo_shape = (samples, 3, rows_y, 8, width)
    halo_below = jnp.broadcast_to(below[:, :, :, None], halo_shape)
    halo_above = jnp.broadcast_to(above[:, :, :, None], halo_shape)
    vmem = pl.BlockSpec(memory_space=pltpu.VMEM)
    size = samples * 3 * rows_y * depth * width
    return pl.pallas_call(
        stencil_kernel,
        out_shape=jax.ShapeDtypeStruct(field.shape, jnp.float32),
        in_specs=[vmem] * 5,
        out_specs=vmem,
        cost_estimate=pl.CostEstimate(flops=26 * 20 * size, bytes_accessed=4 * (2 * size + 28 * size // samples // 3), transcendentals=0),
    )(field, halo_below, halo_above, edges, centre_mod)


def lookup_modulus(material, moduli):
    modulus = jnp.zeros(material.shape, jnp.float32)
    for index in range(MATERIALS):
        modulus = modulus + jnp.where(material == index, moduli[index], jnp.float32(0.0))
    return modulus


def neighbour_devices(part_device, partners):
    count = part_device.shape[0]
    ids = jnp.arange(count, dtype=jnp.int32)
    place = jnp.zeros((count,), jnp.int32).at[part_device].set(ids)
    parity = place % 2
    up_dev = partners[parity, ids]
    low_dev = partners[1 - parity, ids]
    return up_dev, low_dev


def exchange(first, last, up_dev, low_dev):
    col = lax.axis_index("col")
    grp = lax.axis_index("grp")
    me = col * GROUP + grp
    cols = up_dev.shape[0] // GROUP
    pack = jnp.stack([first, last], axis=0)[None]
    held = lax.all_gather(pack, "grp", axis=0, tiled=True)
    targets = jnp.arange(cols, dtype=jnp.int32) * GROUP + grp
    t_up = up_dev[targets]
    t_low = low_dev[targets]
    up_here = (t_up // GROUP) == col
    low_here = (t_low // GROUP) == col
    from_up = held[t_up % GROUP, 0]
    from_low = held[t_low % GROUP, 1]
    shape = (cols,) + (1,) * (from_up.ndim - 1)
    from_up = jnp.where(up_here.reshape(shape), from_up, jnp.float32(0.0))
    from_low = jnp.where(low_here.reshape(shape), from_low, jnp.float32(0.0))
    slots = jnp.stack([from_up, from_low], axis=1)
    got = lax.all_to_all(slots, "col", 0, 0, tiled=True)
    my_up = up_dev[me]
    my_low = low_dev[me]
    above = got[my_up // GROUP, 0]
    below = got[my_low // GROUP, 1]
    above = jnp.where(my_up != me, above, jnp.float32(0.0))
    below = jnp.where(my_low != me, below, jnp.float32(0.0))
    return below, above


def on_device(loads, modal_disp, material, moduli, part_device, partners, low_bound, high_bound):
    up_dev, low_dev = neighbour_devices(part_device, partners)
    samples, _, depth, rows_y, width = loads.shape
    loads = jnp.transpose(loads, (0, 1, 3, 2, 4))
    modal_disp = jnp.transpose(modal_disp, (0, 1, 3, 2, 4))
    modulus = jnp.transpose(lookup_modulus(material, moduli), (1, 0, 2))
    plane = (samples, 3, rows_y, width)
    plane_size = samples * 3 * rows_y * width
    mod_size = rows_y * width

    def pack(md_rows, load_rows):
        parts = [modal_disp[:, :, :, r].reshape(-1) for r in md_rows]
        parts += [loads[:, :, :, r].reshape(-1) for r in load_rows]
        parts += [modulus[:, r].reshape(-1) for r in md_rows]
        return jnp.concatenate(parts)

    first = pack((0, 1, 2), (0, 1))
    last = pack((depth - 3, depth - 2, depth - 1), (depth - 2, depth - 1))
    below, above = exchange(first, last, up_dev, low_dev)

    def planes_of(got, count, start, size, shape):
        return [got[start + i * size : start + (i + 1) * size].reshape(shape) for i in range(count)]

    md_below = planes_of(below, 3, 0, plane_size, plane)
    md_above = planes_of(above, 3, 0, plane_size, plane)
    ld_below = planes_of(below, 2, 3 * plane_size, plane_size, plane)
    ld_above = planes_of(above, 2, 3 * plane_size, plane_size, plane)
    mod_below = planes_of(below, 3, 5 * plane_size, mod_size, (rows_y, width))
    mod_above = planes_of(above, 3, 5 * plane_size, mod_size, (rows_y, width))

    def extend(own, lower, upper, axis):
        zero = jnp.zeros_like(lower[0])
        rows = [zero] * (8 - len(lower)) + list(lower)
        tail = list(upper) + [zero] * (8 - len(upper))
        return jnp.concatenate(
            [jnp.stack(rows, axis=axis), own, jnp.stack(tail, axis=axis)], axis=axis
        )

    md_ext = extend(modal_disp, md_below, md_above, 3)
    loads_ext = extend(loads, ld_below, ld_above, 3)
    mod_ext = extend(modulus, mod_below, mod_above, 1)
    low_on = low_dev[col_grp_index()] != col_grp_index()
    up_on = up_dev[col_grp_index()] != col_grp_index()
    zero_mod = jnp.zeros((rows_y, width), jnp.float32)
    edges, centre_mod, jacobi = edges_and_diagonal(mod_ext, zero_mod, zero_mod)

    row = lax.broadcasted_iota(jnp.int32, (depth + 16,), 0) - 8

    def valid(reach):
        keep = (row >= 0) & (row < depth)
        keep = keep | (low_on & (row >= -reach) & (row < 0))
        keep = keep | (up_on & (row >= depth) & (row < depth + reach))
        return keep.reshape(depth + 16, 1)

    zero_plane = jnp.zeros(plane, jnp.float32)

    def apply(field):
        return stiffness(field, zero_plane, zero_plane, edges, centre_mod)

    theta = (high_bound[0] + low_bound[0]) / 2.0
    half = (high_bound[0] - low_bound[0]) / 2.0
    sigma = theta / half
    rho0 = 1.0 / sigma
    rho1 = 1.0 / (2.0 * sigma - rho0)
    start = loads_ext - apply(md_ext)
    step0 = jnp.where(valid(2), start / (theta * jacobi), jnp.float32(0.0))
    residual1 = start - apply(step0)
    step1 = jnp.where(
        valid(1), rho1 * rho0 * step0 + 2.0 * rho1 / half * residual1 / jacobi, jnp.float32(0.0)
    )
    inner = slice(8, 8 + depth)
    displacement = modal_disp + step0[:, :, :, inner] + step1[:, :, :, inner]
    residual = residual1[:, :, :, inner] - apply(step1)[:, :, :, inner]
    return (
        jnp.transpose(displacement, (0, 1, 3, 2, 4)),
        jnp.transpose(residual, (0, 1, 3, 2, 4)),
    )


def col_grp_index():
    return lax.axis_index("col") * GROUP + lax.axis_index("grp")


def solution(mesh):
    devices = mesh.devices.reshape(-1)
    grid = Mesh(devices.reshape(devices.size // GROUP, GROUP), ("col", "grp"))
    slab = ("col", "grp")
    in_specs = (
        P(None, None, slab, None, None),
        P(None, None, slab, None, None),
        P(slab, None, None),
        P(),
        P(),
        P(),
        P(),
        P(),
    )
    out_specs = (P(None, None, slab, None, None), P(None, None, slab, None, None))
    return jax.shard_map(
        on_device, mesh=grid, in_specs=in_specs, out_specs=out_specs, check_vma=False
    )
```

```python
import jax
import jax.numpy as jnp
from jax import lax
from jax.experimental import pallas as pl
from jax.experimental.pallas import tpu as pltpu
from jax.sharding import Mesh, PartitionSpec as P

MATERIALS = 8
GROUP = 8

GAMMA = 0.2
BETA = 0.5
EDGE_WEIGHTS = (0.0, 1.0, 0.5, 0.25)
OFFSETS = [
    (a, b, c) for a in (-1, 0, 1) for b in (-1, 0, 1) for c in (-1, 0, 1) if (a, b, c) != (0, 0, 0)
]


def shift_cells(array, axis, step):
    if step == 0:
        return array
    length = array.shape[axis]
    zero = jnp.zeros_like(lax.slice_in_dim(array, 0, 1, axis=axis))
    if step > 0:
        return jnp.concatenate([lax.slice_in_dim(array, 1, length, axis=axis), zero], axis=axis)
    return jnp.concatenate([zero, lax.slice_in_dim(array, 0, length - 1, axis=axis)], axis=axis)


def mod_neighbour(mod_ext, off_x, off_y, off_z, depth):
    rows = lax.slice_in_dim(mod_ext, 1 + off_x, 1 + off_x + depth, axis=1)
    return shift_cells(shift_cells(rows, 0, off_y), 2, off_z)


def edges_of(mod_ext, depth):
    centre = mod_neighbour(mod_ext, 0, 0, 0, depth)
    edges = []
    for offset in OFFSETS:
        norm_sq = offset[0] * offset[0] + offset[1] * offset[1] + offset[2] * offset[2]
        edges.append(
            EDGE_WEIGHTS[norm_sq]
            * 0.5
            * (centre + mod_neighbour(mod_ext, offset[0], offset[1], offset[2], depth))
        )
    return centre, edges


def diagonal_of(centre, edges):
    comps = [GAMMA * centre, GAMMA * centre, GAMMA * centre]
    for offset, edge in zip(OFFSETS, edges):
        norm_sq = offset[0] * offset[0] + offset[1] * offset[1] + offset[2] * offset[2]
        for comp in range(3):
            comps[comp] = comps[comp] + edge * (1.0 + BETA * offset[comp] * offset[comp] / norm_sq)
    return jnp.stack(comps, axis=0)


def edges_kernel(mod_ref, below_ref, above_ref, edge_ref, centre_ref, diag_ref):
    rows_y, depth, width = mod_ref.shape
    chunks = depth // 8
    sub = lax.broadcasted_iota(jnp.int32, (8, width), 0)
    lane = lax.broadcasted_iota(jnp.int32, (8, width), 1)

    def body(it, carry):
        r = pl.multiple_of(it * 8, 8)
        centre = [mod_ref[y, pl.ds(r, 8), :] for y in range(rows_y)]
        prev = [
            jnp.where(it == 0, below_ref[y], mod_ref[y, pl.ds(jnp.maximum(r - 8, 0), 8), :])
            for y in range(rows_y)
        ]
        nxt = [
            jnp.where(
                it == chunks - 1, above_ref[y], mod_ref[y, pl.ds(jnp.minimum(r + 8, depth - 8), 8), :]
            )
            for y in range(rows_y)
        ]
        comps = [[GAMMA * centre[y] for y in range(rows_y)] for c in range(3)]
        index = 0
        for off_x in (-1, 0, 1):
            if off_x == 0:
                shifted_x = centre
            elif off_x < 0:
                shifted_x = [
                    jnp.where(sub == 0, pltpu.roll(prev[y], 1, 0), pltpu.roll(centre[y], 1, 0))
                    for y in range(rows_y)
                ]
            else:
                shifted_x = [
                    jnp.where(sub == 7, pltpu.roll(nxt[y], 7, 0), pltpu.roll(centre[y], 7, 0))
                    for y in range(rows_y)
                ]
            shifted = {0: shifted_x}
            shifted[-1] = [jnp.where(lane == 0, jnp.float32(0.0), pltpu.roll(v, 1, 1)) for v in shifted_x]
            shifted[1] = [
                jnp.where(lane == width - 1, jnp.float32(0.0), pltpu.roll(v, width - 1, 1))
                for v in shifted_x
            ]
            for off_y in (-1, 0, 1):
                for off_z in (-1, 0, 1):
                    if (off_x, off_y, off_z) == (0, 0, 0):
                        continue
                    offset = (off_x, off_y, off_z)
                    norm_sq = off_x * off_x + off_y * off_y + off_z * off_z
                    for y in range(rows_y):
                        source = y + off_y
                        if 0 <= source < rows_y:
                            other = shifted[off_z][source]
                        else:
                            other = jnp.zeros_like(centre[y])
                        edge = EDGE_WEIGHTS[norm_sq] * 0.5 * (centre[y] + other)
                        edge_ref[index, y, pl.ds(r, 8), :] = edge
                        for c in range(3):
                            comps[c][y] = comps[c][y] + edge * (
                                1.0 + BETA * offset[c] * offset[c] / norm_sq
                            )
                    index += 1
        for y in range(rows_y):
            centre_ref[y, pl.ds(r, 8), :] = centre[y]
            for c in range(3):
                diag_ref[c, y, pl.ds(r, 8), :] = comps[c][y]
        return carry

    lax.fori_loop(0, chunks, body, 0)


def edges_and_diagonal(modulus, below, above):
    rows_y, depth, width = modulus.shape
    vmem = pl.BlockSpec(memory_space=pltpu.VMEM)
    halo_below = jnp.broadcast_to(below[:, None], (rows_y, 8, width))
    halo_above = jnp.broadcast_to(above[:, None], (rows_y, 8, width))
    return pl.pallas_call(
        edges_kernel,
        out_shape=(
            jax.ShapeDtypeStruct((len(OFFSETS), rows_y, depth, width), jnp.float32),
            jax.ShapeDtypeStruct((rows_y, depth, width), jnp.float32),
            jax.ShapeDtypeStruct((3, rows_y, depth, width), jnp.float32),
        ),
        in_specs=[vmem, vmem, vmem],
        out_specs=(vmem, vmem, vmem),
        cost_estimate=pl.CostEstimate(
            flops=26 * 8 * modulus.size, bytes_accessed=4 * 31 * modulus.size, transcendentals=0
        ),
    )(modulus, halo_below, halo_above)


def stencil_kernel(field_ref, below_ref, above_ref, edge_ref, cm_ref, out_ref):
    samples, _, rows_y, depth, width = field_ref.shape
    chunks = depth // 8
    sub = lax.broadcasted_iota(jnp.int32, (8, width), 0)
    lane = lax.broadcasted_iota(jnp.int32, (8, width), 1)

    def body(it, carry):
        s = it // chunks
        r = pl.multiple_of((it % chunks) * 8, 8)

        first = (it % chunks) == 0
        last = (it % chunks) == chunks - 1

        def rows(c, y, off):
            if off == 0:
                return field_ref[s, c, y, pl.ds(r, 8), :]
            if off < 0:
                return jnp.where(
                    first, below_ref[s, c, y], field_ref[s, c, y, pl.ds(jnp.maximum(r - 8, 0), 8), :]
                )
            return jnp.where(
                last, above_ref[s, c, y], field_ref[s, c, y, pl.ds(jnp.minimum(r + 8, depth - 8), 8), :]
            )

        centre = [[rows(c, y, 0) for y in range(rows_y)] for c in range(3)]
        acc = [
            [GAMMA * cm_ref[y, pl.ds(r, 8), :] * centre[c][y] for y in range(rows_y)]
            for c in range(3)
        ]
        index = 0
        for off_x in (-1, 0, 1):
            if off_x == 0:
                shifted_x = centre
            elif off_x < 0:
                shifted_x = [
                    [
                        jnp.where(
                            sub == 0,
                            pltpu.roll(rows(c, y, -1), 1, 0),
                            pltpu.roll(centre[c][y], 1, 0),
                        )
                        for y in range(rows_y)
                    ]
                    for c in range(3)
                ]
            else:
                shifted_x = [
                    [
                        jnp.where(
                            sub == 7,
                            pltpu.roll(rows(c, y, 1), 7, 0),
                            pltpu.roll(centre[c][y], 7, 0),
                        )
                        for y in range(rows_y)
                    ]
                    for c in range(3)
                ]
            shifted = {}
            for off_z in (-1, 0, 1):
                if off_z == 0:
                    shifted[off_z] = shifted_x
                elif off_z < 0:
                    shifted[off_z] = [
                        [
                            jnp.where(lane == 0, jnp.float32(0.0), pltpu.roll(v, 1, 1))
                            for v in per_c
                        ]
                        for per_c in shifted_x
                    ]
                else:
                    shifted[off_z] = [
                        [
                            jnp.where(lane == width - 1, jnp.float32(0.0), pltpu.roll(v, width - 1, 1))
                            for v in per_c
                        ]
                        for per_c in shifted_x
                    ]
            for off_y in (-1, 0, 1):
                for off_z in (-1, 0, 1):
                    if (off_x, off_y, off_z) == (0, 0, 0):
                        continue
                    offset = (off_x, off_y, off_z)
                    norm_sq = off_x * off_x + off_y * off_y + off_z * off_z
                    for y in range(rows_y):
                        edge = edge_ref[index, y, pl.ds(r, 8), :]
                        source = y + off_y
                        if 0 <= source < rows_y:
                            delta = [centre[c][y] - shifted[off_z][c][source] for c in range(3)]
                        else:
                            delta = [centre[c][y] for c in range(3)]
                        project = None
                        for c in range(3):
                            if offset[c] > 0:
                                project = delta[c] if project is None else project + delta[c]
                            elif offset[c] < 0:
                                project = -delta[c] if project is None else project - delta[c]
                        if norm_sq == 2:
                            project = project * 0.5
                        elif norm_sq == 3:
                            project = project * (1.0 / 3.0)
                        for c in range(3):
                            if offset[c] != 0:
                                acc[c][y] = acc[c][y] + edge * (delta[c] + BETA * offset[c] * project)
                            else:
                                acc[c][y] = acc[c][y] + edge * delta[c]
                    index += 1
        for c in range(3):
            for y in range(rows_y):
                out_ref[s, c, y, pl.ds(r, 8), :] = acc[c][y]
        return carry

    lax.fori_loop(0, samples * chunks, body, 0)


def stiffness(field, below, above, edges, centre_mod):
    samples, _, rows_y, depth, width = field.shape
    halo_shape = (samples, 3, rows_y, 8, width)
    halo_below = jnp.broadcast_to(below[:, :, :, None], halo_shape)
    halo_above = jnp.broadcast_to(above[:, :, :, None], halo_shape)
    vmem = pl.BlockSpec(memory_space=pltpu.VMEM)
    size = samples * 3 * rows_y * depth * width
    return pl.pallas_call(
        stencil_kernel,
        out_shape=jax.ShapeDtypeStruct(field.shape, jnp.float32),
        in_specs=[vmem] * 5,
        out_specs=vmem,
        cost_estimate=pl.CostEstimate(flops=26 * 20 * size, bytes_accessed=4 * (2 * size + 28 * size // samples // 3), transcendentals=0),
    )(field, halo_below, halo_above, edges, centre_mod)


def lookup_modulus(material, moduli):
    modulus = jnp.zeros(material.shape, jnp.float32)
    for index in range(MATERIALS):
        modulus = modulus + jnp.where(material == index, moduli[index], jnp.float32(0.0))
    return modulus


def neighbour_devices(part_device, partners):
    count = part_device.shape[0]
    ids = jnp.arange(count, dtype=jnp.int32)
    place = jnp.zeros((count,), jnp.int32).at[part_device].set(ids)
    parity = place % 2
    up_dev = partners[parity, ids]
    low_dev = partners[1 - parity, ids]
    return up_dev, low_dev


def exchange(first, last, up_dev, low_dev):
    col = lax.axis_index("col")
    grp = lax.axis_index("grp")
    me = col * GROUP + grp
    cols = up_dev.shape[0] // GROUP
    pack = jnp.stack([first, last], axis=0)[None]
    held = lax.all_gather(pack, "grp", axis=0, tiled=True)
    targets = jnp.arange(cols, dtype=jnp.int32) * GROUP + grp
    t_up = up_dev[targets]
    t_low = low_dev[targets]
    up_here = (t_up // GROUP) == col
    low_here = (t_low // GROUP) == col
    from_up = held[t_up % GROUP, 0]
    from_low = held[t_low % GROUP, 1]
    shape = (cols,) + (1,) * (from_up.ndim - 1)
    from_up = jnp.where(up_here.reshape(shape), from_up, jnp.float32(0.0))
    from_low = jnp.where(low_here.reshape(shape), from_low, jnp.float32(0.0))
    slots = jnp.stack([from_up, from_low], axis=1)
    got = lax.all_to_all(slots, "col", 0, 0, tiled=True)
    my_up = up_dev[me]
    my_low = low_dev[me]
    above = got[my_up // GROUP, 0]
    below = got[my_low // GROUP, 1]
    above = jnp.where(my_up != me, above, jnp.float32(0.0))
    below = jnp.where(my_low != me, below, jnp.float32(0.0))
    return below, above


def on_device(loads, modal_disp, material, moduli, part_device, partners, low_bound, high_bound):
    up_dev, low_dev = neighbour_devices(part_device, partners)
    samples, _, depth, rows_y, width = loads.shape
    loads = jnp.transpose(loads, (0, 1, 3, 2, 4))
    modal_disp = jnp.transpose(modal_disp, (0, 1, 3, 2, 4))
    modulus = jnp.transpose(lookup_modulus(material, moduli), (1, 0, 2))
    plane = (samples, 3, rows_y, width)
    plane_size = samples * 3 * rows_y * width
    mod_size = rows_y * width

    def pack(md_rows, load_rows):
        parts = [modal_disp[:, :, :, r].reshape(-1) for r in md_rows]
        parts += [loads[:, :, :, r].reshape(-1) for r in load_rows]
        parts += [modulus[:, r].reshape(-1) for r in md_rows]
        return jnp.concatenate(parts)

    first = pack((0, 1, 2), (0, 1))
    last = pack((depth - 3, depth - 2, depth - 1), (depth - 2, depth - 1))
    below, above = exchange(first, last, up_dev, low_dev)

    def planes_of(got, count, start, size, shape):
        return [got[start + i * size : start + (i + 1) * size].reshape(shape) for i in range(count)]

    md_below = planes_of(below, 3, 0, plane_size, plane)
    md_above = planes_of(above, 3, 0, plane_size, plane)
    ld_below = planes_of(below, 2, 3 * plane_size, plane_size, plane)
    ld_above = planes_of(above, 2, 3 * plane_size, plane_size, plane)
    mod_below = planes_of(below, 3, 5 * plane_size, mod_size, (rows_y, width))
    mod_above = planes_of(above, 3, 5 * plane_size, mod_size, (rows_y, width))

    def extend(own, lower, upper, axis):
        zero = jnp.zeros_like(lower[0])
        rows = [zero] * (8 - len(lower)) + list(lower)
        tail = list(upper) + [zero] * (8 - len(upper))
        return jnp.concatenate(
            [jnp.stack(rows, axis=axis), own, jnp.stack(tail, axis=axis)], axis=axis
        )

    low_on = low_dev[col_grp_index()] != col_grp_index()
    up_on = up_dev[col_grp_index()] != col_grp_index()
    zero_mod = jnp.zeros((rows_y, width), jnp.float32)
    zero_plane = jnp.zeros(plane, jnp.float32)

    theta = (high_bound[0] + low_bound[0]) / 2.0
    half = (high_bound[0] - low_bound[0]) / 2.0
    sigma = theta / half
    rho0 = 1.0 / sigma
    rho1 = 1.0 / (2.0 * sigma - rho0)

    def chain(md, ld, mod, valid):
        edges, centre_mod, jacobi = edges_and_diagonal(mod, zero_mod, zero_mod)

        def apply(field):
            return stiffness(field, zero_plane, zero_plane, edges, centre_mod)

        start = ld - apply(md)
        step0 = start / (theta * jacobi)
        if valid is not None:
            step0 = jnp.where(valid(2), step0, jnp.float32(0.0))
        residual1 = start - apply(step0)
        step1 = rho1 * rho0 * step0 + 2.0 * rho1 / half * residual1 / jacobi
        if valid is not None:
            step1 = jnp.where(valid(1), step1, jnp.float32(0.0))
        displacement = md + step0 + step1
        residual = residual1 - apply(step1)
        return displacement, residual

    disp_local, res_local = chain(modal_disp, loads, modulus, None)

    edge_rows = 16
    head = slice(0, edge_rows)
    tail = slice(depth - edge_rows, depth)

    def window(own, lower, upper, axis):
        zero = jnp.zeros_like(lower[0])
        rows = [zero] * (8 - len(lower)) + list(lower)
        after = list(upper) + [zero] * (8 - len(upper))
        index = [slice(None)] * own.ndim
        index[axis] = head
        own_head = own[tuple(index)]
        index[axis] = tail
        own_tail = own[tuple(index)]
        return jnp.concatenate(
            [jnp.stack(rows, axis=axis), own_head, own_tail, jnp.stack(after, axis=axis)], axis=axis
        )

    md_win = window(modal_disp, md_below, md_above, 3)
    ld_win = window(loads, ld_below, ld_above, 3)
    mod_win = window(modulus, mod_below, mod_above, 1)
    logical = jnp.concatenate(
        [
            jnp.arange(-8, edge_rows, dtype=jnp.int32),
            jnp.arange(depth - edge_rows, depth + 8, dtype=jnp.int32),
        ]
    )

    def valid(reach):
        keep = (logical >= 0) & (logical < depth)
        keep = keep | (low_on & (logical >= -reach) & (logical < 0))
        keep = keep | (up_on & (logical >= depth) & (logical < depth + reach))
        return keep.reshape(-1, 1)

    disp_win, res_win = chain(md_win, ld_win, mod_win, valid)

    def merge(local, win):
        return jnp.concatenate(
            [
                win[:, :, :, 8:16],
                local[:, :, :, 8 : depth - 8],
                win[:, :, :, 8 + 2 * edge_rows - 8 : 8 + 2 * edge_rows],
            ],
            axis=3,
        )

    displacement = merge(disp_local, disp_win)
    residual = merge(res_local, res_win)
    return (
        jnp.transpose(displacement, (0, 1, 3, 2, 4)),
        jnp.transpose(residual, (0, 1, 3, 2, 4)),
    )


def col_grp_index():
    return lax.axis_index("col") * GROUP + lax.axis_index("grp")


def solution(mesh):
    devices = mesh.devices.reshape(-1)
    grid = Mesh(devices.reshape(devices.size // GROUP, GROUP), ("col", "grp"))
    slab = ("col", "grp")
    in_specs = (
        P(None, None, slab, None, None),
        P(None, None, slab, None, None),
        P(slab, None, None),
        P(),
        P(),
        P(),
        P(),
        P(),
    )
    out_specs = (P(None, None, slab, None, None), P(None, None, slab, None, None))
    return jax.shard_map(
        on_device, mesh=grid, in_specs=in_specs, out_specs=out_specs, check_vma=False
    )
```

```python
import jax
import jax.numpy as jnp
from jax import lax
from jax.experimental import pallas as pl
from jax.experimental.pallas import tpu as pltpu
from jax.sharding import Mesh, PartitionSpec as P

MATERIALS = 8
GROUP = 8

GAMMA = 0.2
BETA = 0.5
EDGE_WEIGHTS = (0.0, 1.0, 0.5, 0.25)
OFFSETS = [
    (a, b, c) for a in (-1, 0, 1) for b in (-1, 0, 1) for c in (-1, 0, 1) if (a, b, c) != (0, 0, 0)
]


def shift_cells(array, axis, step):
    if step == 0:
        return array
    length = array.shape[axis]
    zero = jnp.zeros_like(lax.slice_in_dim(array, 0, 1, axis=axis))
    if step > 0:
        return jnp.concatenate([lax.slice_in_dim(array, 1, length, axis=axis), zero], axis=axis)
    return jnp.concatenate([zero, lax.slice_in_dim(array, 0, length - 1, axis=axis)], axis=axis)


def mod_neighbour(mod_ext, off_x, off_y, off_z, depth):
    rows = lax.slice_in_dim(mod_ext, 1 + off_x, 1 + off_x + depth, axis=1)
    return shift_cells(shift_cells(rows, 0, off_y), 2, off_z)


def edges_of(mod_ext, depth):
    centre = mod_neighbour(mod_ext, 0, 0, 0, depth)
    edges = []
    for offset in OFFSETS:
        norm_sq = offset[0] * offset[0] + offset[1] * offset[1] + offset[2] * offset[2]
        edges.append(
            EDGE_WEIGHTS[norm_sq]
            * 0.5
            * (centre + mod_neighbour(mod_ext, offset[0], offset[1], offset[2], depth))
        )
    return centre, edges


def diagonal_of(centre, edges):
    comps = [GAMMA * centre, GAMMA * centre, GAMMA * centre]
    for offset, edge in zip(OFFSETS, edges):
        norm_sq = offset[0] * offset[0] + offset[1] * offset[1] + offset[2] * offset[2]
        for comp in range(3):
            comps[comp] = comps[comp] + edge * (1.0 + BETA * offset[comp] * offset[comp] / norm_sq)
    return jnp.stack(comps, axis=0)


def edges_kernel(mod_ref, below_ref, above_ref, edge_ref, centre_ref, diag_ref):
    rows_y, depth, width = mod_ref.shape
    chunks = depth // 8
    sub = lax.broadcasted_iota(jnp.int32, (8, width), 0)
    lane = lax.broadcasted_iota(jnp.int32, (8, width), 1)

    def body(it, carry):
        r = pl.multiple_of(it * 8, 8)
        centre = [mod_ref[y, pl.ds(r, 8), :] for y in range(rows_y)]
        prev = [
            jnp.where(it == 0, below_ref[y], mod_ref[y, pl.ds(jnp.maximum(r - 8, 0), 8), :])
            for y in range(rows_y)
        ]
        nxt = [
            jnp.where(
                it == chunks - 1, above_ref[y], mod_ref[y, pl.ds(jnp.minimum(r + 8, depth - 8), 8), :]
            )
            for y in range(rows_y)
        ]
        comps = [[GAMMA * centre[y] for y in range(rows_y)] for c in range(3)]
        index = 0
        for off_x in (-1, 0, 1):
            if off_x == 0:
                shifted_x = centre
            elif off_x < 0:
                shifted_x = [
                    jnp.where(sub == 0, pltpu.roll(prev[y], 1, 0), pltpu.roll(centre[y], 1, 0))
                    for y in range(rows_y)
                ]
            else:
                shifted_x = [
                    jnp.where(sub == 7, pltpu.roll(nxt[y], 7, 0), pltpu.roll(centre[y], 7, 0))
                    for y in range(rows_y)
                ]
            shifted = {0: shifted_x}
            shifted[-1] = [jnp.where(lane == 0, jnp.float32(0.0), pltpu.roll(v, 1, 1)) for v in shifted_x]
            shifted[1] = [
                jnp.where(lane == width - 1, jnp.float32(0.0), pltpu.roll(v, width - 1, 1))
                for v in shifted_x
            ]
            for off_y in (-1, 0, 1):
                for off_z in (-1, 0, 1):
                    if (off_x, off_y, off_z) == (0, 0, 0):
                        continue
                    offset = (off_x, off_y, off_z)
                    norm_sq = off_x * off_x + off_y * off_y + off_z * off_z
                    for y in range(rows_y):
                        source = y + off_y
                        if 0 <= source < rows_y:
                            other = shifted[off_z][source]
                        else:
                            other = jnp.zeros_like(centre[y])
                        edge = EDGE_WEIGHTS[norm_sq] * 0.5 * (centre[y] + other)
                        edge_ref[index, y, pl.ds(r, 8), :] = edge
                        for c in range(3):
                            comps[c][y] = comps[c][y] + edge * (
                                1.0 + BETA * offset[c] * offset[c] / norm_sq
                            )
                    index += 1
        for y in range(rows_y):
            centre_ref[y, pl.ds(r, 8), :] = centre[y]
            for c in range(3):
                diag_ref[c, y, pl.ds(r, 8), :] = comps[c][y]
        return carry

    lax.fori_loop(0, chunks, body, 0)


def edges_and_diagonal(modulus, below, above):
    rows_y, depth, width = modulus.shape
    vmem = pl.BlockSpec(memory_space=pltpu.VMEM)
    halo_below = jnp.broadcast_to(below[:, None], (rows_y, 8, width))
    halo_above = jnp.broadcast_to(above[:, None], (rows_y, 8, width))
    return pl.pallas_call(
        edges_kernel,
        out_shape=(
            jax.ShapeDtypeStruct((len(OFFSETS), rows_y, depth, width), jnp.float32),
            jax.ShapeDtypeStruct((rows_y, depth, width), jnp.float32),
            jax.ShapeDtypeStruct((3, rows_y, depth, width), jnp.float32),
        ),
        in_specs=[vmem, vmem, vmem],
        out_specs=(vmem, vmem, vmem),
        cost_estimate=pl.CostEstimate(
            flops=26 * 8 * modulus.size, bytes_accessed=4 * 31 * modulus.size, transcendentals=0
        ),
    )(modulus, halo_below, halo_above)


def stencil_kernel(field_ref, below_ref, above_ref, edge_ref, cm_ref, out_ref):
    samples, _, rows_y, depth, width = field_ref.shape
    chunks = depth // 8
    sub = lax.broadcasted_iota(jnp.int32, (8, width), 0)
    lane = lax.broadcasted_iota(jnp.int32, (8, width), 1)

    def body(it, carry):
        s = it // chunks
        r = pl.multiple_of((it % chunks) * 8, 8)

        first = (it % chunks) == 0
        last = (it % chunks) == chunks - 1

        def rows(c, y, off):
            if off == 0:
                return field_ref[s, c, y, pl.ds(r, 8), :]
            if off < 0:
                return jnp.where(
                    first, below_ref[s, c, y], field_ref[s, c, y, pl.ds(jnp.maximum(r - 8, 0), 8), :]
                )
            return jnp.where(
                last, above_ref[s, c, y], field_ref[s, c, y, pl.ds(jnp.minimum(r + 8, depth - 8), 8), :]
            )

        centre = [[rows(c, y, 0) for y in range(rows_y)] for c in range(3)]
        acc = [
            [GAMMA * cm_ref[y, pl.ds(r, 8), :] * centre[c][y] for y in range(rows_y)]
            for c in range(3)
        ]
        index = 0
        for off_x in (-1, 0, 1):
            if off_x == 0:
                shifted_x = centre
            elif off_x < 0:
                shifted_x = [
                    [
                        jnp.where(
                            sub == 0,
                            pltpu.roll(rows(c, y, -1), 1, 0),
                            pltpu.roll(centre[c][y], 1, 0),
                        )
                        for y in range(rows_y)
                    ]
                    for c in range(3)
                ]
            else:
                shifted_x = [
                    [
                        jnp.where(
                            sub == 7,
                            pltpu.roll(rows(c, y, 1), 7, 0),
                            pltpu.roll(centre[c][y], 7, 0),
                        )
                        for y in range(rows_y)
                    ]
                    for c in range(3)
                ]
            shifted = {}
            for off_z in (-1, 0, 1):
                if off_z == 0:
                    shifted[off_z] = shifted_x
                elif off_z < 0:
                    shifted[off_z] = [
                        [
                            jnp.where(lane == 0, jnp.float32(0.0), pltpu.roll(v, 1, 1))
                            for v in per_c
                        ]
                        for per_c in shifted_x
                    ]
                else:
                    shifted[off_z] = [
                        [
                            jnp.where(lane == width - 1, jnp.float32(0.0), pltpu.roll(v, width - 1, 1))
                            for v in per_c
                        ]
                        for per_c in shifted_x
                    ]
            for off_y in (-1, 0, 1):
                for off_z in (-1, 0, 1):
                    if (off_x, off_y, off_z) == (0, 0, 0):
                        continue
                    offset = (off_x, off_y, off_z)
                    norm_sq = off_x * off_x + off_y * off_y + off_z * off_z
                    for y in range(rows_y):
                        edge = edge_ref[index, y, pl.ds(r, 8), :]
                        source = y + off_y
                        if 0 <= source < rows_y:
                            delta = [centre[c][y] - shifted[off_z][c][source] for c in range(3)]
                        else:
                            delta = [centre[c][y] for c in range(3)]
                        project = None
                        for c in range(3):
                            if offset[c] > 0:
                                project = delta[c] if project is None else project + delta[c]
                            elif offset[c] < 0:
                                project = -delta[c] if project is None else project - delta[c]
                        if norm_sq == 2:
                            project = project * 0.5
                        elif norm_sq == 3:
                            project = project * (1.0 / 3.0)
                        for c in range(3):
                            if offset[c] != 0:
                                acc[c][y] = acc[c][y] + edge * (delta[c] + BETA * offset[c] * project)
                            else:
                                acc[c][y] = acc[c][y] + edge * delta[c]
                    index += 1
        for c in range(3):
            for y in range(rows_y):
                out_ref[s, c, y, pl.ds(r, 8), :] = acc[c][y]
        return carry

    lax.fori_loop(0, samples * chunks, body, 0)


def stiffness(field, below, above, edges, centre_mod):
    samples, _, rows_y, depth, width = field.shape
    halo_shape = (samples, 3, rows_y, 8, width)
    halo_below = jnp.broadcast_to(below[:, :, :, None], halo_shape)
    halo_above = jnp.broadcast_to(above[:, :, :, None], halo_shape)
    vmem = pl.BlockSpec(memory_space=pltpu.VMEM)
    size = samples * 3 * rows_y * depth * width
    return pl.pallas_call(
        stencil_kernel,
        out_shape=jax.ShapeDtypeStruct(field.shape, jnp.float32),
        in_specs=[vmem] * 5,
        out_specs=vmem,
        cost_estimate=pl.CostEstimate(flops=26 * 20 * size, bytes_accessed=4 * (2 * size + 28 * size // samples // 3), transcendentals=0),
    )(field, halo_below, halo_above, edges, centre_mod)


def lookup_modulus(material, moduli):
    modulus = jnp.zeros(material.shape, jnp.float32)
    for index in range(MATERIALS):
        modulus = modulus + jnp.where(material == index, moduli[index], jnp.float32(0.0))
    return modulus


def neighbour_devices(part_device, partners):
    count = part_device.shape[0]
    ids = jnp.arange(count, dtype=jnp.int32)
    place = jnp.zeros((count,), jnp.int32).at[part_device].set(ids)
    parity = place % 2
    up_dev = partners[parity, ids]
    low_dev = partners[1 - parity, ids]
    return up_dev, low_dev


def exchange(first, last, up_dev, low_dev):
    col = lax.axis_index("col")
    grp = lax.axis_index("grp")
    me = col * GROUP + grp
    cols = up_dev.shape[0] // GROUP
    pack = jnp.stack([first, last], axis=0)[None]
    held = lax.all_gather(pack, "grp", axis=0, tiled=True)
    targets = jnp.arange(cols, dtype=jnp.int32) * GROUP + grp
    t_up = up_dev[targets]
    t_low = low_dev[targets]
    up_here = (t_up // GROUP) == col
    low_here = (t_low // GROUP) == col
    from_up = held[t_up % GROUP, 0]
    from_low = held[t_low % GROUP, 1]
    shape = (cols,) + (1,) * (from_up.ndim - 1)
    from_up = jnp.where(up_here.reshape(shape), from_up, jnp.float32(0.0))
    from_low = jnp.where(low_here.reshape(shape), from_low, jnp.float32(0.0))
    slots = jnp.stack([from_up, from_low], axis=1)
    got = lax.all_to_all(slots, "col", 0, 0, tiled=True)
    my_up = up_dev[me]
    my_low = low_dev[me]
    above = got[my_up // GROUP, 0]
    below = got[my_low // GROUP, 1]
    above = jnp.where(my_up != me, above, jnp.float32(0.0))
    below = jnp.where(my_low != me, below, jnp.float32(0.0))
    return below, above


def on_device(loads, modal_disp, material, moduli, part_device, partners, low_bound, high_bound):
    up_dev, low_dev = neighbour_devices(part_device, partners)
    samples, _, depth, rows_y, width = loads.shape
    loads = jnp.transpose(loads, (0, 1, 3, 2, 4))
    modal_disp = jnp.transpose(modal_disp, (0, 1, 3, 2, 4))
    modulus = jnp.transpose(lookup_modulus(material, moduli), (1, 0, 2))
    plane = (samples, 3, rows_y, width)
    plane_size = samples * 3 * rows_y * width
    mod_size = rows_y * width

    def pack(md_rows, load_rows):
        parts = [modal_disp[:, :, :, r].reshape(-1) for r in md_rows]
        parts += [loads[:, :, :, r].reshape(-1) for r in load_rows]
        parts += [modulus[:, r].reshape(-1) for r in md_rows]
        return jnp.concatenate(parts)

    first = pack((0, 1, 2), (0, 1))
    last = pack((depth - 3, depth - 2, depth - 1), (depth - 2, depth - 1))
    below, above = exchange(first, last, up_dev, low_dev)

    def planes_of(got, count, start, size, shape):
        return [got[start + i * size : start + (i + 1) * size].reshape(shape) for i in range(count)]

    md_below = planes_of(below, 3, 0, plane_size, plane)
    md_above = planes_of(above, 3, 0, plane_size, plane)
    ld_below = planes_of(below, 2, 3 * plane_size, plane_size, plane)
    ld_above = planes_of(above, 2, 3 * plane_size, plane_size, plane)
    mod_below = planes_of(below, 3, 5 * plane_size, mod_size, (rows_y, width))
    mod_above = planes_of(above, 3, 5 * plane_size, mod_size, (rows_y, width))

    def extend(own, lower, upper, axis):
        zero = jnp.zeros_like(lower[0])
        rows = [zero] * (8 - len(lower)) + list(lower)
        tail = list(upper) + [zero] * (8 - len(upper))
        return jnp.concatenate(
            [jnp.stack(rows, axis=axis), own, jnp.stack(tail, axis=axis)], axis=axis
        )

    low_on = low_dev[col_grp_index()] != col_grp_index()
    up_on = up_dev[col_grp_index()] != col_grp_index()
    zero_mod = jnp.zeros((rows_y, width), jnp.float32)
    zero_plane = jnp.zeros(plane, jnp.float32)

    theta = (high_bound[0] + low_bound[0]) / 2.0
    half = (high_bound[0] - low_bound[0]) / 2.0
    sigma = theta / half
    rho0 = 1.0 / sigma
    rho1 = 1.0 / (2.0 * sigma - rho0)

    def chain(md, ld, mod, valid):
        edges, centre_mod, jacobi = edges_and_diagonal(mod, zero_mod, zero_mod)

        def apply(field):
            return stiffness(field, zero_plane, zero_plane, edges, centre_mod)

        start = ld - apply(md)
        step0 = start / (theta * jacobi)
        if valid is not None:
            step0 = jnp.where(valid(2), step0, jnp.float32(0.0))
        residual1 = start - apply(step0)
        step1 = rho1 * rho0 * step0 + 2.0 * rho1 / half * residual1 / jacobi
        if valid is not None:
            step1 = jnp.where(valid(1), step1, jnp.float32(0.0))
        displacement = md + step0 + step1
        residual = residual1 - apply(step1)
        return displacement, residual

    disp_local, res_local = chain(modal_disp, loads, modulus, None)

    edge_rows = 8
    head = slice(0, edge_rows)
    tail = slice(depth - edge_rows, depth)

    def window(own, lower, upper, axis):
        zero = jnp.zeros_like(lower[0])
        rows = [zero] * (8 - len(lower)) + list(lower)
        after = list(upper) + [zero] * (8 - len(upper))
        index = [slice(None)] * own.ndim
        index[axis] = head
        own_head = own[tuple(index)]
        index[axis] = tail
        own_tail = own[tuple(index)]
        return jnp.concatenate(
            [jnp.stack(rows, axis=axis), own_head, own_tail, jnp.stack(after, axis=axis)], axis=axis
        )

    md_win = window(modal_disp, md_below, md_above, 3)
    ld_win = window(loads, ld_below, ld_above, 3)
    mod_win = window(modulus, mod_below, mod_above, 1)
    logical = jnp.concatenate(
        [
            jnp.arange(-8, edge_rows, dtype=jnp.int32),
            jnp.arange(depth - edge_rows, depth + 8, dtype=jnp.int32),
        ]
    )

    def valid(reach):
        keep = (logical >= 0) & (logical < depth)
        keep = keep | (low_on & (logical >= -reach) & (logical < 0))
        keep = keep | (up_on & (logical >= depth) & (logical < depth + reach))
        return keep.reshape(-1, 1)

    disp_win, res_win = chain(md_win, ld_win, mod_win, valid)

    reach = 3
    sub_row = lax.broadcasted_iota(jnp.int32, (8, 1), 0)

    def merge(local, win):
        top = jnp.where(sub_row < reach, win[:, :, :, 8:16], local[:, :, :, 0:8])
        bottom = jnp.where(sub_row >= 8 - reach, win[:, :, :, 16:24], local[:, :, :, depth - 8 : depth])
        return jnp.concatenate([top, local[:, :, :, 8 : depth - 8], bottom], axis=3)

    displacement = merge(disp_local, disp_win)
    residual = merge(res_local, res_win)
    return (
        jnp.transpose(displacement, (0, 1, 3, 2, 4)),
        jnp.transpose(residual, (0, 1, 3, 2, 4)),
    )


def col_grp_index():
    return lax.axis_index("col") * GROUP + lax.axis_index("grp")


def solution(mesh):
    devices = mesh.devices.reshape(-1)
    grid = Mesh(devices.reshape(devices.size // GROUP, GROUP), ("col", "grp"))
    slab = ("col", "grp")
    in_specs = (
        P(None, None, slab, None, None),
        P(None, None, slab, None, None),
        P(slab, None, None),
        P(),
        P(),
        P(),
        P(),
        P(),
    )
    out_specs = (P(None, None, slab, None, None), P(None, None, slab, None, None))
    return jax.shard_map(
        on_device, mesh=grid, in_specs=in_specs, out_specs=out_specs, check_vma=False
    )
```

```python
import jax
import jax.numpy as jnp
from jax import lax
from jax.experimental import pallas as pl
from jax.experimental.pallas import tpu as pltpu
from jax.sharding import Mesh, PartitionSpec as P

MATERIALS = 8
GROUP = 8

GAMMA = 0.2
BETA = 0.5
EDGE_WEIGHTS = (0.0, 1.0, 0.5, 0.25)
OFFSETS = [
    (a, b, c) for a in (-1, 0, 1) for b in (-1, 0, 1) for c in (-1, 0, 1) if (a, b, c) != (0, 0, 0)
]


def shift_cells(array, axis, step):
    if step == 0:
        return array
    length = array.shape[axis]
    zero = jnp.zeros_like(lax.slice_in_dim(array, 0, 1, axis=axis))
    if step > 0:
        return jnp.concatenate([lax.slice_in_dim(array, 1, length, axis=axis), zero], axis=axis)
    return jnp.concatenate([zero, lax.slice_in_dim(array, 0, length - 1, axis=axis)], axis=axis)


def mod_neighbour(mod_ext, off_x, off_y, off_z, depth):
    rows = lax.slice_in_dim(mod_ext, 1 + off_x, 1 + off_x + depth, axis=1)
    return shift_cells(shift_cells(rows, 0, off_y), 2, off_z)


def edges_of(mod_ext, depth):
    centre = mod_neighbour(mod_ext, 0, 0, 0, depth)
    edges = []
    for offset in OFFSETS:
        norm_sq = offset[0] * offset[0] + offset[1] * offset[1] + offset[2] * offset[2]
        edges.append(
            EDGE_WEIGHTS[norm_sq]
            * 0.5
            * (centre + mod_neighbour(mod_ext, offset[0], offset[1], offset[2], depth))
        )
    return centre, edges


def diagonal_of(centre, edges):
    comps = [GAMMA * centre, GAMMA * centre, GAMMA * centre]
    for offset, edge in zip(OFFSETS, edges):
        norm_sq = offset[0] * offset[0] + offset[1] * offset[1] + offset[2] * offset[2]
        for comp in range(3):
            comps[comp] = comps[comp] + edge * (1.0 + BETA * offset[comp] * offset[comp] / norm_sq)
    return jnp.stack(comps, axis=0)


def edges_body(mod_ref, edge_ref, centre_ref, diag_ref):
    rows_y, depth, width = mod_ref.shape
    chunks = depth // 8
    sub = lax.broadcasted_iota(jnp.int32, (8, width), 0)
    lane = lax.broadcasted_iota(jnp.int32, (8, width), 1)
    zero = jnp.zeros((8, width), jnp.float32)

    def body(it, carry):
        r = pl.multiple_of(it * 8, 8)
        centre = [mod_ref[y, pl.ds(r, 8), :] for y in range(rows_y)]
        prev = [
            jnp.where(it == 0, zero, mod_ref[y, pl.ds(jnp.maximum(r - 8, 0), 8), :])
            for y in range(rows_y)
        ]
        nxt = [
            jnp.where(it == chunks - 1, zero, mod_ref[y, pl.ds(jnp.minimum(r + 8, depth - 8), 8), :])
            for y in range(rows_y)
        ]
        comps = [[GAMMA * centre[y] for y in range(rows_y)] for c in range(3)]
        index = 0
        for off_x in (-1, 0, 1):
            if off_x == 0:
                shifted_x = centre
            elif off_x < 0:
                shifted_x = [
                    jnp.where(sub == 0, pltpu.roll(prev[y], 1, 0), pltpu.roll(centre[y], 1, 0))
                    for y in range(rows_y)
                ]
            else:
                shifted_x = [
                    jnp.where(sub == 7, pltpu.roll(nxt[y], 7, 0), pltpu.roll(centre[y], 7, 0))
                    for y in range(rows_y)
                ]
            shifted = {0: shifted_x}
            shifted[-1] = [jnp.where(lane == 0, jnp.float32(0.0), pltpu.roll(v, 1, 1)) for v in shifted_x]
            shifted[1] = [
                jnp.where(lane == width - 1, jnp.float32(0.0), pltpu.roll(v, width - 1, 1))
                for v in shifted_x
            ]
            for off_y in (-1, 0, 1):
                for off_z in (-1, 0, 1):
                    if (off_x, off_y, off_z) == (0, 0, 0):
                        continue
                    offset = (off_x, off_y, off_z)
                    norm_sq = off_x * off_x + off_y * off_y + off_z * off_z
                    for y in range(rows_y):
                        source = y + off_y
                        if 0 <= source < rows_y:
                            other = shifted[off_z][source]
                        else:
                            other = zero
                        edge = EDGE_WEIGHTS[norm_sq] * 0.5 * (centre[y] + other)
                        edge_ref[index, y, pl.ds(r, 8), :] = edge
                        for c in range(3):
                            comps[c][y] = comps[c][y] + edge * (
                                1.0 + BETA * offset[c] * offset[c] / norm_sq
                            )
                    index += 1
        for y in range(rows_y):
            centre_ref[y, pl.ds(r, 8), :] = centre[y]
            for c in range(3):
                diag_ref[c, y, pl.ds(r, 8), :] = comps[c][y]
        return carry

    lax.fori_loop(0, chunks, body, 0)


def stencil_body(field_ref, edge_ref, cm_ref, out_ref):
    samples, _, rows_y, depth, width = field_ref.shape
    chunks = depth // 8
    sub = lax.broadcasted_iota(jnp.int32, (8, width), 0)
    lane = lax.broadcasted_iota(jnp.int32, (8, width), 1)
    zero = jnp.zeros((8, width), jnp.float32)

    def body(it, carry):
        s = it // chunks
        part = it % chunks
        r = pl.multiple_of(part * 8, 8)

        def rows(c, y, off):
            if off == 0:
                return field_ref[s, c, y, pl.ds(r, 8), :]
            if off < 0:
                return jnp.where(
                    part == 0, zero, field_ref[s, c, y, pl.ds(jnp.maximum(r - 8, 0), 8), :]
                )
            return jnp.where(
                part == chunks - 1,
                zero,
                field_ref[s, c, y, pl.ds(jnp.minimum(r + 8, depth - 8), 8), :],
            )

        centre = [[rows(c, y, 0) for y in range(rows_y)] for c in range(3)]
        acc = [
            [GAMMA * cm_ref[y, pl.ds(r, 8), :] * centre[c][y] for y in range(rows_y)]
            for c in range(3)
        ]
        index = 0
        for off_x in (-1, 0, 1):
            if off_x == 0:
                shifted_x = centre
            elif off_x < 0:
                shifted_x = [
                    [
                        jnp.where(
                            sub == 0,
                            pltpu.roll(rows(c, y, -1), 1, 0),
                            pltpu.roll(centre[c][y], 1, 0),
                        )
                        for y in range(rows_y)
                    ]
                    for c in range(3)
                ]
            else:
                shifted_x = [
                    [
                        jnp.where(
                            sub == 7,
                            pltpu.roll(rows(c, y, 1), 7, 0),
                            pltpu.roll(centre[c][y], 7, 0),
                        )
                        for y in range(rows_y)
                    ]
                    for c in range(3)
                ]
            shifted = {0: shifted_x}
            shifted[-1] = [
                [jnp.where(lane == 0, jnp.float32(0.0), pltpu.roll(v, 1, 1)) for v in per_c]
                for per_c in shifted_x
            ]
            shifted[1] = [
                [
                    jnp.where(lane == width - 1, jnp.float32(0.0), pltpu.roll(v, width - 1, 1))
                    for v in per_c
                ]
                for per_c in shifted_x
            ]
            for off_y in (-1, 0, 1):
                for off_z in (-1, 0, 1):
                    if (off_x, off_y, off_z) == (0, 0, 0):
                        continue
                    offset = (off_x, off_y, off_z)
                    norm_sq = off_x * off_x + off_y * off_y + off_z * off_z
                    for y in range(rows_y):
                        edge = edge_ref[index, y, pl.ds(r, 8), :]
                        source = y + off_y
                        if 0 <= source < rows_y:
                            delta = [centre[c][y] - shifted[off_z][c][source] for c in range(3)]
                        else:
                            delta = [centre[c][y] for c in range(3)]
                        project = None
                        for c in range(3):
                            if offset[c] > 0:
                                project = delta[c] if project is None else project + delta[c]
                            elif offset[c] < 0:
                                project = -delta[c] if project is None else project - delta[c]
                        if norm_sq == 2:
                            project = project * 0.5
                        elif norm_sq == 3:
                            project = project * (1.0 / 3.0)
                        for c in range(3):
                            if offset[c] != 0:
                                acc[c][y] = acc[c][y] + edge * (delta[c] + BETA * offset[c] * project)
                            else:
                                acc[c][y] = acc[c][y] + edge * delta[c]
                    index += 1
        for c in range(3):
            for y in range(rows_y):
                out_ref[s, c, y, pl.ds(r, 8), :] = acc[c][y]
        return carry

    lax.fori_loop(0, samples * chunks, body, 0)


def chain_kernel(
    scal_ref, mask_ref, md_ref, ld_ref, mod_ref, disp_ref, res_ref,
    edge_s, cm_s, jac_s, k_s, a_s, step0_s, step1_s,
):
    samples, _, rows_y, depth, width = md_ref.shape
    theta = scal_ref[0]
    c1 = scal_ref[1]
    c2 = scal_ref[2]
    edges_body(mod_ref, edge_s, cm_s, jac_s)
    stencil_body(md_ref, edge_s, cm_s, k_s)
    keep0 = mask_ref[0] > 0.0
    keep1 = mask_ref[1] > 0.0

    def first(it, carry):
        s = it // 3
        c = it % 3
        for y in range(rows_y):
            start = ld_ref[s, c, y] - k_s[s, c, y]
            a_s[s, c, y] = start
            step0_s[s, c, y] = jnp.where(keep0, start / (theta * jac_s[c, y]), jnp.float32(0.0))
        return carry

    lax.fori_loop(0, samples * 3, first, 0)
    stencil_body(step0_s, edge_s, cm_s, k_s)

    def second(it, carry):
        s = it // 3
        c = it % 3
        for y in range(rows_y):
            residual1 = a_s[s, c, y] - k_s[s, c, y]
            a_s[s, c, y] = residual1
            step0 = step0_s[s, c, y]
            step1 = jnp.where(
                keep1, c1 * step0 + c2 * residual1 / jac_s[c, y], jnp.float32(0.0)
            )
            step1_s[s, c, y] = step1
            disp_ref[s, c, y] = md_ref[s, c, y] + step0 + step1
        return carry

    lax.fori_loop(0, samples * 3, second, 0)
    stencil_body(step1_s, edge_s, cm_s, k_s)

    def third(it, carry):
        s = it // 3
        c = it % 3
        for y in range(rows_y):
            res_ref[s, c, y] = a_s[s, c, y] - k_s[s, c, y]
        return carry

    lax.fori_loop(0, samples * 3, third, 0)


def run_chain(scalars, masks, md, ld, mod):
    samples, _, rows_y, depth, width = md.shape
    vmem = pl.BlockSpec(memory_space=pltpu.VMEM)
    smem = pl.BlockSpec(memory_space=pltpu.SMEM)
    field = jax.ShapeDtypeStruct(md.shape, jnp.float32)
    size = md.size
    return pl.pallas_call(
        chain_kernel,
        out_shape=(field, field),
        in_specs=[smem, vmem, vmem, vmem, vmem],
        out_specs=(vmem, vmem),
        scratch_shapes=[
            pltpu.VMEM((len(OFFSETS), rows_y, depth, width), jnp.float32),
            pltpu.VMEM((rows_y, depth, width), jnp.float32),
            pltpu.VMEM((3, rows_y, depth, width), jnp.float32),
        ]
        + [pltpu.VMEM(md.shape, jnp.float32)] * 4,
        compiler_params=pltpu.CompilerParams(vmem_limit_bytes=48 * 1024 * 1024),
        cost_estimate=pl.CostEstimate(
            flops=3 * 26 * 20 * size, bytes_accessed=4 * 5 * size, transcendentals=0
        ),
    )(scalars, masks, md, ld, mod)


def lookup_modulus(material, moduli):
    modulus = jnp.zeros(material.shape, jnp.float32)
    for index in range(MATERIALS):
        modulus = modulus + jnp.where(material == index, moduli[index], jnp.float32(0.0))
    return modulus


def neighbour_devices(part_device, partners):
    count = part_device.shape[0]
    ids = jnp.arange(count, dtype=jnp.int32)
    place = jnp.zeros((count,), jnp.int32).at[part_device].set(ids)
    parity = place % 2
    up_dev = partners[parity, ids]
    low_dev = partners[1 - parity, ids]
    return up_dev, low_dev


def exchange(first, last, up_dev, low_dev):
    col = lax.axis_index("col")
    grp = lax.axis_index("grp")
    me = col * GROUP + grp
    cols = up_dev.shape[0] // GROUP
    pack = jnp.stack([first, last], axis=0)[None]
    held = lax.all_gather(pack, "grp", axis=0, tiled=True)
    targets = jnp.arange(cols, dtype=jnp.int32) * GROUP + grp
    t_up = up_dev[targets]
    t_low = low_dev[targets]
    up_here = (t_up // GROUP) == col
    low_here = (t_low // GROUP) == col
    from_up = held[t_up % GROUP, 0]
    from_low = held[t_low % GROUP, 1]
    shape = (cols,) + (1,) * (from_up.ndim - 1)
    from_up = jnp.where(up_here.reshape(shape), from_up, jnp.float32(0.0))
    from_low = jnp.where(low_here.reshape(shape), from_low, jnp.float32(0.0))
    slots = jnp.stack([from_up, from_low], axis=1)
    got = lax.all_to_all(slots, "col", 0, 0, tiled=True)
    my_up = up_dev[me]
    my_low = low_dev[me]
    above = got[my_up // GROUP, 0]
    below = got[my_low // GROUP, 1]
    above = jnp.where(my_up != me, above, jnp.float32(0.0))
    below = jnp.where(my_low != me, below, jnp.float32(0.0))
    return below, above


def on_device(loads, modal_disp, material, moduli, part_device, partners, low_bound, high_bound):
    up_dev, low_dev = neighbour_devices(part_device, partners)
    samples, _, depth, rows_y, width = loads.shape
    loads = jnp.transpose(loads, (0, 1, 3, 2, 4))
    modal_disp = jnp.transpose(modal_disp, (0, 1, 3, 2, 4))
    modulus = jnp.transpose(lookup_modulus(material, moduli), (1, 0, 2))
    plane = (samples, 3, rows_y, width)
    plane_size = samples * 3 * rows_y * width
    mod_size = rows_y * width

    def pack(md_rows, load_rows):
        parts = [modal_disp[:, :, :, r].reshape(-1) for r in md_rows]
        parts += [loads[:, :, :, r].reshape(-1) for r in load_rows]
        parts += [modulus[:, r].reshape(-1) for r in md_rows]
        return jnp.concatenate(parts)

    first = pack((0, 1, 2), (0, 1))
    last = pack((depth - 3, depth - 2, depth - 1), (depth - 2, depth - 1))
    below, above = exchange(first, last, up_dev, low_dev)

    def planes_of(got, count, start, size, shape):
        return [got[start + i * size : start + (i + 1) * size].reshape(shape) for i in range(count)]

    md_below = planes_of(below, 3, 0, plane_size, plane)
    md_above = planes_of(above, 3, 0, plane_size, plane)
    ld_below = planes_of(below, 2, 3 * plane_size, plane_size, plane)
    ld_above = planes_of(above, 2, 3 * plane_size, plane_size, plane)
    mod_below = planes_of(below, 3, 5 * plane_size, mod_size, (rows_y, width))
    mod_above = planes_of(above, 3, 5 * plane_size, mod_size, (rows_y, width))

    def extend(own, lower, upper, axis):
        zero = jnp.zeros_like(lower[0])
        rows = [zero] * (8 - len(lower)) + list(lower)
        tail = list(upper) + [zero] * (8 - len(upper))
        return jnp.concatenate(
            [jnp.stack(rows, axis=axis), own, jnp.stack(tail, axis=axis)], axis=axis
        )

    low_on = low_dev[col_grp_index()] != col_grp_index()
    up_on = up_dev[col_grp_index()] != col_grp_index()
    zero_mod = jnp.zeros((rows_y, width), jnp.float32)
    zero_plane = jnp.zeros(plane, jnp.float32)

    theta = (high_bound[0] + low_bound[0]) / 2.0
    half = (high_bound[0] - low_bound[0]) / 2.0
    sigma = theta / half
    rho0 = 1.0 / sigma
    rho1 = 1.0 / (2.0 * sigma - rho0)

    scalars = jnp.stack([theta, rho1 * rho0, 2.0 * rho1 / half]).astype(jnp.float32)

    def chain(md, ld, mod, masks):
        return run_chain(scalars, masks, md, ld, mod)

    disp_local, res_local = chain(modal_disp, loads, modulus, jnp.ones((2, depth, width), jnp.float32))

    edge_rows = 8
    head = slice(0, edge_rows)
    tail = slice(depth - edge_rows, depth)

    def window(own, lower, upper, axis):
        zero = jnp.zeros_like(lower[0])
        rows = [zero] * (8 - len(lower)) + list(lower)
        after = list(upper) + [zero] * (8 - len(upper))
        index = [slice(None)] * own.ndim
        index[axis] = head
        own_head = own[tuple(index)]
        index[axis] = tail
        own_tail = own[tuple(index)]
        return jnp.concatenate(
            [jnp.stack(rows, axis=axis), own_head, own_tail, jnp.stack(after, axis=axis)], axis=axis
        )

    md_win = window(modal_disp, md_below, md_above, 3)
    ld_win = window(loads, ld_below, ld_above, 3)
    mod_win = window(modulus, mod_below, mod_above, 1)
    logical = jnp.concatenate(
        [
            jnp.arange(-8, edge_rows, dtype=jnp.int32),
            jnp.arange(depth - edge_rows, depth + 8, dtype=jnp.int32),
        ]
    )

    def valid(reach):
        keep = (logical >= 0) & (logical < depth)
        keep = keep | (low_on & (logical >= -reach) & (logical < 0))
        keep = keep | (up_on & (logical >= depth) & (logical < depth + reach))
        return jnp.broadcast_to(keep.astype(jnp.float32)[:, None], (logical.shape[0], width))

    masks = jnp.stack([valid(2), valid(1)], axis=0)
    disp_win, res_win = chain(md_win, ld_win, mod_win, masks)

    reach = 3
    sub_row = lax.broadcasted_iota(jnp.int32, (8, 1), 0)

    def merge(local, win):
        top = jnp.where(sub_row < reach, win[:, :, :, 8:16], local[:, :, :, 0:8])
        bottom = jnp.where(sub_row >= 8 - reach, win[:, :, :, 16:24], local[:, :, :, depth - 8 : depth])
        return jnp.concatenate([top, local[:, :, :, 8 : depth - 8], bottom], axis=3)

    displacement = merge(disp_local, disp_win)
    residual = merge(res_local, res_win)
    return (
        jnp.transpose(displacement, (0, 1, 3, 2, 4)),
        jnp.transpose(residual, (0, 1, 3, 2, 4)),
    )


def col_grp_index():
    return lax.axis_index("col") * GROUP + lax.axis_index("grp")


def solution(mesh):
    devices = mesh.devices.reshape(-1)
    grid = Mesh(devices.reshape(devices.size // GROUP, GROUP), ("col", "grp"))
    slab = ("col", "grp")
    in_specs = (
        P(None, None, slab, None, None),
        P(None, None, slab, None, None),
        P(slab, None, None),
        P(),
        P(),
        P(),
        P(),
        P(),
    )
    out_specs = (P(None, None, slab, None, None), P(None, None, slab, None, None))
    return jax.shard_map(
        on_device, mesh=grid, in_specs=in_specs, out_specs=out_specs, check_vma=False
    )
```

```python
import jax
import jax.numpy as jnp
from jax import lax
from jax.experimental import pallas as pl
from jax.experimental.pallas import tpu as pltpu
from jax.sharding import Mesh, PartitionSpec as P

MATERIALS = 8
GROUP = 8

GAMMA = 0.2
BETA = 0.5
EDGE_WEIGHTS = (0.0, 1.0, 0.5, 0.25)
OFFSETS = [
    (a, b, c) for a in (-1, 0, 1) for b in (-1, 0, 1) for c in (-1, 0, 1) if (a, b, c) != (0, 0, 0)
]


def shift_cells(array, axis, step):
    if step == 0:
        return array
    length = array.shape[axis]
    zero = jnp.zeros_like(lax.slice_in_dim(array, 0, 1, axis=axis))
    if step > 0:
        return jnp.concatenate([lax.slice_in_dim(array, 1, length, axis=axis), zero], axis=axis)
    return jnp.concatenate([zero, lax.slice_in_dim(array, 0, length - 1, axis=axis)], axis=axis)


def mod_neighbour(mod_ext, off_x, off_y, off_z, depth):
    rows = lax.slice_in_dim(mod_ext, 1 + off_x, 1 + off_x + depth, axis=1)
    return shift_cells(shift_cells(rows, 0, off_y), 2, off_z)


def edges_of(mod_ext, depth):
    centre = mod_neighbour(mod_ext, 0, 0, 0, depth)
    edges = []
    for offset in OFFSETS:
        norm_sq = offset[0] * offset[0] + offset[1] * offset[1] + offset[2] * offset[2]
        edges.append(
            EDGE_WEIGHTS[norm_sq]
            * 0.5
            * (centre + mod_neighbour(mod_ext, offset[0], offset[1], offset[2], depth))
        )
    return centre, edges


def diagonal_of(centre, edges):
    comps = [GAMMA * centre, GAMMA * centre, GAMMA * centre]
    for offset, edge in zip(OFFSETS, edges):
        norm_sq = offset[0] * offset[0] + offset[1] * offset[1] + offset[2] * offset[2]
        for comp in range(3):
            comps[comp] = comps[comp] + edge * (1.0 + BETA * offset[comp] * offset[comp] / norm_sq)
    return jnp.stack(comps, axis=0)


def edges_body(mod_ref, edge_ref, centre_ref, diag_ref):
    rows_y, depth, width = mod_ref.shape
    chunks = depth // 8
    sub = lax.broadcasted_iota(jnp.int32, (8, width), 0)
    lane = lax.broadcasted_iota(jnp.int32, (8, width), 1)
    zero = jnp.zeros((8, width), jnp.float32)

    def body(it, carry):
        r = pl.multiple_of(it * 8, 8)
        centre = [mod_ref[y, pl.ds(r, 8), :] for y in range(rows_y)]
        prev = [
            jnp.where(it == 0, zero, mod_ref[y, pl.ds(jnp.maximum(r - 8, 0), 8), :])
            for y in range(rows_y)
        ]
        nxt = [
            jnp.where(it == chunks - 1, zero, mod_ref[y, pl.ds(jnp.minimum(r + 8, depth - 8), 8), :])
            for y in range(rows_y)
        ]
        comps = [[GAMMA * centre[y] for y in range(rows_y)] for c in range(3)]
        index = 0
        for off_x in (-1, 0, 1):
            if off_x == 0:
                shifted_x = centre
            elif off_x < 0:
                shifted_x = [
                    jnp.where(sub == 0, pltpu.roll(prev[y], 1, 0), pltpu.roll(centre[y], 1, 0))
                    for y in range(rows_y)
                ]
            else:
                shifted_x = [
                    jnp.where(sub == 7, pltpu.roll(nxt[y], 7, 0), pltpu.roll(centre[y], 7, 0))
                    for y in range(rows_y)
                ]
            shifted = {0: shifted_x}
            shifted[-1] = [jnp.where(lane == 0, jnp.float32(0.0), pltpu.roll(v, 1, 1)) for v in shifted_x]
            shifted[1] = [
                jnp.where(lane == width - 1, jnp.float32(0.0), pltpu.roll(v, width - 1, 1))
                for v in shifted_x
            ]
            for off_y in (-1, 0, 1):
                for off_z in (-1, 0, 1):
                    if (off_x, off_y, off_z) == (0, 0, 0):
                        continue
                    offset = (off_x, off_y, off_z)
                    norm_sq = off_x * off_x + off_y * off_y + off_z * off_z
                    for y in range(rows_y):
                        source = y + off_y
                        if 0 <= source < rows_y:
                            other = shifted[off_z][source]
                        else:
                            other = zero
                        edge = EDGE_WEIGHTS[norm_sq] * 0.5 * (centre[y] + other)
                        edge_ref[index, y, pl.ds(r, 8), :] = edge
                        for c in range(3):
                            comps[c][y] = comps[c][y] + edge * (
                                1.0 + BETA * offset[c] * offset[c] / norm_sq
                            )
                    index += 1
        for y in range(rows_y):
            centre_ref[y, pl.ds(r, 8), :] = centre[y]
            for c in range(3):
                diag_ref[c, y, pl.ds(r, 8), :] = comps[c][y]
        return carry

    lax.fori_loop(0, chunks, body, 0)


def stencil_body(field_ref, edge_ref, cm_ref, out_ref):
    samples, _, rows_y, depth, width = field_ref.shape
    chunks = depth // 8
    sub = lax.broadcasted_iota(jnp.int32, (8, width), 0)
    lane = lax.broadcasted_iota(jnp.int32, (8, width), 1)
    zero = jnp.zeros((8, width), jnp.float32)

    def body(it, carry):
        s = it // chunks
        part = it % chunks
        r = pl.multiple_of(part * 8, 8)

        def rows(c, y, off):
            if off == 0:
                return field_ref[s, c, y, pl.ds(r, 8), :]
            if off < 0:
                return jnp.where(
                    part == 0, zero, field_ref[s, c, y, pl.ds(jnp.maximum(r - 8, 0), 8), :]
                )
            return jnp.where(
                part == chunks - 1,
                zero,
                field_ref[s, c, y, pl.ds(jnp.minimum(r + 8, depth - 8), 8), :],
            )

        centre = [[rows(c, y, 0) for y in range(rows_y)] for c in range(3)]
        acc = [
            [GAMMA * cm_ref[y, pl.ds(r, 8), :] * centre[c][y] for y in range(rows_y)]
            for c in range(3)
        ]
        index = 0
        for off_x in (-1, 0, 1):
            if off_x == 0:
                shifted_x = centre
            elif off_x < 0:
                shifted_x = [
                    [
                        jnp.where(
                            sub == 0,
                            pltpu.roll(rows(c, y, -1), 1, 0),
                            pltpu.roll(centre[c][y], 1, 0),
                        )
                        for y in range(rows_y)
                    ]
                    for c in range(3)
                ]
            else:
                shifted_x = [
                    [
                        jnp.where(
                            sub == 7,
                            pltpu.roll(rows(c, y, 1), 7, 0),
                            pltpu.roll(centre[c][y], 7, 0),
                        )
                        for y in range(rows_y)
                    ]
                    for c in range(3)
                ]
            shifted = {0: shifted_x}
            shifted[-1] = [
                [jnp.where(lane == 0, jnp.float32(0.0), pltpu.roll(v, 1, 1)) for v in per_c]
                for per_c in shifted_x
            ]
            shifted[1] = [
                [
                    jnp.where(lane == width - 1, jnp.float32(0.0), pltpu.roll(v, width - 1, 1))
                    for v in per_c
                ]
                for per_c in shifted_x
            ]
            for off_y in (-1, 0, 1):
                for off_z in (-1, 0, 1):
                    if (off_x, off_y, off_z) == (0, 0, 0):
                        continue
                    offset = (off_x, off_y, off_z)
                    norm_sq = off_x * off_x + off_y * off_y + off_z * off_z
                    for y in range(rows_y):
                        edge = edge_ref[index, y, pl.ds(r, 8), :]
                        source = y + off_y
                        if 0 <= source < rows_y:
                            delta = [centre[c][y] - shifted[off_z][c][source] for c in range(3)]
                        else:
                            delta = [centre[c][y] for c in range(3)]
                        project = None
                        for c in range(3):
                            if offset[c] > 0:
                                project = delta[c] if project is None else project + delta[c]
                            elif offset[c] < 0:
                                project = -delta[c] if project is None else project - delta[c]
                        if norm_sq == 2:
                            project = project * 0.5
                        elif norm_sq == 3:
                            project = project * (1.0 / 3.0)
                        for c in range(3):
                            if offset[c] != 0:
                                acc[c][y] = acc[c][y] + edge * (delta[c] + BETA * offset[c] * project)
                            else:
                                acc[c][y] = acc[c][y] + edge * delta[c]
                    index += 1
        for c in range(3):
            for y in range(rows_y):
                out_ref[s, c, y, pl.ds(r, 8), :] = acc[c][y]
        return carry

    lax.fori_loop(0, samples * chunks, body, 0)


def chain_kernel(
    scal_ref, mask_ref, md_ref, ld_ref, mod_ref, disp_ref, res_ref,
    edge_s, cm_s, jac_s, k_s, a_s, step0_s, step1_s,
):
    samples, _, rows_y, depth, width = md_ref.shape
    theta = scal_ref[0]
    c1 = scal_ref[1]
    c2 = scal_ref[2]
    edges_body(mod_ref, edge_s, cm_s, jac_s)
    stencil_body(md_ref, edge_s, cm_s, k_s)
    keep0 = mask_ref[0] > 0.0
    keep1 = mask_ref[1] > 0.0

    def first(it, carry):
        s = it // 3
        c = it % 3
        for y in range(rows_y):
            start = ld_ref[s, c, y] - k_s[s, c, y]
            a_s[s, c, y] = start
            step0_s[s, c, y] = jnp.where(keep0, start / (theta * jac_s[c, y]), jnp.float32(0.0))
        return carry

    lax.fori_loop(0, samples * 3, first, 0)
    stencil_body(step0_s, edge_s, cm_s, k_s)

    def second(it, carry):
        s = it // 3
        c = it % 3
        for y in range(rows_y):
            residual1 = a_s[s, c, y] - k_s[s, c, y]
            a_s[s, c, y] = residual1
            step0 = step0_s[s, c, y]
            step1 = jnp.where(
                keep1, c1 * step0 + c2 * residual1 / jac_s[c, y], jnp.float32(0.0)
            )
            step1_s[s, c, y] = step1
            disp_ref[s, c, y] = md_ref[s, c, y] + step0 + step1
        return carry

    lax.fori_loop(0, samples * 3, second, 0)
    stencil_body(step1_s, edge_s, cm_s, k_s)

    def third(it, carry):
        s = it // 3
        c = it % 3
        for y in range(rows_y):
            res_ref[s, c, y] = a_s[s, c, y] - k_s[s, c, y]
        return carry

    lax.fori_loop(0, samples * 3, third, 0)


def run_chain(scalars, masks, md, ld, mod):
    samples, _, rows_y, depth, width = md.shape
    vmem = pl.BlockSpec(memory_space=pltpu.VMEM)
    smem = pl.BlockSpec(memory_space=pltpu.SMEM)
    field = jax.ShapeDtypeStruct(md.shape, jnp.float32)
    size = md.size
    return pl.pallas_call(
        chain_kernel,
        out_shape=(field, field),
        in_specs=[smem, vmem, vmem, vmem, vmem],
        out_specs=(vmem, vmem),
        scratch_shapes=[
            pltpu.VMEM((len(OFFSETS), rows_y, depth, width), jnp.float32),
            pltpu.VMEM((rows_y, depth, width), jnp.float32),
            pltpu.VMEM((3, rows_y, depth, width), jnp.float32),
        ]
        + [pltpu.VMEM(md.shape, jnp.float32)] * 4,
        compiler_params=pltpu.CompilerParams(vmem_limit_bytes=48 * 1024 * 1024),
        cost_estimate=pl.CostEstimate(
            flops=3 * 26 * 20 * size, bytes_accessed=4 * 5 * size, transcendentals=0
        ),
    )(scalars, masks, md, ld, mod)


def lookup_modulus(material, moduli):
    modulus = jnp.zeros(material.shape, jnp.float32)
    for index in range(MATERIALS):
        modulus = modulus + jnp.where(material == index, moduli[index], jnp.float32(0.0))
    return modulus


def neighbour_devices(part_device, partners):
    count = part_device.shape[0]
    ids = jnp.arange(count, dtype=jnp.int32)
    hit = part_device[None, :] == ids[:, None]
    place = jnp.sum(jnp.where(hit, ids[None, :], 0), axis=1)
    upper = place % 2 == 0
    up_dev = jnp.where(upper, partners[0], partners[1])
    low_dev = jnp.where(upper, partners[1], partners[0])
    return up_dev, low_dev


def exchange(first, last, up_dev, low_dev):
    col = lax.axis_index("col")
    grp = lax.axis_index("grp")
    me = col * GROUP + grp
    cols = up_dev.shape[0] // GROUP
    pack = jnp.stack([first, last], axis=0)[None]
    held = lax.all_gather(pack, "grp", axis=0, tiled=True)
    pick = (jnp.arange(GROUP, dtype=jnp.int32) == grp)[None, :]
    t_up = jnp.sum(jnp.where(pick, up_dev.reshape(cols, GROUP), 0), axis=1)
    t_low = jnp.sum(jnp.where(pick, low_dev.reshape(cols, GROUP), 0), axis=1)
    up_at = jnp.where(t_up // GROUP == col, t_up % GROUP, -1)[:, None]
    low_at = jnp.where(t_low // GROUP == col, t_low % GROUP, -1)[:, None]
    from_up = jnp.zeros((cols, first.shape[0]), jnp.float32)
    from_low = jnp.zeros((cols, first.shape[0]), jnp.float32)
    for k in range(GROUP):
        from_up = jnp.where(up_at == k, held[k, 0][None, :], from_up)
        from_low = jnp.where(low_at == k, held[k, 1][None, :], from_low)
    slots = jnp.stack([from_up, from_low], axis=1)
    got = lax.all_to_all(slots, "col", 0, 0, tiled=True)
    my_up = up_dev[me]
    my_low = low_dev[me]
    above = lax.dynamic_index_in_dim(got, my_up // GROUP, axis=0, keepdims=False)[0]
    below = lax.dynamic_index_in_dim(got, my_low // GROUP, axis=0, keepdims=False)[1]
    above = jnp.where(my_up != me, above, jnp.float32(0.0))
    below = jnp.where(my_low != me, below, jnp.float32(0.0))
    return below, above


def on_device(loads, modal_disp, material, moduli, part_device, partners, low_bound, high_bound):
    up_dev, low_dev = neighbour_devices(part_device, partners)
    samples, _, depth, rows_y, width = loads.shape
    loads = jnp.transpose(loads, (0, 1, 3, 2, 4))
    modal_disp = jnp.transpose(modal_disp, (0, 1, 3, 2, 4))
    modulus = lookup_modulus(jnp.transpose(material, (1, 0, 2)), moduli)
    plane = (samples, 3, rows_y, width)
    plane_size = samples * 3 * rows_y * width
    mod_size = rows_y * width

    def pack(md_rows, load_rows):
        parts = [modal_disp[:, :, :, r].reshape(-1) for r in md_rows]
        parts += [loads[:, :, :, r].reshape(-1) for r in load_rows]
        parts += [modulus[:, r].reshape(-1) for r in md_rows]
        return jnp.concatenate(parts)

    first = pack((0, 1, 2), (0, 1))
    last = pack((depth - 3, depth - 2, depth - 1), (depth - 2, depth - 1))
    below, above = exchange(first, last, up_dev, low_dev)

    def planes_of(got, count, start, size, shape):
        return [got[start + i * size : start + (i + 1) * size].reshape(shape) for i in range(count)]

    md_below = planes_of(below, 3, 0, plane_size, plane)
    md_above = planes_of(above, 3, 0, plane_size, plane)
    ld_below = planes_of(below, 2, 3 * plane_size, plane_size, plane)
    ld_above = planes_of(above, 2, 3 * plane_size, plane_size, plane)
    mod_below = planes_of(below, 3, 5 * plane_size, mod_size, (rows_y, width))
    mod_above = planes_of(above, 3, 5 * plane_size, mod_size, (rows_y, width))

    def extend(own, lower, upper, axis):
        zero = jnp.zeros_like(lower[0])
        rows = [zero] * (8 - len(lower)) + list(lower)
        tail = list(upper) + [zero] * (8 - len(upper))
        return jnp.concatenate(
            [jnp.stack(rows, axis=axis), own, jnp.stack(tail, axis=axis)], axis=axis
        )

    low_on = low_dev[col_grp_index()] != col_grp_index()
    up_on = up_dev[col_grp_index()] != col_grp_index()
    zero_mod = jnp.zeros((rows_y, width), jnp.float32)
    zero_plane = jnp.zeros(plane, jnp.float32)

    theta = (high_bound[0] + low_bound[0]) / 2.0
    half = (high_bound[0] - low_bound[0]) / 2.0
    sigma = theta / half
    rho0 = 1.0 / sigma
    rho1 = 1.0 / (2.0 * sigma - rho0)

    scalars = jnp.stack([theta, rho1 * rho0, 2.0 * rho1 / half]).astype(jnp.float32)

    def chain(md, ld, mod, masks):
        return run_chain(scalars, masks, md, ld, mod)

    disp_local, res_local = chain(modal_disp, loads, modulus, jnp.ones((2, depth, width), jnp.float32))

    edge_rows = 8
    head = slice(0, edge_rows)
    tail = slice(depth - edge_rows, depth)

    def window(own, lower, upper, axis):
        zero = jnp.zeros_like(lower[0])
        rows = [zero] * (8 - len(lower)) + list(lower)
        after = list(upper) + [zero] * (8 - len(upper))
        index = [slice(None)] * own.ndim
        index[axis] = head
        own_head = own[tuple(index)]
        index[axis] = tail
        own_tail = own[tuple(index)]
        return jnp.concatenate(
            [jnp.stack(rows, axis=axis), own_head, own_tail, jnp.stack(after, axis=axis)], axis=axis
        )

    md_win = window(modal_disp, md_below, md_above, 3)
    ld_win = window(loads, ld_below, ld_above, 3)
    mod_win = window(modulus, mod_below, mod_above, 1)
    logical = jnp.concatenate(
        [
            jnp.arange(-8, edge_rows, dtype=jnp.int32),
            jnp.arange(depth - edge_rows, depth + 8, dtype=jnp.int32),
        ]
    )

    def valid(reach):
        keep = (logical >= 0) & (logical < depth)
        keep = keep | (low_on & (logical >= -reach) & (logical < 0))
        keep = keep | (up_on & (logical >= depth) & (logical < depth + reach))
        return jnp.broadcast_to(keep.astype(jnp.float32)[:, None], (logical.shape[0], width))

    masks = jnp.stack([valid(2), valid(1)], axis=0)
    disp_win, res_win = chain(md_win, ld_win, mod_win, masks)

    reach = 3
    sub_row = lax.broadcasted_iota(jnp.int32, (8, 1), 0)

    def merge(local, win):
        top = jnp.where(sub_row < reach, win[:, :, :, 8:16], local[:, :, :, 0:8])
        bottom = jnp.where(sub_row >= 8 - reach, win[:, :, :, 16:24], local[:, :, :, depth - 8 : depth])
        return jnp.concatenate([top, local[:, :, :, 8 : depth - 8], bottom], axis=3)

    displacement = merge(disp_local, disp_win)
    residual = merge(res_local, res_win)
    return (
        jnp.transpose(displacement, (0, 1, 3, 2, 4)),
        jnp.transpose(residual, (0, 1, 3, 2, 4)),
    )


def col_grp_index():
    return lax.axis_index("col") * GROUP + lax.axis_index("grp")


def solution(mesh):
    devices = mesh.devices.reshape(-1)
    grid = Mesh(devices.reshape(devices.size // GROUP, GROUP), ("col", "grp"))
    slab = ("col", "grp")
    in_specs = (
        P(None, None, slab, None, None),
        P(None, None, slab, None, None),
        P(slab, None, None),
        P(),
        P(),
        P(),
        P(),
        P(),
    )
    out_specs = (P(None, None, slab, None, None), P(None, None, slab, None, None))
    return jax.shard_map(
        on_device, mesh=grid, in_specs=in_specs, out_specs=out_specs, check_vma=False
    )
```

```python
import jax
import jax.numpy as jnp
from jax import lax
from jax.experimental import pallas as pl
from jax.experimental.pallas import tpu as pltpu
from jax.sharding import Mesh, PartitionSpec as P

MATERIALS = 8
GROUP = 8

GAMMA = 0.2
BETA = 0.5
EDGE_WEIGHTS = (0.0, 1.0, 0.5, 0.25)
OFFSETS = [
    (a, b, c) for a in (-1, 0, 1) for b in (-1, 0, 1) for c in (-1, 0, 1) if (a, b, c) != (0, 0, 0)
]


def shift_cells(array, axis, step):
    if step == 0:
        return array
    length = array.shape[axis]
    zero = jnp.zeros_like(lax.slice_in_dim(array, 0, 1, axis=axis))
    if step > 0:
        return jnp.concatenate([lax.slice_in_dim(array, 1, length, axis=axis), zero], axis=axis)
    return jnp.concatenate([zero, lax.slice_in_dim(array, 0, length - 1, axis=axis)], axis=axis)


def mod_neighbour(mod_ext, off_x, off_y, off_z, depth):
    rows = lax.slice_in_dim(mod_ext, 1 + off_x, 1 + off_x + depth, axis=1)
    return shift_cells(shift_cells(rows, 0, off_y), 2, off_z)


def edges_of(mod_ext, depth):
    centre = mod_neighbour(mod_ext, 0, 0, 0, depth)
    edges = []
    for offset in OFFSETS:
        norm_sq = offset[0] * offset[0] + offset[1] * offset[1] + offset[2] * offset[2]
        edges.append(
            EDGE_WEIGHTS[norm_sq]
            * 0.5
            * (centre + mod_neighbour(mod_ext, offset[0], offset[1], offset[2], depth))
        )
    return centre, edges


def diagonal_of(centre, edges):
    comps = [GAMMA * centre, GAMMA * centre, GAMMA * centre]
    for offset, edge in zip(OFFSETS, edges):
        norm_sq = offset[0] * offset[0] + offset[1] * offset[1] + offset[2] * offset[2]
        for comp in range(3):
            comps[comp] = comps[comp] + edge * (1.0 + BETA * offset[comp] * offset[comp] / norm_sq)
    return jnp.stack(comps, axis=0)


def edges_body(mod_ref, edge_ref, centre_ref, diag_ref):
    rows_y, depth, width = mod_ref.shape
    chunks = depth // 8
    sub = lax.broadcasted_iota(jnp.int32, (8, width), 0)
    lane = lax.broadcasted_iota(jnp.int32, (8, width), 1)
    zero = jnp.zeros((8, width), jnp.float32)

    def body(it, carry):
        r = pl.multiple_of(it * 8, 8)
        centre = [mod_ref[y, pl.ds(r, 8), :] for y in range(rows_y)]
        prev = [
            jnp.where(it == 0, zero, mod_ref[y, pl.ds(jnp.maximum(r - 8, 0), 8), :])
            for y in range(rows_y)
        ]
        nxt = [
            jnp.where(it == chunks - 1, zero, mod_ref[y, pl.ds(jnp.minimum(r + 8, depth - 8), 8), :])
            for y in range(rows_y)
        ]
        comps = [[GAMMA * centre[y] for y in range(rows_y)] for c in range(3)]
        index = 0
        for off_x in (-1, 0, 1):
            if off_x == 0:
                shifted_x = centre
            elif off_x < 0:
                shifted_x = [
                    jnp.where(sub == 0, pltpu.roll(prev[y], 1, 0), pltpu.roll(centre[y], 1, 0))
                    for y in range(rows_y)
                ]
            else:
                shifted_x = [
                    jnp.where(sub == 7, pltpu.roll(nxt[y], 7, 0), pltpu.roll(centre[y], 7, 0))
                    for y in range(rows_y)
                ]
            shifted = {0: shifted_x}
            shifted[-1] = [jnp.where(lane == 0, jnp.float32(0.0), pltpu.roll(v, 1, 1)) for v in shifted_x]
            shifted[1] = [
                jnp.where(lane == width - 1, jnp.float32(0.0), pltpu.roll(v, width - 1, 1))
                for v in shifted_x
            ]
            for off_y in (-1, 0, 1):
                for off_z in (-1, 0, 1):
                    if (off_x, off_y, off_z) == (0, 0, 0):
                        continue
                    offset = (off_x, off_y, off_z)
                    norm_sq = off_x * off_x + off_y * off_y + off_z * off_z
                    for y in range(rows_y):
                        source = y + off_y
                        if 0 <= source < rows_y:
                            other = shifted[off_z][source]
                        else:
                            other = zero
                        edge = EDGE_WEIGHTS[norm_sq] * 0.5 * (centre[y] + other)
                        edge_ref[index, y, pl.ds(r, 8), :] = edge
                        for c in range(3):
                            comps[c][y] = comps[c][y] + edge * (
                                1.0 + BETA * offset[c] * offset[c] / norm_sq
                            )
                    index += 1
        for y in range(rows_y):
            centre_ref[y, pl.ds(r, 8), :] = centre[y]
            for c in range(3):
                diag_ref[c, y, pl.ds(r, 8), :] = comps[c][y]
        return carry

    lax.fori_loop(0, chunks, body, 0)


def stencil_body(field_ref, edge_ref, cm_ref, out_ref):
    samples, _, rows_y, depth, width = field_ref.shape
    chunks = depth // 8
    sub = lax.broadcasted_iota(jnp.int32, (8, width), 0)
    lane = lax.broadcasted_iota(jnp.int32, (8, width), 1)
    zero = jnp.zeros((8, width), jnp.float32)

    def body(it, carry):
        s = it // chunks
        part = it % chunks
        r = pl.multiple_of(part * 8, 8)

        def rows(c, y, off):
            if off == 0:
                return field_ref[s, c, y, pl.ds(r, 8), :]
            if off < 0:
                return jnp.where(
                    part == 0, zero, field_ref[s, c, y, pl.ds(jnp.maximum(r - 8, 0), 8), :]
                )
            return jnp.where(
                part == chunks - 1,
                zero,
                field_ref[s, c, y, pl.ds(jnp.minimum(r + 8, depth - 8), 8), :],
            )

        centre = [[rows(c, y, 0) for y in range(rows_y)] for c in range(3)]
        acc = [
            [GAMMA * cm_ref[y, pl.ds(r, 8), :] * centre[c][y] for y in range(rows_y)]
            for c in range(3)
        ]
        index = 0
        for off_x in (-1, 0, 1):
            if off_x == 0:
                shifted_x = centre
            elif off_x < 0:
                shifted_x = [
                    [
                        jnp.where(
                            sub == 0,
                            pltpu.roll(rows(c, y, -1), 1, 0),
                            pltpu.roll(centre[c][y], 1, 0),
                        )
                        for y in range(rows_y)
                    ]
                    for c in range(3)
                ]
            else:
                shifted_x = [
                    [
                        jnp.where(
                            sub == 7,
                            pltpu.roll(rows(c, y, 1), 7, 0),
                            pltpu.roll(centre[c][y], 7, 0),
                        )
                        for y in range(rows_y)
                    ]
                    for c in range(3)
                ]
            shifted = {0: shifted_x}
            shifted[-1] = [
                [jnp.where(lane == 0, jnp.float32(0.0), pltpu.roll(v, 1, 1)) for v in per_c]
                for per_c in shifted_x
            ]
            shifted[1] = [
                [
                    jnp.where(lane == width - 1, jnp.float32(0.0), pltpu.roll(v, width - 1, 1))
                    for v in per_c
                ]
                for per_c in shifted_x
            ]
            for off_y in (-1, 0, 1):
                for off_z in (-1, 0, 1):
                    if (off_x, off_y, off_z) == (0, 0, 0):
                        continue
                    offset = (off_x, off_y, off_z)
                    norm_sq = off_x * off_x + off_y * off_y + off_z * off_z
                    for y in range(rows_y):
                        edge = edge_ref[index, y, pl.ds(r, 8), :]
                        source = y + off_y
                        if 0 <= source < rows_y:
                            delta = [centre[c][y] - shifted[off_z][c][source] for c in range(3)]
                        else:
                            delta = [centre[c][y] for c in range(3)]
                        project = None
                        for c in range(3):
                            if offset[c] > 0:
                                project = delta[c] if project is None else project + delta[c]
                            elif offset[c] < 0:
                                project = -delta[c] if project is None else project - delta[c]
                        if norm_sq == 2:
                            project = project * 0.5
                        elif norm_sq == 3:
                            project = project * (1.0 / 3.0)
                        for c in range(3):
                            if offset[c] != 0:
                                acc[c][y] = acc[c][y] + edge * (delta[c] + BETA * offset[c] * project)
                            else:
                                acc[c][y] = acc[c][y] + edge * delta[c]
                    index += 1
        for c in range(3):
            for y in range(rows_y):
                out_ref[s, c, y, pl.ds(r, 8), :] = acc[c][y]
        return carry

    lax.fori_loop(0, samples * chunks, body, 0)


def chain_kernel(
    scal_ref, mask_ref, md_ref, ld_ref, mod_ref, disp_ref, res_ref,
    edge_s, cm_s, jac_s, k_s, a_s, step0_s, step1_s,
):
    samples, _, rows_y, depth, width = md_ref.shape
    theta = scal_ref[0]
    c1 = scal_ref[1]
    c2 = scal_ref[2]
    edges_body(mod_ref, edge_s, cm_s, jac_s)
    stencil_body(md_ref, edge_s, cm_s, k_s)
    keep0 = mask_ref[0] > 0.0
    keep1 = mask_ref[1] > 0.0

    def first(it, carry):
        s = it // 3
        c = it % 3
        for y in range(rows_y):
            start = ld_ref[s, c, y] - k_s[s, c, y]
            a_s[s, c, y] = start
            step0_s[s, c, y] = jnp.where(keep0, start / (theta * jac_s[c, y]), jnp.float32(0.0))
        return carry

    lax.fori_loop(0, samples * 3, first, 0)
    stencil_body(step0_s, edge_s, cm_s, k_s)

    def second(it, carry):
        s = it // 3
        c = it % 3
        for y in range(rows_y):
            residual1 = a_s[s, c, y] - k_s[s, c, y]
            a_s[s, c, y] = residual1
            step0 = step0_s[s, c, y]
            step1 = jnp.where(
                keep1, c1 * step0 + c2 * residual1 / jac_s[c, y], jnp.float32(0.0)
            )
            step1_s[s, c, y] = step1
            disp_ref[s, c, y] = md_ref[s, c, y] + step0 + step1
        return carry

    lax.fori_loop(0, samples * 3, second, 0)
    stencil_body(step1_s, edge_s, cm_s, k_s)

    def third(it, carry):
        s = it // 3
        c = it % 3
        for y in range(rows_y):
            res_ref[s, c, y] = a_s[s, c, y] - k_s[s, c, y]
        return carry

    lax.fori_loop(0, samples * 3, third, 0)


def run_chain(scalars, masks, md, ld, mod):
    samples, _, rows_y, depth, width = md.shape
    vmem = pl.BlockSpec(memory_space=pltpu.VMEM)
    smem = pl.BlockSpec(memory_space=pltpu.SMEM)
    field = jax.ShapeDtypeStruct(md.shape, jnp.float32)
    size = md.size
    return pl.pallas_call(
        chain_kernel,
        out_shape=(field, field),
        in_specs=[smem, vmem, vmem, vmem, vmem],
        out_specs=(vmem, vmem),
        scratch_shapes=[
            pltpu.VMEM((len(OFFSETS), rows_y, depth, width), jnp.float32),
            pltpu.VMEM((rows_y, depth, width), jnp.float32),
            pltpu.VMEM((3, rows_y, depth, width), jnp.float32),
        ]
        + [pltpu.VMEM(md.shape, jnp.float32)] * 4,
        compiler_params=pltpu.CompilerParams(vmem_limit_bytes=48 * 1024 * 1024),
        cost_estimate=pl.CostEstimate(
            flops=3 * 26 * 20 * size, bytes_accessed=4 * 5 * size, transcendentals=0
        ),
    )(scalars, masks, md, ld, mod)


def lookup_modulus(material, moduli):
    modulus = jnp.zeros(material.shape, jnp.float32)
    for index in range(MATERIALS):
        modulus = modulus + jnp.where(material == index, moduli[index], jnp.float32(0.0))
    return modulus


def neighbour_devices(part_device, partners):
    count = part_device.shape[0]
    ids = jnp.arange(count, dtype=jnp.int32)
    hit = part_device[None, :] == ids[:, None]
    place = jnp.sum(jnp.where(hit, ids[None, :], 0), axis=1)
    upper = place % 2 == 0
    up_dev = jnp.where(upper, partners[0], partners[1])
    low_dev = jnp.where(upper, partners[1], partners[0])
    return up_dev, low_dev


def exchange(first, last, up_dev, low_dev):
    col = lax.axis_index("col")
    grp = lax.axis_index("grp")
    me = col * GROUP + grp
    cols = up_dev.shape[0] // GROUP
    pack = jnp.stack([first, last], axis=0)[None]
    held = lax.all_gather(pack, "grp", axis=0, tiled=True)
    pick = (jnp.arange(GROUP, dtype=jnp.int32) == grp)[None, :]
    t_up = jnp.sum(jnp.where(pick, up_dev.reshape(cols, GROUP), 0), axis=1)
    t_low = jnp.sum(jnp.where(pick, low_dev.reshape(cols, GROUP), 0), axis=1)
    up_at = jnp.where(t_up // GROUP == col, t_up % GROUP, -1)[:, None]
    low_at = jnp.where(t_low // GROUP == col, t_low % GROUP, -1)[:, None]
    up_at = up_at[:, :, None]
    low_at = low_at[:, :, None]
    from_up = jnp.zeros((cols,) + first.shape, jnp.float32)
    from_low = jnp.zeros((cols,) + first.shape, jnp.float32)
    for k in range(GROUP):
        from_up = jnp.where(up_at == k, held[k, 0][None], from_up)
        from_low = jnp.where(low_at == k, held[k, 1][None], from_low)
    slots = jnp.stack([from_up, from_low], axis=1)
    got = lax.all_to_all(slots, "col", 0, 0, tiled=True)
    my_up = up_dev[me]
    my_low = low_dev[me]
    above = lax.dynamic_index_in_dim(got, my_up // GROUP, axis=0, keepdims=False)[0]
    below = lax.dynamic_index_in_dim(got, my_low // GROUP, axis=0, keepdims=False)[1]
    above = jnp.where(my_up != me, above, jnp.float32(0.0))
    below = jnp.where(my_low != me, below, jnp.float32(0.0))
    return below, above


def on_device(loads, modal_disp, material, moduli, part_device, partners, low_bound, high_bound):
    up_dev, low_dev = neighbour_devices(part_device, partners)
    samples, _, depth, rows_y, width = loads.shape
    loads = jnp.transpose(loads, (0, 1, 3, 2, 4))
    modal_disp = jnp.transpose(modal_disp, (0, 1, 3, 2, 4))
    flat_mod = lookup_modulus(material.reshape(depth, rows_y * width), moduli)
    modulus = jnp.stack([flat_mod[:, y * width : (y + 1) * width] for y in range(rows_y)], axis=0)
    plane = (samples, 3, rows_y, width)
    plane_size = samples * 3 * rows_y * width
    mod_size = rows_y * width

    def pack(md_rows, load_rows):
        parts = [modal_disp[:, :, :, r].reshape(-1) for r in md_rows]
        parts += [loads[:, :, :, r].reshape(-1) for r in load_rows]
        parts += [modulus[:, r].reshape(-1) for r in md_rows]
        flat = jnp.concatenate(parts)
        return flat.reshape(flat.shape[0] // width, width)

    first = pack((0, 1, 2), (0, 1))
    last = pack((depth - 3, depth - 2, depth - 1), (depth - 2, depth - 1))
    below, above = exchange(first, last, up_dev, low_dev)
    below = below.reshape(-1)
    above = above.reshape(-1)

    def planes_of(got, count, start, size, shape):
        return [got[start + i * size : start + (i + 1) * size].reshape(shape) for i in range(count)]

    md_below = planes_of(below, 3, 0, plane_size, plane)
    md_above = planes_of(above, 3, 0, plane_size, plane)
    ld_below = planes_of(below, 2, 3 * plane_size, plane_size, plane)
    ld_above = planes_of(above, 2, 3 * plane_size, plane_size, plane)
    mod_below = planes_of(below, 3, 5 * plane_size, mod_size, (rows_y, width))
    mod_above = planes_of(above, 3, 5 * plane_size, mod_size, (rows_y, width))

    def extend(own, lower, upper, axis):
        zero = jnp.zeros_like(lower[0])
        rows = [zero] * (8 - len(lower)) + list(lower)
        tail = list(upper) + [zero] * (8 - len(upper))
        return jnp.concatenate(
            [jnp.stack(rows, axis=axis), own, jnp.stack(tail, axis=axis)], axis=axis
        )

    low_on = low_dev[col_grp_index()] != col_grp_index()
    up_on = up_dev[col_grp_index()] != col_grp_index()
    zero_mod = jnp.zeros((rows_y, width), jnp.float32)
    zero_plane = jnp.zeros(plane, jnp.float32)

    theta = (high_bound[0] + low_bound[0]) / 2.0
    half = (high_bound[0] - low_bound[0]) / 2.0
    sigma = theta / half
    rho0 = 1.0 / sigma
    rho1 = 1.0 / (2.0 * sigma - rho0)

    scalars = jnp.stack([theta, rho1 * rho0, 2.0 * rho1 / half]).astype(jnp.float32)

    def chain(md, ld, mod, masks):
        return run_chain(scalars, masks, md, ld, mod)

    disp_local, res_local = chain(modal_disp, loads, modulus, jnp.ones((2, depth, width), jnp.float32))

    edge_rows = 8
    head = slice(0, edge_rows)
    tail = slice(depth - edge_rows, depth)

    def window(own, lower, upper, axis):
        zero = jnp.zeros_like(lower[0])
        rows = [zero] * (8 - len(lower)) + list(lower)
        after = list(upper) + [zero] * (8 - len(upper))
        index = [slice(None)] * own.ndim
        index[axis] = head
        own_head = own[tuple(index)]
        index[axis] = tail
        own_tail = own[tuple(index)]
        return jnp.concatenate(
            [jnp.stack(rows, axis=axis), own_head, own_tail, jnp.stack(after, axis=axis)], axis=axis
        )

    md_win = window(modal_disp, md_below, md_above, 3)
    ld_win = window(loads, ld_below, ld_above, 3)
    mod_win = window(modulus, mod_below, mod_above, 1)
    logical = jnp.concatenate(
        [
            jnp.arange(-8, edge_rows, dtype=jnp.int32),
            jnp.arange(depth - edge_rows, depth + 8, dtype=jnp.int32),
        ]
    )

    def valid(reach):
        keep = (logical >= 0) & (logical < depth)
        keep = keep | (low_on & (logical >= -reach) & (logical < 0))
        keep = keep | (up_on & (logical >= depth) & (logical < depth + reach))
        return jnp.broadcast_to(keep.astype(jnp.float32)[:, None], (logical.shape[0], width))

    masks = jnp.stack([valid(2), valid(1)], axis=0)
    disp_win, res_win = chain(md_win, ld_win, mod_win, masks)

    reach = 3
    sub_row = lax.broadcasted_iota(jnp.int32, (8, 1), 0)

    def merge(local, win):
        top = jnp.where(sub_row < reach, win[:, :, :, 8:16], local[:, :, :, 0:8])
        bottom = jnp.where(sub_row >= 8 - reach, win[:, :, :, 16:24], local[:, :, :, depth - 8 : depth])
        return jnp.concatenate([top, local[:, :, :, 8 : depth - 8], bottom], axis=3)

    displacement = merge(disp_local, disp_win)
    residual = merge(res_local, res_win)
    return (
        jnp.transpose(displacement, (0, 1, 3, 2, 4)),
        jnp.transpose(residual, (0, 1, 3, 2, 4)),
    )


def col_grp_index():
    return lax.axis_index("col") * GROUP + lax.axis_index("grp")


def solution(mesh):
    devices = mesh.devices.reshape(-1)
    grid = Mesh(devices.reshape(devices.size // GROUP, GROUP), ("col", "grp"))
    slab = ("col", "grp")
    in_specs = (
        P(None, None, slab, None, None),
        P(None, None, slab, None, None),
        P(slab, None, None),
        P(),
        P(),
        P(),
        P(),
        P(),
    )
    out_specs = (P(None, None, slab, None, None), P(None, None, slab, None, None))
    return jax.shard_map(
        on_device, mesh=grid, in_specs=in_specs, out_specs=out_specs, check_vma=False
    )
```

```python
import jax
import jax.numpy as jnp
from jax import lax
from jax.experimental import pallas as pl
from jax.experimental.pallas import tpu as pltpu
from jax.sharding import Mesh, PartitionSpec as P

MATERIALS = 8
GROUP = 8

GAMMA = 0.2
BETA = 0.5
EDGE_WEIGHTS = (0.0, 1.0, 0.5, 0.25)
OFFSETS = [
    (a, b, c) for a in (-1, 0, 1) for b in (-1, 0, 1) for c in (-1, 0, 1) if (a, b, c) != (0, 0, 0)
]


def shift_cells(array, axis, step):
    if step == 0:
        return array
    length = array.shape[axis]
    zero = jnp.zeros_like(lax.slice_in_dim(array, 0, 1, axis=axis))
    if step > 0:
        return jnp.concatenate([lax.slice_in_dim(array, 1, length, axis=axis), zero], axis=axis)
    return jnp.concatenate([zero, lax.slice_in_dim(array, 0, length - 1, axis=axis)], axis=axis)


def mod_neighbour(mod_ext, off_x, off_y, off_z, depth):
    rows = lax.slice_in_dim(mod_ext, 1 + off_x, 1 + off_x + depth, axis=1)
    return shift_cells(shift_cells(rows, 0, off_y), 2, off_z)


def edges_of(mod_ext, depth):
    centre = mod_neighbour(mod_ext, 0, 0, 0, depth)
    edges = []
    for offset in OFFSETS:
        norm_sq = offset[0] * offset[0] + offset[1] * offset[1] + offset[2] * offset[2]
        edges.append(
            EDGE_WEIGHTS[norm_sq]
            * 0.5
            * (centre + mod_neighbour(mod_ext, offset[0], offset[1], offset[2], depth))
        )
    return centre, edges


def diagonal_of(centre, edges):
    comps = [GAMMA * centre, GAMMA * centre, GAMMA * centre]
    for offset, edge in zip(OFFSETS, edges):
        norm_sq = offset[0] * offset[0] + offset[1] * offset[1] + offset[2] * offset[2]
        for comp in range(3):
            comps[comp] = comps[comp] + edge * (1.0 + BETA * offset[comp] * offset[comp] / norm_sq)
    return jnp.stack(comps, axis=0)


def edges_body(mod_ref, edge_ref, centre_ref, diag_ref):
    rows_y, depth, width = mod_ref.shape
    chunks = depth // 8
    sub = lax.broadcasted_iota(jnp.int32, (8, width), 0)
    lane = lax.broadcasted_iota(jnp.int32, (8, width), 1)
    zero = jnp.zeros((8, width), jnp.float32)

    def body(it, carry):
        r = pl.multiple_of(it * 8, 8)
        centre = [mod_ref[y, pl.ds(r, 8), :] for y in range(rows_y)]
        prev = [
            jnp.where(it == 0, zero, mod_ref[y, pl.ds(jnp.maximum(r - 8, 0), 8), :])
            for y in range(rows_y)
        ]
        nxt = [
            jnp.where(it == chunks - 1, zero, mod_ref[y, pl.ds(jnp.minimum(r + 8, depth - 8), 8), :])
            for y in range(rows_y)
        ]
        comps = [[GAMMA * centre[y] for y in range(rows_y)] for c in range(3)]
        index = 0
        for off_x in (-1, 0, 1):
            if off_x == 0:
                shifted_x = centre
            elif off_x < 0:
                shifted_x = [
                    jnp.where(sub == 0, pltpu.roll(prev[y], 1, 0), pltpu.roll(centre[y], 1, 0))
                    for y in range(rows_y)
                ]
            else:
                shifted_x = [
                    jnp.where(sub == 7, pltpu.roll(nxt[y], 7, 0), pltpu.roll(centre[y], 7, 0))
                    for y in range(rows_y)
                ]
            shifted = {0: shifted_x}
            shifted[-1] = [jnp.where(lane == 0, jnp.float32(0.0), pltpu.roll(v, 1, 1)) for v in shifted_x]
            shifted[1] = [
                jnp.where(lane == width - 1, jnp.float32(0.0), pltpu.roll(v, width - 1, 1))
                for v in shifted_x
            ]
            for off_y in (-1, 0, 1):
                for off_z in (-1, 0, 1):
                    if (off_x, off_y, off_z) == (0, 0, 0):
                        continue
                    offset = (off_x, off_y, off_z)
                    norm_sq = off_x * off_x + off_y * off_y + off_z * off_z
                    for y in range(rows_y):
                        source = y + off_y
                        if 0 <= source < rows_y:
                            other = shifted[off_z][source]
                        else:
                            other = zero
                        edge = EDGE_WEIGHTS[norm_sq] * 0.5 * (centre[y] + other)
                        edge_ref[index, y, pl.ds(r, 8), :] = edge
                        for c in range(3):
                            comps[c][y] = comps[c][y] + edge * (
                                1.0 + BETA * offset[c] * offset[c] / norm_sq
                            )
                    index += 1
        for y in range(rows_y):
            centre_ref[y, pl.ds(r, 8), :] = centre[y]
            for c in range(3):
                diag_ref[c, y, pl.ds(r, 8), :] = comps[c][y]
        return carry

    lax.fori_loop(0, chunks, body, 0)


def stencil_body(field_ref, edge_ref, cm_ref, out_ref):
    samples, _, rows_y, depth, width = field_ref.shape
    chunks = depth // 8
    sub = lax.broadcasted_iota(jnp.int32, (8, width), 0)
    lane = lax.broadcasted_iota(jnp.int32, (8, width), 1)
    zero = jnp.zeros((8, width), jnp.float32)

    def body(it, carry):
        s = it // chunks
        part = it % chunks
        r = pl.multiple_of(part * 8, 8)

        def rows(c, y, off):
            if off == 0:
                return field_ref[s, c, y, pl.ds(r, 8), :]
            if off < 0:
                return jnp.where(
                    part == 0, zero, field_ref[s, c, y, pl.ds(jnp.maximum(r - 8, 0), 8), :]
                )
            return jnp.where(
                part == chunks - 1,
                zero,
                field_ref[s, c, y, pl.ds(jnp.minimum(r + 8, depth - 8), 8), :],
            )

        centre = [[rows(c, y, 0) for y in range(rows_y)] for c in range(3)]
        acc = [
            [GAMMA * cm_ref[y, pl.ds(r, 8), :] * centre[c][y] for y in range(rows_y)]
            for c in range(3)
        ]
        index = 0
        for off_x in (-1, 0, 1):
            if off_x == 0:
                shifted_x = centre
            elif off_x < 0:
                shifted_x = [
                    [
                        jnp.where(
                            sub == 0,
                            pltpu.roll(rows(c, y, -1), 1, 0),
                            pltpu.roll(centre[c][y], 1, 0),
                        )
                        for y in range(rows_y)
                    ]
                    for c in range(3)
                ]
            else:
                shifted_x = [
                    [
                        jnp.where(
                            sub == 7,
                            pltpu.roll(rows(c, y, 1), 7, 0),
                            pltpu.roll(centre[c][y], 7, 0),
                        )
                        for y in range(rows_y)
                    ]
                    for c in range(3)
                ]
            shifted = {0: shifted_x}
            shifted[-1] = [
                [jnp.where(lane == 0, jnp.float32(0.0), pltpu.roll(v, 1, 1)) for v in per_c]
                for per_c in shifted_x
            ]
            shifted[1] = [
                [
                    jnp.where(lane == width - 1, jnp.float32(0.0), pltpu.roll(v, width - 1, 1))
                    for v in per_c
                ]
                for per_c in shifted_x
            ]
            for off_y in (-1, 0, 1):
                for off_z in (-1, 0, 1):
                    if (off_x, off_y, off_z) == (0, 0, 0):
                        continue
                    offset = (off_x, off_y, off_z)
                    norm_sq = off_x * off_x + off_y * off_y + off_z * off_z
                    for y in range(rows_y):
                        edge = edge_ref[index, y, pl.ds(r, 8), :]
                        source = y + off_y
                        if 0 <= source < rows_y:
                            delta = [centre[c][y] - shifted[off_z][c][source] for c in range(3)]
                        else:
                            delta = [centre[c][y] for c in range(3)]
                        project = None
                        for c in range(3):
                            if offset[c] > 0:
                                project = delta[c] if project is None else project + delta[c]
                            elif offset[c] < 0:
                                project = -delta[c] if project is None else project - delta[c]
                        if norm_sq == 2:
                            project = project * 0.5
                        elif norm_sq == 3:
                            project = project * (1.0 / 3.0)
                        for c in range(3):
                            if offset[c] != 0:
                                acc[c][y] = acc[c][y] + edge * (delta[c] + BETA * offset[c] * project)
                            else:
                                acc[c][y] = acc[c][y] + edge * delta[c]
                    index += 1
        for c in range(3):
            for y in range(rows_y):
                out_ref[s, c, y, pl.ds(r, 8), :] = acc[c][y]
        return carry

    lax.fori_loop(0, samples * chunks, body, 0)


def chain_kernel(
    scal_ref, mask_ref, md_ref, ld_ref, mod_ref, disp_ref, res_ref,
    edge_s, cm_s, jac_s, k_s, a_s, step0_s, step1_s,
):
    samples, _, rows_y, depth, width = md_ref.shape
    theta = scal_ref[0]
    c1 = scal_ref[1]
    c2 = scal_ref[2]
    edges_body(mod_ref, edge_s, cm_s, jac_s)
    stencil_body(md_ref, edge_s, cm_s, k_s)
    keep0 = mask_ref[0] > 0.0
    keep1 = mask_ref[1] > 0.0

    def first(it, carry):
        s = it // 3
        c = it % 3
        for y in range(rows_y):
            start = ld_ref[s, c, y] - k_s[s, c, y]
            a_s[s, c, y] = start
            step0_s[s, c, y] = jnp.where(keep0, start / (theta * jac_s[c, y]), jnp.float32(0.0))
        return carry

    lax.fori_loop(0, samples * 3, first, 0)
    stencil_body(step0_s, edge_s, cm_s, k_s)

    def second(it, carry):
        s = it // 3
        c = it % 3
        for y in range(rows_y):
            residual1 = a_s[s, c, y] - k_s[s, c, y]
            a_s[s, c, y] = residual1
            step0 = step0_s[s, c, y]
            step1 = jnp.where(
                keep1, c1 * step0 + c2 * residual1 / jac_s[c, y], jnp.float32(0.0)
            )
            step1_s[s, c, y] = step1
            disp_ref[s, c, y] = md_ref[s, c, y] + step0 + step1
        return carry

    lax.fori_loop(0, samples * 3, second, 0)
    stencil_body(step1_s, edge_s, cm_s, k_s)

    def third(it, carry):
        s = it // 3
        c = it % 3
        for y in range(rows_y):
            res_ref[s, c, y] = a_s[s, c, y] - k_s[s, c, y]
        return carry

    lax.fori_loop(0, samples * 3, third, 0)


def run_chain(scalars, masks, md, ld, mod):
    samples, _, rows_y, depth, width = md.shape
    vmem = pl.BlockSpec(memory_space=pltpu.VMEM)
    smem = pl.BlockSpec(memory_space=pltpu.SMEM)
    field = jax.ShapeDtypeStruct(md.shape, jnp.float32)
    size = md.size
    return pl.pallas_call(
        chain_kernel,
        out_shape=(field, field),
        in_specs=[smem, vmem, vmem, vmem, vmem],
        out_specs=(vmem, vmem),
        scratch_shapes=[
            pltpu.VMEM((len(OFFSETS), rows_y, depth, width), jnp.float32),
            pltpu.VMEM((rows_y, depth, width), jnp.float32),
            pltpu.VMEM((3, rows_y, depth, width), jnp.float32),
        ]
        + [pltpu.VMEM(md.shape, jnp.float32)] * 4,
        compiler_params=pltpu.CompilerParams(vmem_limit_bytes=48 * 1024 * 1024),
        cost_estimate=pl.CostEstimate(
            flops=3 * 26 * 20 * size, bytes_accessed=4 * 5 * size, transcendentals=0
        ),
    )(scalars, masks, md, ld, mod)


def lookup_modulus(material, moduli):
    modulus = jnp.zeros(material.shape, jnp.float32)
    for index in range(MATERIALS):
        modulus = modulus + jnp.where(material == index, moduli[index], jnp.float32(0.0))
    return modulus


def neighbour_devices(part_device, partners):
    count = part_device.shape[0]
    ids = jnp.arange(count, dtype=jnp.int32)
    hit = part_device[None, :] == ids[:, None]
    place = jnp.sum(jnp.where(hit, ids[None, :], 0), axis=1)
    upper = place % 2 == 0
    up_dev = jnp.where(upper, partners[0], partners[1])
    low_dev = jnp.where(upper, partners[1], partners[0])
    return up_dev, low_dev


def exchange(first, last, up_dev, low_dev):
    col = lax.axis_index("col")
    grp = lax.axis_index("grp")
    me = col * GROUP + grp
    cols = up_dev.shape[0] // GROUP
    rows = first.shape[0]
    pack = jnp.concatenate([first, last], axis=0)[None]
    held = lax.all_gather(pack, "grp", axis=0, tiled=True)
    pick = (jnp.arange(GROUP, dtype=jnp.int32) == grp)[None, :]
    t_up = jnp.sum(jnp.where(pick, up_dev.reshape(cols, GROUP), 0), axis=1)
    t_low = jnp.sum(jnp.where(pick, low_dev.reshape(cols, GROUP), 0), axis=1)
    up_at = jnp.where(t_up // GROUP == col, t_up % GROUP, -1)[:, None]
    low_at = jnp.where(t_low // GROUP == col, t_low % GROUP, -1)[:, None]
    up_at = up_at[:, :, None]
    low_at = low_at[:, :, None]
    from_up = jnp.zeros((cols,) + first.shape, jnp.float32)
    from_low = jnp.zeros((cols,) + first.shape, jnp.float32)
    for k in range(GROUP):
        from_up = jnp.where(up_at == k, held[k, :rows][None], from_up)
        from_low = jnp.where(low_at == k, held[k, rows:][None], from_low)
    rows = first.shape[0]
    slots = jnp.concatenate([from_up, from_low], axis=1)
    got = lax.all_to_all(slots, "col", 0, 0, tiled=True)
    my_up = up_dev[me]
    my_low = low_dev[me]
    above = lax.dynamic_index_in_dim(got, my_up // GROUP, axis=0, keepdims=False)[:rows]
    below = lax.dynamic_index_in_dim(got, my_low // GROUP, axis=0, keepdims=False)[rows:]
    above = jnp.where(my_up != me, above, jnp.float32(0.0))
    below = jnp.where(my_low != me, below, jnp.float32(0.0))
    return below, above


def on_device(loads, modal_disp, material, moduli, part_device, partners, low_bound, high_bound):
    up_dev, low_dev = neighbour_devices(part_device, partners)
    samples, _, depth, rows_y, width = loads.shape
    loads = jnp.transpose(loads, (0, 1, 3, 2, 4))
    modal_disp = jnp.transpose(modal_disp, (0, 1, 3, 2, 4))
    flat_mod = lookup_modulus(material.reshape(depth, rows_y * width), moduli)
    modulus = jnp.stack([flat_mod[:, y * width : (y + 1) * width] for y in range(rows_y)], axis=0)
    plane = (samples, 3, rows_y, width)
    plane_size = samples * 3 * rows_y * width
    mod_size = rows_y * width

    def pack(md_rows, load_rows):
        parts = [modal_disp[:, :, :, r].reshape(-1) for r in md_rows]
        parts += [loads[:, :, :, r].reshape(-1) for r in load_rows]
        parts += [modulus[:, r].reshape(-1) for r in md_rows]
        flat = jnp.concatenate(parts)
        return flat.reshape(flat.shape[0] // width, width)

    first = pack((0, 1, 2), (0, 1))
    last = pack((depth - 3, depth - 2, depth - 1), (depth - 2, depth - 1))
    below, above = exchange(first, last, up_dev, low_dev)
    below = below.reshape(-1)
    above = above.reshape(-1)

    def planes_of(got, count, start, size, shape):
        return [got[start + i * size : start + (i + 1) * size].reshape(shape) for i in range(count)]

    md_below = planes_of(below, 3, 0, plane_size, plane)
    md_above = planes_of(above, 3, 0, plane_size, plane)
    ld_below = planes_of(below, 2, 3 * plane_size, plane_size, plane)
    ld_above = planes_of(above, 2, 3 * plane_size, plane_size, plane)
    mod_below = planes_of(below, 3, 5 * plane_size, mod_size, (rows_y, width))
    mod_above = planes_of(above, 3, 5 * plane_size, mod_size, (rows_y, width))

    def extend(own, lower, upper, axis):
        zero = jnp.zeros_like(lower[0])
        rows = [zero] * (8 - len(lower)) + list(lower)
        tail = list(upper) + [zero] * (8 - len(upper))
        return jnp.concatenate(
            [jnp.stack(rows, axis=axis), own, jnp.stack(tail, axis=axis)], axis=axis
        )

    low_on = low_dev[col_grp_index()] != col_grp_index()
    up_on = up_dev[col_grp_index()] != col_grp_index()
    zero_mod = jnp.zeros((rows_y, width), jnp.float32)
    zero_plane = jnp.zeros(plane, jnp.float32)

    theta = (high_bound[0] + low_bound[0]) / 2.0
    half = (high_bound[0] - low_bound[0]) / 2.0
    sigma = theta / half
    rho0 = 1.0 / sigma
    rho1 = 1.0 / (2.0 * sigma - rho0)

    scalars = jnp.stack([theta, rho1 * rho0, 2.0 * rho1 / half]).astype(jnp.float32)

    def chain(md, ld, mod, masks):
        return run_chain(scalars, masks, md, ld, mod)

    disp_local, res_local = chain(modal_disp, loads, modulus, jnp.ones((2, depth, width), jnp.float32))

    edge_rows = 8
    head = slice(0, edge_rows)
    tail = slice(depth - edge_rows, depth)

    def window(own, lower, upper, axis):
        zero = jnp.zeros_like(lower[0])
        rows = [zero] * (8 - len(lower)) + list(lower)
        after = list(upper) + [zero] * (8 - len(upper))
        index = [slice(None)] * own.ndim
        index[axis] = head
        own_head = own[tuple(index)]
        index[axis] = tail
        own_tail = own[tuple(index)]
        return jnp.concatenate(
            [jnp.stack(rows, axis=axis), own_head, own_tail, jnp.stack(after, axis=axis)], axis=axis
        )

    md_win = window(modal_disp, md_below, md_above, 3)
    ld_win = window(loads, ld_below, ld_above, 3)
    mod_win = window(modulus, mod_below, mod_above, 1)
    logical = jnp.concatenate(
        [
            jnp.arange(-8, edge_rows, dtype=jnp.int32),
            jnp.arange(depth - edge_rows, depth + 8, dtype=jnp.int32),
        ]
    )

    def valid(reach):
        keep = (logical >= 0) & (logical < depth)
        keep = keep | (low_on & (logical >= -reach) & (logical < 0))
        keep = keep | (up_on & (logical >= depth) & (logical < depth + reach))
        return jnp.broadcast_to(keep.astype(jnp.float32)[:, None], (logical.shape[0], width))

    masks = jnp.stack([valid(2), valid(1)], axis=0)
    disp_win, res_win = chain(md_win, ld_win, mod_win, masks)

    reach = 3
    sub_row = lax.broadcasted_iota(jnp.int32, (8, 1), 0)

    def merge(local, win):
        top = jnp.where(sub_row < reach, win[:, :, :, 8:16], local[:, :, :, 0:8])
        bottom = jnp.where(sub_row >= 8 - reach, win[:, :, :, 16:24], local[:, :, :, depth - 8 : depth])
        return jnp.concatenate([top, local[:, :, :, 8 : depth - 8], bottom], axis=3)

    displacement = merge(disp_local, disp_win)
    residual = merge(res_local, res_win)
    return (
        jnp.transpose(displacement, (0, 1, 3, 2, 4)),
        jnp.transpose(residual, (0, 1, 3, 2, 4)),
    )


def col_grp_index():
    return lax.axis_index("col") * GROUP + lax.axis_index("grp")


def solution(mesh):
    devices = mesh.devices.reshape(-1)
    grid = Mesh(devices.reshape(devices.size // GROUP, GROUP), ("col", "grp"))
    slab = ("col", "grp")
    in_specs = (
        P(None, None, slab, None, None),
        P(None, None, slab, None, None),
        P(slab, None, None),
        P(),
        P(),
        P(),
        P(),
        P(),
    )
    out_specs = (P(None, None, slab, None, None), P(None, None, slab, None, None))
    return jax.shard_map(
        on_device, mesh=grid, in_specs=in_specs, out_specs=out_specs, check_vma=False
    )
```

```python
import jax
import jax.numpy as jnp
from jax import lax
from jax.experimental import pallas as pl
from jax.experimental.pallas import tpu as pltpu
from jax.sharding import Mesh, PartitionSpec as P

MATERIALS = 8
GROUP = 8

GAMMA = 0.2
BETA = 0.5
EDGE_WEIGHTS = (0.0, 1.0, 0.5, 0.25)
OFFSETS = [
    (a, b, c) for a in (-1, 0, 1) for b in (-1, 0, 1) for c in (-1, 0, 1) if (a, b, c) != (0, 0, 0)
]


def shift_cells(array, axis, step):
    if step == 0:
        return array
    length = array.shape[axis]
    zero = jnp.zeros_like(lax.slice_in_dim(array, 0, 1, axis=axis))
    if step > 0:
        return jnp.concatenate([lax.slice_in_dim(array, 1, length, axis=axis), zero], axis=axis)
    return jnp.concatenate([zero, lax.slice_in_dim(array, 0, length - 1, axis=axis)], axis=axis)


def mod_neighbour(mod_ext, off_x, off_y, off_z, depth):
    rows = lax.slice_in_dim(mod_ext, 1 + off_x, 1 + off_x + depth, axis=1)
    return shift_cells(shift_cells(rows, 0, off_y), 2, off_z)


def edges_of(mod_ext, depth):
    centre = mod_neighbour(mod_ext, 0, 0, 0, depth)
    edges = []
    for offset in OFFSETS:
        norm_sq = offset[0] * offset[0] + offset[1] * offset[1] + offset[2] * offset[2]
        edges.append(
            EDGE_WEIGHTS[norm_sq]
            * 0.5
            * (centre + mod_neighbour(mod_ext, offset[0], offset[1], offset[2], depth))
        )
    return centre, edges


def diagonal_of(centre, edges):
    comps = [GAMMA * centre, GAMMA * centre, GAMMA * centre]
    for offset, edge in zip(OFFSETS, edges):
        norm_sq = offset[0] * offset[0] + offset[1] * offset[1] + offset[2] * offset[2]
        for comp in range(3):
            comps[comp] = comps[comp] + edge * (1.0 + BETA * offset[comp] * offset[comp] / norm_sq)
    return jnp.stack(comps, axis=0)


def edges_body(mod_ref, edge_ref, centre_ref, diag_ref):
    rows_y, depth, width = mod_ref.shape
    chunks = depth // 8
    sub = lax.broadcasted_iota(jnp.int32, (8, width), 0)
    lane = lax.broadcasted_iota(jnp.int32, (8, width), 1)
    zero = jnp.zeros((8, width), jnp.float32)

    def body(it, carry):
        r = pl.multiple_of(it * 8, 8)
        centre = [mod_ref[y, pl.ds(r, 8), :] for y in range(rows_y)]
        prev = [
            jnp.where(it == 0, zero, mod_ref[y, pl.ds(jnp.maximum(r - 8, 0), 8), :])
            for y in range(rows_y)
        ]
        nxt = [
            jnp.where(it == chunks - 1, zero, mod_ref[y, pl.ds(jnp.minimum(r + 8, depth - 8), 8), :])
            for y in range(rows_y)
        ]
        comps = [[GAMMA * centre[y] for y in range(rows_y)] for c in range(3)]
        index = 0
        for off_x in (-1, 0, 1):
            if off_x == 0:
                shifted_x = centre
            elif off_x < 0:
                shifted_x = [
                    jnp.where(sub == 0, pltpu.roll(prev[y], 1, 0), pltpu.roll(centre[y], 1, 0))
                    for y in range(rows_y)
                ]
            else:
                shifted_x = [
                    jnp.where(sub == 7, pltpu.roll(nxt[y], 7, 0), pltpu.roll(centre[y], 7, 0))
                    for y in range(rows_y)
                ]
            shifted = {0: shifted_x}
            shifted[-1] = [jnp.where(lane == 0, jnp.float32(0.0), pltpu.roll(v, 1, 1)) for v in shifted_x]
            shifted[1] = [
                jnp.where(lane == width - 1, jnp.float32(0.0), pltpu.roll(v, width - 1, 1))
                for v in shifted_x
            ]
            for off_y in (-1, 0, 1):
                for off_z in (-1, 0, 1):
                    if (off_x, off_y, off_z) == (0, 0, 0):
                        continue
                    offset = (off_x, off_y, off_z)
                    norm_sq = off_x * off_x + off_y * off_y + off_z * off_z
                    for y in range(rows_y):
                        source = y + off_y
                        if 0 <= source < rows_y:
                            other = shifted[off_z][source]
                        else:
                            other = zero
                        edge = EDGE_WEIGHTS[norm_sq] * 0.5 * (centre[y] + other)
                        edge_ref[index, y, pl.ds(r, 8), :] = edge
                        for c in range(3):
                            comps[c][y] = comps[c][y] + edge * (
                                1.0 + BETA * offset[c] * offset[c] / norm_sq
                            )
                    index += 1
        for y in range(rows_y):
            centre_ref[y, pl.ds(r, 8), :] = centre[y]
            for c in range(3):
                diag_ref[c, y, pl.ds(r, 8), :] = comps[c][y]
        return carry

    lax.fori_loop(0, chunks, body, 0)


def stencil_body(field_ref, edge_ref, cm_ref, out_ref):
    samples, _, rows_y, depth, width = field_ref.shape
    chunks = depth // 8
    sub = lax.broadcasted_iota(jnp.int32, (8, width), 0)
    lane = lax.broadcasted_iota(jnp.int32, (8, width), 1)
    zero = jnp.zeros((8, width), jnp.float32)

    def body(it, carry):
        s = it // chunks
        part = it % chunks
        r = pl.multiple_of(part * 8, 8)

        def rows(c, y, off):
            if off == 0:
                return field_ref[s, c, y, pl.ds(r, 8), :]
            if off < 0:
                return jnp.where(
                    part == 0, zero, field_ref[s, c, y, pl.ds(jnp.maximum(r - 8, 0), 8), :]
                )
            return jnp.where(
                part == chunks - 1,
                zero,
                field_ref[s, c, y, pl.ds(jnp.minimum(r + 8, depth - 8), 8), :],
            )

        centre = [[rows(c, y, 0) for y in range(rows_y)] for c in range(3)]
        acc = [
            [GAMMA * cm_ref[y, pl.ds(r, 8), :] * centre[c][y] for y in range(rows_y)]
            for c in range(3)
        ]
        index = 0
        for off_x in (-1, 0, 1):
            if off_x == 0:
                shifted_x = centre
            elif off_x < 0:
                shifted_x = [
                    [
                        jnp.where(
                            sub == 0,
                            pltpu.roll(rows(c, y, -1), 1, 0),
                            pltpu.roll(centre[c][y], 1, 0),
                        )
                        for y in range(rows_y)
                    ]
                    for c in range(3)
                ]
            else:
                shifted_x = [
                    [
                        jnp.where(
                            sub == 7,
                            pltpu.roll(rows(c, y, 1), 7, 0),
                            pltpu.roll(centre[c][y], 7, 0),
                        )
                        for y in range(rows_y)
                    ]
                    for c in range(3)
                ]
            shifted = {0: shifted_x}
            shifted[-1] = [
                [jnp.where(lane == 0, jnp.float32(0.0), pltpu.roll(v, 1, 1)) for v in per_c]
                for per_c in shifted_x
            ]
            shifted[1] = [
                [
                    jnp.where(lane == width - 1, jnp.float32(0.0), pltpu.roll(v, width - 1, 1))
                    for v in per_c
                ]
                for per_c in shifted_x
            ]
            for off_y in (-1, 0, 1):
                for off_z in (-1, 0, 1):
                    if (off_x, off_y, off_z) == (0, 0, 0):
                        continue
                    offset = (off_x, off_y, off_z)
                    norm_sq = off_x * off_x + off_y * off_y + off_z * off_z
                    for y in range(rows_y):
                        edge = edge_ref[index, y, pl.ds(r, 8), :]
                        source = y + off_y
                        if 0 <= source < rows_y:
                            delta = [centre[c][y] - shifted[off_z][c][source] for c in range(3)]
                        else:
                            delta = [centre[c][y] for c in range(3)]
                        project = None
                        for c in range(3):
                            if offset[c] > 0:
                                project = delta[c] if project is None else project + delta[c]
                            elif offset[c] < 0:
                                project = -delta[c] if project is None else project - delta[c]
                        if norm_sq == 2:
                            project = project * 0.5
                        elif norm_sq == 3:
                            project = project * (1.0 / 3.0)
                        for c in range(3):
                            if offset[c] != 0:
                                acc[c][y] = acc[c][y] + edge * (delta[c] + BETA * offset[c] * project)
                            else:
                                acc[c][y] = acc[c][y] + edge * delta[c]
                    index += 1
        for c in range(3):
            for y in range(rows_y):
                out_ref[s, c, y, pl.ds(r, 8), :] = acc[c][y]
        return carry

    lax.fori_loop(0, samples * chunks, body, 0)


def chain_kernel(
    scal_ref, mask_ref, md_ref, ld_ref, mod_ref, disp_ref, res_ref,
    edge_s, cm_s, jac_s, k_s, a_s, step0_s, step1_s,
):
    samples, _, rows_y, depth, width = md_ref.shape
    theta = scal_ref[0]
    c1 = scal_ref[1]
    c2 = scal_ref[2]
    edges_body(mod_ref, edge_s, cm_s, jac_s)
    stencil_body(md_ref, edge_s, cm_s, k_s)
    keep0 = mask_ref[0] > 0.0
    keep1 = mask_ref[1] > 0.0

    def first(it, carry):
        s = it // 3
        c = it % 3
        for y in range(rows_y):
            start = ld_ref[s, c, y] - k_s[s, c, y]
            a_s[s, c, y] = start
            step0_s[s, c, y] = jnp.where(keep0, start / (theta * jac_s[c, y]), jnp.float32(0.0))
        return carry

    lax.fori_loop(0, samples * 3, first, 0)
    stencil_body(step0_s, edge_s, cm_s, k_s)

    def second(it, carry):
        s = it // 3
        c = it % 3
        for y in range(rows_y):
            residual1 = a_s[s, c, y] - k_s[s, c, y]
            a_s[s, c, y] = residual1
            step0 = step0_s[s, c, y]
            step1 = jnp.where(
                keep1, c1 * step0 + c2 * residual1 / jac_s[c, y], jnp.float32(0.0)
            )
            step1_s[s, c, y] = step1
            disp_ref[s, c, y] = md_ref[s, c, y] + step0 + step1
        return carry

    lax.fori_loop(0, samples * 3, second, 0)
    stencil_body(step1_s, edge_s, cm_s, k_s)

    def third(it, carry):
        s = it // 3
        c = it % 3
        for y in range(rows_y):
            res_ref[s, c, y] = a_s[s, c, y] - k_s[s, c, y]
        return carry

    lax.fori_loop(0, samples * 3, third, 0)


def run_chain(scalars, masks, md, ld, mod):
    samples, _, rows_y, depth, width = md.shape
    vmem = pl.BlockSpec(memory_space=pltpu.VMEM)
    smem = pl.BlockSpec(memory_space=pltpu.SMEM)
    field = jax.ShapeDtypeStruct(md.shape, jnp.float32)
    size = md.size
    return pl.pallas_call(
        chain_kernel,
        out_shape=(field, field),
        in_specs=[smem, vmem, vmem, vmem, vmem],
        out_specs=(vmem, vmem),
        scratch_shapes=[
            pltpu.VMEM((len(OFFSETS), rows_y, depth, width), jnp.float32),
            pltpu.VMEM((rows_y, depth, width), jnp.float32),
            pltpu.VMEM((3, rows_y, depth, width), jnp.float32),
        ]
        + [pltpu.VMEM(md.shape, jnp.float32)] * 4,
        compiler_params=pltpu.CompilerParams(vmem_limit_bytes=48 * 1024 * 1024),
        cost_estimate=pl.CostEstimate(
            flops=3 * 26 * 20 * size, bytes_accessed=4 * 5 * size, transcendentals=0
        ),
    )(scalars, masks, md, ld, mod)


def lookup_modulus(material, moduli):
    modulus = jnp.zeros(material.shape, jnp.float32)
    for index in range(MATERIALS):
        modulus = modulus + jnp.where(material == float(index), moduli[index], jnp.float32(0.0))
    return modulus


def neighbour_devices(part_device, partners):
    count = part_device.shape[0]
    ids = jnp.arange(count, dtype=jnp.int32)
    hit = part_device[None, :] == ids[:, None]
    place = jnp.sum(jnp.where(hit, ids[None, :], 0), axis=1)
    upper = place % 2 == 0
    up_dev = jnp.where(upper, partners[0], partners[1])
    low_dev = jnp.where(upper, partners[1], partners[0])
    return up_dev, low_dev


def exchange(first, last, up_dev, low_dev):
    col = lax.axis_index("col")
    grp = lax.axis_index("grp")
    me = col * GROUP + grp
    cols = up_dev.shape[0] // GROUP
    rows = first.shape[0]
    pack = jnp.concatenate([first, last], axis=0)[None]
    held = lax.all_gather(pack, "grp", axis=0, tiled=True)
    pick = (jnp.arange(GROUP, dtype=jnp.int32) == grp)[None, :]
    t_up = jnp.sum(jnp.where(pick, up_dev.reshape(cols, GROUP), 0), axis=1)
    t_low = jnp.sum(jnp.where(pick, low_dev.reshape(cols, GROUP), 0), axis=1)
    up_at = jnp.where(t_up // GROUP == col, t_up % GROUP, -1)[:, None]
    low_at = jnp.where(t_low // GROUP == col, t_low % GROUP, -1)[:, None]
    up_at = up_at[:, :, None]
    low_at = low_at[:, :, None]
    from_up = jnp.zeros((cols,) + first.shape, jnp.float32)
    from_low = jnp.zeros((cols,) + first.shape, jnp.float32)
    for k in range(GROUP):
        from_up = jnp.where(up_at == k, held[k, :rows][None], from_up)
        from_low = jnp.where(low_at == k, held[k, rows:][None], from_low)
    rows = first.shape[0]
    slots = jnp.concatenate([from_up, from_low], axis=1)
    got = lax.all_to_all(slots, "col", 0, 0, tiled=True)
    my_up = up_dev[me]
    my_low = low_dev[me]
    above = lax.dynamic_index_in_dim(got, my_up // GROUP, axis=0, keepdims=False)[:rows]
    below = lax.dynamic_index_in_dim(got, my_low // GROUP, axis=0, keepdims=False)[rows:]
    above = jnp.where(my_up != me, above, jnp.float32(0.0))
    below = jnp.where(my_low != me, below, jnp.float32(0.0))
    return below, above


def on_device(loads, modal_disp, material, moduli, part_device, partners, low_bound, high_bound):
    up_dev, low_dev = neighbour_devices(part_device, partners)
    samples, _, depth, rows_y, width = loads.shape
    loads = jnp.transpose(loads, (0, 1, 3, 2, 4))
    modal_disp = jnp.transpose(modal_disp, (0, 1, 3, 2, 4))
    ids = lax.optimization_barrier(jnp.transpose(material.astype(jnp.float32), (1, 0, 2)))
    modulus = lookup_modulus(ids, moduli)
    plane = (samples, 3, rows_y, width)
    plane_size = samples * 3 * rows_y * width
    mod_size = rows_y * width

    def pack(md_rows, load_rows):
        parts = [modal_disp[:, :, :, r].reshape(-1) for r in md_rows]
        parts += [loads[:, :, :, r].reshape(-1) for r in load_rows]
        parts += [modulus[:, r].reshape(-1) for r in md_rows]
        flat = jnp.concatenate(parts)
        return flat.reshape(flat.shape[0] // width, width)

    first = pack((0, 1, 2), (0, 1))
    last = pack((depth - 3, depth - 2, depth - 1), (depth - 2, depth - 1))
    below, above = exchange(first, last, up_dev, low_dev)
    below = below.reshape(-1)
    above = above.reshape(-1)

    def planes_of(got, count, start, size, shape):
        return [got[start + i * size : start + (i + 1) * size].reshape(shape) for i in range(count)]

    md_below = planes_of(below, 3, 0, plane_size, plane)
    md_above = planes_of(above, 3, 0, plane_size, plane)
    ld_below = planes_of(below, 2, 3 * plane_size, plane_size, plane)
    ld_above = planes_of(above, 2, 3 * plane_size, plane_size, plane)
    mod_below = planes_of(below, 3, 5 * plane_size, mod_size, (rows_y, width))
    mod_above = planes_of(above, 3, 5 * plane_size, mod_size, (rows_y, width))

    def extend(own, lower, upper, axis):
        zero = jnp.zeros_like(lower[0])
        rows = [zero] * (8 - len(lower)) + list(lower)
        tail = list(upper) + [zero] * (8 - len(upper))
        return jnp.concatenate(
            [jnp.stack(rows, axis=axis), own, jnp.stack(tail, axis=axis)], axis=axis
        )

    low_on = low_dev[col_grp_index()] != col_grp_index()
    up_on = up_dev[col_grp_index()] != col_grp_index()
    zero_mod = jnp.zeros((rows_y, width), jnp.float32)
    zero_plane = jnp.zeros(plane, jnp.float32)

    theta = (high_bound[0] + low_bound[0]) / 2.0
    half = (high_bound[0] - low_bound[0]) / 2.0
    sigma = theta / half
    rho0 = 1.0 / sigma
    rho1 = 1.0 / (2.0 * sigma - rho0)

    scalars = jnp.stack([theta, rho1 * rho0, 2.0 * rho1 / half]).astype(jnp.float32)

    def chain(md, ld, mod, masks):
        return run_chain(scalars, masks, md, ld, mod)

    disp_local, res_local = chain(modal_disp, loads, modulus, jnp.ones((2, depth, width), jnp.float32))

    edge_rows = 8
    head = slice(0, edge_rows)
    tail = slice(depth - edge_rows, depth)

    def window(own, lower, upper, axis):
        zero = jnp.zeros_like(lower[0])
        rows = [zero] * (8 - len(lower)) + list(lower)
        after = list(upper) + [zero] * (8 - len(upper))
        index = [slice(None)] * own.ndim
        index[axis] = head
        own_head = own[tuple(index)]
        index[axis] = tail
        own_tail = own[tuple(index)]
        return jnp.concatenate(
            [jnp.stack(rows, axis=axis), own_head, own_tail, jnp.stack(after, axis=axis)], axis=axis
        )

    md_win = window(modal_disp, md_below, md_above, 3)
    ld_win = window(loads, ld_below, ld_above, 3)
    mod_win = window(modulus, mod_below, mod_above, 1)
    logical = jnp.concatenate(
        [
            jnp.arange(-8, edge_rows, dtype=jnp.int32),
            jnp.arange(depth - edge_rows, depth + 8, dtype=jnp.int32),
        ]
    )

    def valid(reach):
        keep = (logical >= 0) & (logical < depth)
        keep = keep | (low_on & (logical >= -reach) & (logical < 0))
        keep = keep | (up_on & (logical >= depth) & (logical < depth + reach))
        return jnp.broadcast_to(keep.astype(jnp.float32)[:, None], (logical.shape[0], width))

    masks = jnp.stack([valid(2), valid(1)], axis=0)
    disp_win, res_win = chain(md_win, ld_win, mod_win, masks)

    reach = 3
    sub_row = lax.broadcasted_iota(jnp.int32, (8, 1), 0)

    def merge(local, win):
        top = jnp.where(sub_row < reach, win[:, :, :, 8:16], local[:, :, :, 0:8])
        bottom = jnp.where(sub_row >= 8 - reach, win[:, :, :, 16:24], local[:, :, :, depth - 8 : depth])
        return jnp.concatenate([top, local[:, :, :, 8 : depth - 8], bottom], axis=3)

    displacement = merge(disp_local, disp_win)
    residual = merge(res_local, res_win)
    return (
        jnp.transpose(displacement, (0, 1, 3, 2, 4)),
        jnp.transpose(residual, (0, 1, 3, 2, 4)),
    )


def col_grp_index():
    return lax.axis_index("col") * GROUP + lax.axis_index("grp")


def solution(mesh):
    devices = mesh.devices.reshape(-1)
    grid = Mesh(devices.reshape(devices.size // GROUP, GROUP), ("col", "grp"))
    slab = ("col", "grp")
    in_specs = (
        P(None, None, slab, None, None),
        P(None, None, slab, None, None),
        P(slab, None, None),
        P(),
        P(),
        P(),
        P(),
        P(),
    )
    out_specs = (P(None, None, slab, None, None), P(None, None, slab, None, None))
    return jax.shard_map(
        on_device, mesh=grid, in_specs=in_specs, out_specs=out_specs, check_vma=False
    )
```

```python
import jax
import jax.numpy as jnp
from jax import lax
from jax.experimental import pallas as pl
from jax.experimental.pallas import tpu as pltpu
from jax.sharding import Mesh, PartitionSpec as P

MATERIALS = 8
GROUP = 8

GAMMA = 0.2
BETA = 0.5
EDGE_WEIGHTS = (0.0, 1.0, 0.5, 0.25)
OFFSETS = [
    (a, b, c) for a in (-1, 0, 1) for b in (-1, 0, 1) for c in (-1, 0, 1) if (a, b, c) != (0, 0, 0)
]


def shift_cells(array, axis, step):
    if step == 0:
        return array
    length = array.shape[axis]
    zero = jnp.zeros_like(lax.slice_in_dim(array, 0, 1, axis=axis))
    if step > 0:
        return jnp.concatenate([lax.slice_in_dim(array, 1, length, axis=axis), zero], axis=axis)
    return jnp.concatenate([zero, lax.slice_in_dim(array, 0, length - 1, axis=axis)], axis=axis)


def mod_neighbour(mod_ext, off_x, off_y, off_z, depth):
    rows = lax.slice_in_dim(mod_ext, 1 + off_x, 1 + off_x + depth, axis=1)
    return shift_cells(shift_cells(rows, 0, off_y), 2, off_z)


def edges_of(mod_ext, depth):
    centre = mod_neighbour(mod_ext, 0, 0, 0, depth)
    edges = []
    for offset in OFFSETS:
        norm_sq = offset[0] * offset[0] + offset[1] * offset[1] + offset[2] * offset[2]
        edges.append(
            EDGE_WEIGHTS[norm_sq]
            * 0.5
            * (centre + mod_neighbour(mod_ext, offset[0], offset[1], offset[2], depth))
        )
    return centre, edges


def diagonal_of(centre, edges):
    comps = [GAMMA * centre, GAMMA * centre, GAMMA * centre]
    for offset, edge in zip(OFFSETS, edges):
        norm_sq = offset[0] * offset[0] + offset[1] * offset[1] + offset[2] * offset[2]
        for comp in range(3):
            comps[comp] = comps[comp] + edge * (1.0 + BETA * offset[comp] * offset[comp] / norm_sq)
    return jnp.stack(comps, axis=0)


def edges_body(mod_ref, edge_ref, centre_ref, diag_ref):
    rows_y, depth, width = mod_ref.shape
    chunks = depth // 8
    sub = lax.broadcasted_iota(jnp.int32, (8, width), 0)
    lane = lax.broadcasted_iota(jnp.int32, (8, width), 1)
    zero = jnp.zeros((8, width), jnp.float32)

    def body(it, carry):
        r = pl.multiple_of(it * 8, 8)
        centre = [mod_ref[y, pl.ds(r, 8), :] for y in range(rows_y)]
        prev = [
            jnp.where(it == 0, zero, mod_ref[y, pl.ds(jnp.maximum(r - 8, 0), 8), :])
            for y in range(rows_y)
        ]
        nxt = [
            jnp.where(it == chunks - 1, zero, mod_ref[y, pl.ds(jnp.minimum(r + 8, depth - 8), 8), :])
            for y in range(rows_y)
        ]
        comps = [[GAMMA * centre[y] for y in range(rows_y)] for c in range(3)]
        index = 0
        for off_x in (-1, 0, 1):
            if off_x == 0:
                shifted_x = centre
            elif off_x < 0:
                shifted_x = [
                    jnp.where(sub == 0, pltpu.roll(prev[y], 1, 0), pltpu.roll(centre[y], 1, 0))
                    for y in range(rows_y)
                ]
            else:
                shifted_x = [
                    jnp.where(sub == 7, pltpu.roll(nxt[y], 7, 0), pltpu.roll(centre[y], 7, 0))
                    for y in range(rows_y)
                ]
            shifted = {0: shifted_x}
            shifted[-1] = [jnp.where(lane == 0, jnp.float32(0.0), pltpu.roll(v, 1, 1)) for v in shifted_x]
            shifted[1] = [
                jnp.where(lane == width - 1, jnp.float32(0.0), pltpu.roll(v, width - 1, 1))
                for v in shifted_x
            ]
            for off_y in (-1, 0, 1):
                for off_z in (-1, 0, 1):
                    if (off_x, off_y, off_z) == (0, 0, 0):
                        continue
                    offset = (off_x, off_y, off_z)
                    norm_sq = off_x * off_x + off_y * off_y + off_z * off_z
                    for y in range(rows_y):
                        source = y + off_y
                        if 0 <= source < rows_y:
                            other = shifted[off_z][source]
                        else:
                            other = zero
                        edge = EDGE_WEIGHTS[norm_sq] * 0.5 * (centre[y] + other)
                        edge_ref[index, y, pl.ds(r, 8), :] = edge
                        for c in range(3):
                            comps[c][y] = comps[c][y] + edge * (
                                1.0 + BETA * offset[c] * offset[c] / norm_sq
                            )
                    index += 1
        for y in range(rows_y):
            centre_ref[y, pl.ds(r, 8), :] = centre[y]
            for c in range(3):
                diag_ref[c, y, pl.ds(r, 8), :] = comps[c][y]
        return carry

    lax.fori_loop(0, chunks, body, 0)


def stencil_body(field_ref, edge_ref, cm_ref, out_ref):
    samples, _, rows_y, depth, width = field_ref.shape
    chunks = depth // 8
    sub = lax.broadcasted_iota(jnp.int32, (8, width), 0)
    lane = lax.broadcasted_iota(jnp.int32, (8, width), 1)
    zero = jnp.zeros((8, width), jnp.float32)

    def body(it, carry):
        s = it // chunks
        part = it % chunks
        r = pl.multiple_of(part * 8, 8)

        def rows(c, y, off):
            if off == 0:
                return field_ref[s, c, y, pl.ds(r, 8), :]
            if off < 0:
                return jnp.where(
                    part == 0, zero, field_ref[s, c, y, pl.ds(jnp.maximum(r - 8, 0), 8), :]
                )
            return jnp.where(
                part == chunks - 1,
                zero,
                field_ref[s, c, y, pl.ds(jnp.minimum(r + 8, depth - 8), 8), :],
            )

        centre = [[rows(c, y, 0) for y in range(rows_y)] for c in range(3)]
        acc = [
            [GAMMA * cm_ref[y, pl.ds(r, 8), :] * centre[c][y] for y in range(rows_y)]
            for c in range(3)
        ]
        index = 0
        for off_x in (-1, 0, 1):
            if off_x == 0:
                shifted_x = centre
            elif off_x < 0:
                shifted_x = [
                    [
                        jnp.where(
                            sub == 0,
                            pltpu.roll(rows(c, y, -1), 1, 0),
                            pltpu.roll(centre[c][y], 1, 0),
                        )
                        for y in range(rows_y)
                    ]
                    for c in range(3)
                ]
            else:
                shifted_x = [
                    [
                        jnp.where(
                            sub == 7,
                            pltpu.roll(rows(c, y, 1), 7, 0),
                            pltpu.roll(centre[c][y], 7, 0),
                        )
                        for y in range(rows_y)
                    ]
                    for c in range(3)
                ]
            shifted = {0: shifted_x}
            shifted[-1] = [
                [jnp.where(lane == 0, jnp.float32(0.0), pltpu.roll(v, 1, 1)) for v in per_c]
                for per_c in shifted_x
            ]
            shifted[1] = [
                [
                    jnp.where(lane == width - 1, jnp.float32(0.0), pltpu.roll(v, width - 1, 1))
                    for v in per_c
                ]
                for per_c in shifted_x
            ]
            for off_y in (-1, 0, 1):
                for off_z in (-1, 0, 1):
                    if (off_x, off_y, off_z) == (0, 0, 0):
                        continue
                    offset = (off_x, off_y, off_z)
                    norm_sq = off_x * off_x + off_y * off_y + off_z * off_z
                    for y in range(rows_y):
                        edge = edge_ref[index, y, pl.ds(r, 8), :]
                        source = y + off_y
                        if 0 <= source < rows_y:
                            delta = [centre[c][y] - shifted[off_z][c][source] for c in range(3)]
                        else:
                            delta = [centre[c][y] for c in range(3)]
                        project = None
                        for c in range(3):
                            if offset[c] > 0:
                                project = delta[c] if project is None else project + delta[c]
                            elif offset[c] < 0:
                                project = -delta[c] if project is None else project - delta[c]
                        if norm_sq == 2:
                            project = project * 0.5
                        elif norm_sq == 3:
                            project = project * (1.0 / 3.0)
                        for c in range(3):
                            if offset[c] != 0:
                                acc[c][y] = acc[c][y] + edge * (delta[c] + BETA * offset[c] * project)
                            else:
                                acc[c][y] = acc[c][y] + edge * delta[c]
                    index += 1
        for c in range(3):
            for y in range(rows_y):
                out_ref[s, c, y, pl.ds(r, 8), :] = acc[c][y]
        return carry

    lax.fori_loop(0, samples * chunks, body, 0)


def chain_kernel(
    scal_ref, mask_ref, md_ref, ld_ref, mod_ref, disp_ref, res_ref,
    edge_s, cm_s, jac_s, k_s, a_s, step0_s, step1_s,
):
    samples, _, rows_y, depth, width = md_ref.shape
    theta = scal_ref[0]
    c1 = scal_ref[1]
    c2 = scal_ref[2]
    edges_body(mod_ref, edge_s, cm_s, jac_s)
    stencil_body(md_ref, edge_s, cm_s, k_s)
    keep0 = mask_ref[0] > 0.0
    keep1 = mask_ref[1] > 0.0

    def first(it, carry):
        s = it // 3
        c = it % 3
        for y in range(rows_y):
            start = ld_ref[s, c, y] - k_s[s, c, y]
            a_s[s, c, y] = start
            step0_s[s, c, y] = jnp.where(keep0, start / (theta * jac_s[c, y]), jnp.float32(0.0))
        return carry

    lax.fori_loop(0, samples * 3, first, 0)
    stencil_body(step0_s, edge_s, cm_s, k_s)

    def second(it, carry):
        s = it // 3
        c = it % 3
        for y in range(rows_y):
            residual1 = a_s[s, c, y] - k_s[s, c, y]
            a_s[s, c, y] = residual1
            step0 = step0_s[s, c, y]
            step1 = jnp.where(
                keep1, c1 * step0 + c2 * residual1 / jac_s[c, y], jnp.float32(0.0)
            )
            step1_s[s, c, y] = step1
            disp_ref[s, c, y] = md_ref[s, c, y] + step0 + step1
        return carry

    lax.fori_loop(0, samples * 3, second, 0)
    stencil_body(step1_s, edge_s, cm_s, k_s)

    def third(it, carry):
        s = it // 3
        c = it % 3
        for y in range(rows_y):
            res_ref[s, c, y] = a_s[s, c, y] - k_s[s, c, y]
        return carry

    lax.fori_loop(0, samples * 3, third, 0)


def run_chain(scalars, masks, md, ld, mod):
    samples, _, rows_y, depth, width = md.shape
    vmem = pl.BlockSpec(memory_space=pltpu.VMEM)
    smem = pl.BlockSpec(memory_space=pltpu.SMEM)
    field = jax.ShapeDtypeStruct(md.shape, jnp.float32)
    size = md.size
    return pl.pallas_call(
        chain_kernel,
        out_shape=(field, field),
        in_specs=[smem, vmem, vmem, vmem, vmem],
        out_specs=(vmem, vmem),
        scratch_shapes=[
            pltpu.VMEM((len(OFFSETS), rows_y, depth, width), jnp.float32),
            pltpu.VMEM((rows_y, depth, width), jnp.float32),
            pltpu.VMEM((3, rows_y, depth, width), jnp.float32),
        ]
        + [pltpu.VMEM(md.shape, jnp.float32)] * 4,
        compiler_params=pltpu.CompilerParams(vmem_limit_bytes=48 * 1024 * 1024),
        cost_estimate=pl.CostEstimate(
            flops=3 * 26 * 20 * size, bytes_accessed=4 * 5 * size, transcendentals=0
        ),
    )(scalars, masks, md, ld, mod)


def lookup_modulus(material, moduli):
    modulus = jnp.zeros(material.shape, jnp.float32)
    for index in range(MATERIALS):
        modulus = modulus + jnp.where(material == float(index), moduli[index], jnp.float32(0.0))
    return modulus


def neighbour_devices(part_device, partners):
    count = part_device.shape[0]
    ids = jnp.arange(count, dtype=jnp.int32)
    hit = part_device[None, :] == ids[:, None]
    place = jnp.sum(jnp.where(hit, ids[None, :], 0), axis=1)
    upper = place % 2 == 0
    up_dev = jnp.where(upper, partners[0], partners[1])
    low_dev = jnp.where(upper, partners[1], partners[0])
    return up_dev, low_dev


def exchange(first, last, up_dev, low_dev):
    col = lax.axis_index("col")
    grp = lax.axis_index("grp")
    me = col * GROUP + grp
    cols = up_dev.shape[0] // GROUP
    rows = first.shape[0]
    pack = jnp.concatenate([first, last], axis=0)[None]
    held = lax.all_gather(pack, "grp", axis=0, tiled=True)
    pick = (jnp.arange(GROUP, dtype=jnp.int32) == grp)[None, :]
    t_up = jnp.sum(jnp.where(pick, up_dev.reshape(cols, GROUP), 0), axis=1)
    t_low = jnp.sum(jnp.where(pick, low_dev.reshape(cols, GROUP), 0), axis=1)
    up_at = jnp.where(t_up // GROUP == col, t_up % GROUP, -1)[:, None]
    low_at = jnp.where(t_low // GROUP == col, t_low % GROUP, -1)[:, None]
    up_at = up_at[:, :, None]
    low_at = low_at[:, :, None]
    from_up = jnp.zeros((cols,) + first.shape, jnp.float32)
    from_low = jnp.zeros((cols,) + first.shape, jnp.float32)
    for k in range(GROUP):
        from_up = jnp.where(up_at == k, held[k, :rows][None], from_up)
        from_low = jnp.where(low_at == k, held[k, rows:][None], from_low)
    rows = first.shape[0]
    slots = jnp.concatenate([from_up, from_low], axis=1)
    got = lax.all_to_all(slots, "col", 0, 0, tiled=True)
    mine = jnp.arange(up_dev.shape[0], dtype=jnp.int32) == me
    my_up = jnp.sum(jnp.where(mine, up_dev, 0))
    my_low = jnp.sum(jnp.where(mine, low_dev, 0))
    above = jnp.zeros(first.shape, jnp.float32)
    below = jnp.zeros(first.shape, jnp.float32)
    for k in range(cols):
        above = jnp.where((my_up // GROUP == k) & (my_up != me), got[k, :rows], above)
        below = jnp.where((my_low // GROUP == k) & (my_low != me), got[k, rows:], below)
    return below, above


def on_device(loads, modal_disp, material, moduli, part_device, partners, low_bound, high_bound):
    up_dev, low_dev = neighbour_devices(part_device, partners)
    samples, _, depth, rows_y, width = loads.shape
    loads = jnp.transpose(loads, (0, 1, 3, 2, 4))
    modal_disp = jnp.transpose(modal_disp, (0, 1, 3, 2, 4))
    ids = lax.optimization_barrier(jnp.transpose(material.astype(jnp.float32), (1, 0, 2)))
    modulus = lookup_modulus(ids, moduli)
    plane = (samples, 3, rows_y, width)
    plane_size = samples * 3 * rows_y * width
    mod_size = rows_y * width

    def pack(md_rows, load_rows):
        parts = [modal_disp[:, :, :, r].reshape(-1) for r in md_rows]
        parts += [loads[:, :, :, r].reshape(-1) for r in load_rows]
        parts += [modulus[:, r].reshape(-1) for r in md_rows]
        flat = jnp.concatenate(parts)
        return flat.reshape(flat.shape[0] // width, width)

    first = pack((0, 1, 2), (0, 1))
    last = pack((depth - 3, depth - 2, depth - 1), (depth - 2, depth - 1))
    below, above = exchange(first, last, up_dev, low_dev)
    below = below.reshape(-1)
    above = above.reshape(-1)

    def planes_of(got, count, start, size, shape):
        return [got[start + i * size : start + (i + 1) * size].reshape(shape) for i in range(count)]

    md_below = planes_of(below, 3, 0, plane_size, plane)
    md_above = planes_of(above, 3, 0, plane_size, plane)
    ld_below = planes_of(below, 2, 3 * plane_size, plane_size, plane)
    ld_above = planes_of(above, 2, 3 * plane_size, plane_size, plane)
    mod_below = planes_of(below, 3, 5 * plane_size, mod_size, (rows_y, width))
    mod_above = planes_of(above, 3, 5 * plane_size, mod_size, (rows_y, width))

    def extend(own, lower, upper, axis):
        zero = jnp.zeros_like(lower[0])
        rows = [zero] * (8 - len(lower)) + list(lower)
        tail = list(upper) + [zero] * (8 - len(upper))
        return jnp.concatenate(
            [jnp.stack(rows, axis=axis), own, jnp.stack(tail, axis=axis)], axis=axis
        )

    mine = jnp.arange(up_dev.shape[0], dtype=jnp.int32) == col_grp_index()
    low_on = jnp.sum(jnp.where(mine, low_dev, 0)) != col_grp_index()
    up_on = jnp.sum(jnp.where(mine, up_dev, 0)) != col_grp_index()
    zero_mod = jnp.zeros((rows_y, width), jnp.float32)
    zero_plane = jnp.zeros(plane, jnp.float32)

    theta = (high_bound[0] + low_bound[0]) / 2.0
    half = (high_bound[0] - low_bound[0]) / 2.0
    sigma = theta / half
    rho0 = 1.0 / sigma
    rho1 = 1.0 / (2.0 * sigma - rho0)

    scalars = jnp.stack([theta, rho1 * rho0, 2.0 * rho1 / half]).astype(jnp.float32)

    def chain(md, ld, mod, masks):
        return run_chain(scalars, masks, md, ld, mod)

    disp_local, res_local = chain(modal_disp, loads, modulus, jnp.ones((2, depth, width), jnp.float32))

    edge_rows = 8
    head = slice(0, edge_rows)
    tail = slice(depth - edge_rows, depth)

    def window(own, lower, upper, axis):
        zero = jnp.zeros_like(lower[0])
        rows = [zero] * (8 - len(lower)) + list(lower)
        after = list(upper) + [zero] * (8 - len(upper))
        index = [slice(None)] * own.ndim
        index[axis] = head
        own_head = own[tuple(index)]
        index[axis] = tail
        own_tail = own[tuple(index)]
        return jnp.concatenate(
            [jnp.stack(rows, axis=axis), own_head, own_tail, jnp.stack(after, axis=axis)], axis=axis
        )

    md_win = window(modal_disp, md_below, md_above, 3)
    ld_win = window(loads, ld_below, ld_above, 3)
    mod_win = window(modulus, mod_below, mod_above, 1)
    logical = jnp.concatenate(
        [
            jnp.arange(-8, edge_rows, dtype=jnp.int32),
            jnp.arange(depth - edge_rows, depth + 8, dtype=jnp.int32),
        ]
    )

    def valid(reach):
        keep = (logical >= 0) & (logical < depth)
        keep = keep | (low_on & (logical >= -reach) & (logical < 0))
        keep = keep | (up_on & (logical >= depth) & (logical < depth + reach))
        return jnp.broadcast_to(keep.astype(jnp.float32)[:, None], (logical.shape[0], width))

    masks = jnp.stack([valid(2), valid(1)], axis=0)
    disp_win, res_win = chain(md_win, ld_win, mod_win, masks)

    reach = 3
    sub_row = lax.broadcasted_iota(jnp.int32, (8, 1), 0)

    def merge(local, win):
        top = jnp.where(sub_row < reach, win[:, :, :, 8:16], local[:, :, :, 0:8])
        bottom = jnp.where(sub_row >= 8 - reach, win[:, :, :, 16:24], local[:, :, :, depth - 8 : depth])
        return jnp.concatenate([top, local[:, :, :, 8 : depth - 8], bottom], axis=3)

    displacement = merge(disp_local, disp_win)
    residual = merge(res_local, res_win)
    return (
        jnp.transpose(displacement, (0, 1, 3, 2, 4)),
        jnp.transpose(residual, (0, 1, 3, 2, 4)),
    )


def col_grp_index():
    return lax.axis_index("col") * GROUP + lax.axis_index("grp")


def solution(mesh):
    devices = mesh.devices.reshape(-1)
    grid = Mesh(devices.reshape(devices.size // GROUP, GROUP), ("col", "grp"))
    slab = ("col", "grp")
    in_specs = (
        P(None, None, slab, None, None),
        P(None, None, slab, None, None),
        P(slab, None, None),
        P(),
        P(),
        P(),
        P(),
        P(),
    )
    out_specs = (P(None, None, slab, None, None), P(None, None, slab, None, None))
    return jax.shard_map(
        on_device, mesh=grid, in_specs=in_specs, out_specs=out_specs, check_vma=False
    )
```

```python
import jax
import jax.numpy as jnp
from jax import lax
from jax.experimental import pallas as pl
from jax.experimental.pallas import tpu as pltpu
from jax.sharding import Mesh, PartitionSpec as P

MATERIALS = 8
GROUP = 8

GAMMA = 0.2
BETA = 0.5
EDGE_WEIGHTS = (0.0, 1.0, 0.5, 0.25)
OFFSETS = [
    (a, b, c) for a in (-1, 0, 1) for b in (-1, 0, 1) for c in (-1, 0, 1) if (a, b, c) != (0, 0, 0)
]


def shift_cells(array, axis, step):
    if step == 0:
        return array
    length = array.shape[axis]
    zero = jnp.zeros_like(lax.slice_in_dim(array, 0, 1, axis=axis))
    if step > 0:
        return jnp.concatenate([lax.slice_in_dim(array, 1, length, axis=axis), zero], axis=axis)
    return jnp.concatenate([zero, lax.slice_in_dim(array, 0, length - 1, axis=axis)], axis=axis)


def mod_neighbour(mod_ext, off_x, off_y, off_z, depth):
    rows = lax.slice_in_dim(mod_ext, 1 + off_x, 1 + off_x + depth, axis=1)
    return shift_cells(shift_cells(rows, 0, off_y), 2, off_z)


def edges_of(mod_ext, depth):
    centre = mod_neighbour(mod_ext, 0, 0, 0, depth)
    edges = []
    for offset in OFFSETS:
        norm_sq = offset[0] * offset[0] + offset[1] * offset[1] + offset[2] * offset[2]
        edges.append(
            EDGE_WEIGHTS[norm_sq]
            * 0.5
            * (centre + mod_neighbour(mod_ext, offset[0], offset[1], offset[2], depth))
        )
    return centre, edges


def diagonal_of(centre, edges):
    comps = [GAMMA * centre, GAMMA * centre, GAMMA * centre]
    for offset, edge in zip(OFFSETS, edges):
        norm_sq = offset[0] * offset[0] + offset[1] * offset[1] + offset[2] * offset[2]
        for comp in range(3):
            comps[comp] = comps[comp] + edge * (1.0 + BETA * offset[comp] * offset[comp] / norm_sq)
    return jnp.stack(comps, axis=0)


def edges_body(mod_ref, edge_ref, centre_ref, diag_ref):
    rows_y, depth, width = mod_ref.shape
    chunks = depth // 8
    sub = lax.broadcasted_iota(jnp.int32, (8, width), 0)
    lane = lax.broadcasted_iota(jnp.int32, (8, width), 1)
    zero = jnp.zeros((8, width), jnp.float32)

    def body(it, carry):
        r = pl.multiple_of(it * 8, 8)
        centre = [mod_ref[y, pl.ds(r, 8), :] for y in range(rows_y)]
        prev = [
            jnp.where(it == 0, zero, mod_ref[y, pl.ds(jnp.maximum(r - 8, 0), 8), :])
            for y in range(rows_y)
        ]
        nxt = [
            jnp.where(it == chunks - 1, zero, mod_ref[y, pl.ds(jnp.minimum(r + 8, depth - 8), 8), :])
            for y in range(rows_y)
        ]
        comps = [[GAMMA * centre[y] for y in range(rows_y)] for c in range(3)]
        index = 0
        for off_x in (-1, 0, 1):
            if off_x == 0:
                shifted_x = centre
            elif off_x < 0:
                shifted_x = [
                    jnp.where(sub == 0, pltpu.roll(prev[y], 1, 0), pltpu.roll(centre[y], 1, 0))
                    for y in range(rows_y)
                ]
            else:
                shifted_x = [
                    jnp.where(sub == 7, pltpu.roll(nxt[y], 7, 0), pltpu.roll(centre[y], 7, 0))
                    for y in range(rows_y)
                ]
            shifted = {0: shifted_x}
            shifted[-1] = [jnp.where(lane == 0, jnp.float32(0.0), pltpu.roll(v, 1, 1)) for v in shifted_x]
            shifted[1] = [
                jnp.where(lane == width - 1, jnp.float32(0.0), pltpu.roll(v, width - 1, 1))
                for v in shifted_x
            ]
            for off_y in (-1, 0, 1):
                for off_z in (-1, 0, 1):
                    if (off_x, off_y, off_z) == (0, 0, 0):
                        continue
                    offset = (off_x, off_y, off_z)
                    norm_sq = off_x * off_x + off_y * off_y + off_z * off_z
                    for y in range(rows_y):
                        source = y + off_y
                        if 0 <= source < rows_y:
                            other = shifted[off_z][source]
                        else:
                            other = zero
                        edge = EDGE_WEIGHTS[norm_sq] * 0.5 * (centre[y] + other)
                        edge_ref[index, y, pl.ds(r, 8), :] = edge
                        for c in range(3):
                            comps[c][y] = comps[c][y] + edge * (
                                1.0 + BETA * offset[c] * offset[c] / norm_sq
                            )
                    index += 1
        for y in range(rows_y):
            centre_ref[y, pl.ds(r, 8), :] = centre[y]
            for c in range(3):
                diag_ref[c, y, pl.ds(r, 8), :] = comps[c][y]
        return carry

    lax.fori_loop(0, chunks, body, 0)


def stencil_body(field_ref, edge_ref, cm_ref, out_ref):
    samples, _, rows_y, depth, width = field_ref.shape
    chunks = depth // 8
    sub = lax.broadcasted_iota(jnp.int32, (8, width), 0)
    lane = lax.broadcasted_iota(jnp.int32, (8, width), 1)
    zero = jnp.zeros((8, width), jnp.float32)

    def body(it, carry):
        s = it // chunks
        part = it % chunks
        r = pl.multiple_of(part * 8, 8)

        def rows(c, y, off):
            if off == 0:
                return field_ref[s, c, y, pl.ds(r, 8), :]
            if off < 0:
                return jnp.where(
                    part == 0, zero, field_ref[s, c, y, pl.ds(jnp.maximum(r - 8, 0), 8), :]
                )
            return jnp.where(
                part == chunks - 1,
                zero,
                field_ref[s, c, y, pl.ds(jnp.minimum(r + 8, depth - 8), 8), :],
            )

        centre = [[rows(c, y, 0) for y in range(rows_y)] for c in range(3)]
        acc = [
            [GAMMA * cm_ref[y, pl.ds(r, 8), :] * centre[c][y] for y in range(rows_y)]
            for c in range(3)
        ]
        index = 0
        for off_x in (-1, 0, 1):
            if off_x == 0:
                shifted_x = centre
            elif off_x < 0:
                shifted_x = [
                    [
                        jnp.where(
                            sub == 0,
                            pltpu.roll(rows(c, y, -1), 1, 0),
                            pltpu.roll(centre[c][y], 1, 0),
                        )
                        for y in range(rows_y)
                    ]
                    for c in range(3)
                ]
            else:
                shifted_x = [
                    [
                        jnp.where(
                            sub == 7,
                            pltpu.roll(rows(c, y, 1), 7, 0),
                            pltpu.roll(centre[c][y], 7, 0),
                        )
                        for y in range(rows_y)
                    ]
                    for c in range(3)
                ]
            shifted = {0: shifted_x}
            shifted[-1] = [
                [jnp.where(lane == 0, jnp.float32(0.0), pltpu.roll(v, 1, 1)) for v in per_c]
                for per_c in shifted_x
            ]
            shifted[1] = [
                [
                    jnp.where(lane == width - 1, jnp.float32(0.0), pltpu.roll(v, width - 1, 1))
                    for v in per_c
                ]
                for per_c in shifted_x
            ]
            for off_y in (-1, 0, 1):
                for off_z in (-1, 0, 1):
                    if (off_x, off_y, off_z) == (0, 0, 0):
                        continue
                    offset = (off_x, off_y, off_z)
                    norm_sq = off_x * off_x + off_y * off_y + off_z * off_z
                    for y in range(rows_y):
                        edge = edge_ref[index, y, pl.ds(r, 8), :]
                        source = y + off_y
                        if 0 <= source < rows_y:
                            delta = [centre[c][y] - shifted[off_z][c][source] for c in range(3)]
                        else:
                            delta = [centre[c][y] for c in range(3)]
                        project = None
                        for c in range(3):
                            if offset[c] > 0:
                                project = delta[c] if project is None else project + delta[c]
                            elif offset[c] < 0:
                                project = -delta[c] if project is None else project - delta[c]
                        if norm_sq == 2:
                            project = project * 0.5
                        elif norm_sq == 3:
                            project = project * (1.0 / 3.0)
                        for c in range(3):
                            if offset[c] != 0:
                                acc[c][y] = acc[c][y] + edge * (delta[c] + BETA * offset[c] * project)
                            else:
                                acc[c][y] = acc[c][y] + edge * delta[c]
                    index += 1
        for c in range(3):
            for y in range(rows_y):
                out_ref[s, c, y, pl.ds(r, 8), :] = acc[c][y]
        return carry

    lax.fori_loop(0, samples * chunks, body, 0)


def chain_kernel(
    scal_ref, mask_ref, md_ref, ld_ref, mod_ref, disp_ref, res_ref,
    edge_s, cm_s, jac_s, k_s, a_s, step0_s, step1_s,
):
    samples, _, rows_y, depth, width = md_ref.shape
    theta = scal_ref[0]
    c1 = scal_ref[1]
    c2 = scal_ref[2]
    edges_body(mod_ref, edge_s, cm_s, jac_s)
    stencil_body(md_ref, edge_s, cm_s, k_s)
    keep0 = mask_ref[0] > 0.0
    keep1 = mask_ref[1] > 0.0

    def first(it, carry):
        s = it // 3
        c = it % 3
        for y in range(rows_y):
            start = ld_ref[s, c, y] - k_s[s, c, y]
            a_s[s, c, y] = start
            step0_s[s, c, y] = jnp.where(keep0, start / (theta * jac_s[c, y]), jnp.float32(0.0))
        return carry

    lax.fori_loop(0, samples * 3, first, 0)
    stencil_body(step0_s, edge_s, cm_s, k_s)

    def second(it, carry):
        s = it // 3
        c = it % 3
        for y in range(rows_y):
            residual1 = a_s[s, c, y] - k_s[s, c, y]
            a_s[s, c, y] = residual1
            step0 = step0_s[s, c, y]
            step1 = jnp.where(
                keep1, c1 * step0 + c2 * residual1 / jac_s[c, y], jnp.float32(0.0)
            )
            step1_s[s, c, y] = step1
            disp_ref[s, c, y] = md_ref[s, c, y] + step0 + step1
        return carry

    lax.fori_loop(0, samples * 3, second, 0)
    stencil_body(step1_s, edge_s, cm_s, k_s)

    def third(it, carry):
        s = it // 3
        c = it % 3
        for y in range(rows_y):
            res_ref[s, c, y] = a_s[s, c, y] - k_s[s, c, y]
        return carry

    lax.fori_loop(0, samples * 3, third, 0)


def run_chain(scalars, masks, md, ld, mod):
    samples, _, rows_y, depth, width = md.shape
    vmem = pl.BlockSpec(memory_space=pltpu.VMEM)
    smem = pl.BlockSpec(memory_space=pltpu.SMEM)
    field = jax.ShapeDtypeStruct(md.shape, jnp.float32)
    size = md.size
    return pl.pallas_call(
        chain_kernel,
        out_shape=(field, field),
        in_specs=[smem, vmem, vmem, vmem, vmem],
        out_specs=(vmem, vmem),
        scratch_shapes=[
            pltpu.VMEM((len(OFFSETS), rows_y, depth, width), jnp.float32),
            pltpu.VMEM((rows_y, depth, width), jnp.float32),
            pltpu.VMEM((3, rows_y, depth, width), jnp.float32),
        ]
        + [pltpu.VMEM(md.shape, jnp.float32)] * 4,
        compiler_params=pltpu.CompilerParams(vmem_limit_bytes=48 * 1024 * 1024),
        cost_estimate=pl.CostEstimate(
            flops=3 * 26 * 20 * size, bytes_accessed=4 * 5 * size, transcendentals=0
        ),
    )(scalars, masks, md, ld, mod)


def lookup_modulus(material, moduli):
    modulus = jnp.zeros(material.shape, jnp.float32)
    for index in range(MATERIALS):
        modulus = modulus + jnp.where(material == float(index), moduli[index], jnp.float32(0.0))
    return modulus


def neighbour_devices(part_device, partners):
    count = part_device.shape[0]
    ids = jnp.arange(count, dtype=jnp.int32)
    hit = part_device[None, :] == ids[:, None]
    place = jnp.sum(jnp.where(hit, ids[None, :], 0), axis=1)
    upper = place % 2 == 0
    up_dev = jnp.where(upper, partners[0], partners[1])
    low_dev = jnp.where(upper, partners[1], partners[0])
    return up_dev, low_dev


def exchange(first, last, up_dev, low_dev):
    col = lax.axis_index("col")
    grp = lax.axis_index("grp")
    me = col * GROUP + grp
    cols = up_dev.shape[0] // GROUP
    rows = first.shape[0]
    pack = jnp.concatenate([first, last], axis=0)[None]
    held = lax.all_gather(pack, "col", axis=0, tiled=True)
    pick = (jnp.arange(cols, dtype=jnp.int32) == col)[:, None]
    t_up = jnp.sum(jnp.where(pick, up_dev.reshape(cols, GROUP), 0), axis=0)
    t_low = jnp.sum(jnp.where(pick, low_dev.reshape(cols, GROUP), 0), axis=0)
    up_at = jnp.where(t_up % GROUP == grp, t_up // GROUP, -1)[:, None, None]
    low_at = jnp.where(t_low % GROUP == grp, t_low // GROUP, -1)[:, None, None]
    from_up = jnp.zeros((GROUP,) + first.shape, jnp.float32)
    from_low = jnp.zeros((GROUP,) + first.shape, jnp.float32)
    for k in range(cols):
        from_up = jnp.where(up_at == k, held[k, :rows][None], from_up)
        from_low = jnp.where(low_at == k, held[k, rows:][None], from_low)
    slots = jnp.concatenate([from_up, from_low], axis=1)
    got = lax.all_to_all(slots, "grp", 0, 0, tiled=True)
    mine = jnp.arange(up_dev.shape[0], dtype=jnp.int32) == me
    my_up = jnp.sum(jnp.where(mine, up_dev, 0))
    my_low = jnp.sum(jnp.where(mine, low_dev, 0))
    above = jnp.zeros(first.shape, jnp.float32)
    below = jnp.zeros(first.shape, jnp.float32)
    for k in range(GROUP):
        above = jnp.where((my_up % GROUP == k) & (my_up != me), got[k, :rows], above)
        below = jnp.where((my_low % GROUP == k) & (my_low != me), got[k, rows:], below)
    return below, above


def on_device(loads, modal_disp, material, moduli, part_device, partners, low_bound, high_bound):
    up_dev, low_dev = neighbour_devices(part_device, partners)
    samples, _, depth, rows_y, width = loads.shape
    loads = jnp.transpose(loads, (0, 1, 3, 2, 4))
    modal_disp = jnp.transpose(modal_disp, (0, 1, 3, 2, 4))
    ids = lax.optimization_barrier(jnp.transpose(material.astype(jnp.float32), (1, 0, 2)))
    modulus = lookup_modulus(ids, moduli)
    plane = (samples, 3, rows_y, width)
    plane_size = samples * 3 * rows_y * width
    mod_size = rows_y * width

    def pack(md_rows, load_rows):
        parts = [modal_disp[:, :, :, r].reshape(-1) for r in md_rows]
        parts += [loads[:, :, :, r].reshape(-1) for r in load_rows]
        parts += [modulus[:, r].reshape(-1) for r in md_rows]
        flat = jnp.concatenate(parts)
        return flat.reshape(flat.shape[0] // width, width)

    first = pack((0, 1, 2), (0, 1))
    last = pack((depth - 3, depth - 2, depth - 1), (depth - 2, depth - 1))
    below, above = exchange(first, last, up_dev, low_dev)
    below = below.reshape(-1)
    above = above.reshape(-1)

    def planes_of(got, count, start, size, shape):
        return [got[start + i * size : start + (i + 1) * size].reshape(shape) for i in range(count)]

    md_below = planes_of(below, 3, 0, plane_size, plane)
    md_above = planes_of(above, 3, 0, plane_size, plane)
    ld_below = planes_of(below, 2, 3 * plane_size, plane_size, plane)
    ld_above = planes_of(above, 2, 3 * plane_size, plane_size, plane)
    mod_below = planes_of(below, 3, 5 * plane_size, mod_size, (rows_y, width))
    mod_above = planes_of(above, 3, 5 * plane_size, mod_size, (rows_y, width))

    def extend(own, lower, upper, axis):
        zero = jnp.zeros_like(lower[0])
        rows = [zero] * (8 - len(lower)) + list(lower)
        tail = list(upper) + [zero] * (8 - len(upper))
        return jnp.concatenate(
            [jnp.stack(rows, axis=axis), own, jnp.stack(tail, axis=axis)], axis=axis
        )

    mine = jnp.arange(up_dev.shape[0], dtype=jnp.int32) == col_grp_index()
    low_on = jnp.sum(jnp.where(mine, low_dev, 0)) != col_grp_index()
    up_on = jnp.sum(jnp.where(mine, up_dev, 0)) != col_grp_index()
    zero_mod = jnp.zeros((rows_y, width), jnp.float32)
    zero_plane = jnp.zeros(plane, jnp.float32)

    theta = (high_bound[0] + low_bound[0]) / 2.0
    half = (high_bound[0] - low_bound[0]) / 2.0
    sigma = theta / half
    rho0 = 1.0 / sigma
    rho1 = 1.0 / (2.0 * sigma - rho0)

    scalars = jnp.stack([theta, rho1 * rho0, 2.0 * rho1 / half]).astype(jnp.float32)

    def chain(md, ld, mod, masks):
        return run_chain(scalars, masks, md, ld, mod)

    disp_local, res_local = chain(modal_disp, loads, modulus, jnp.ones((2, depth, width), jnp.float32))

    edge_rows = 8
    head = slice(0, edge_rows)
    tail = slice(depth - edge_rows, depth)

    def window(own, lower, upper, axis):
        zero = jnp.zeros_like(lower[0])
        rows = [zero] * (8 - len(lower)) + list(lower)
        after = list(upper) + [zero] * (8 - len(upper))
        index = [slice(None)] * own.ndim
        index[axis] = head
        own_head = own[tuple(index)]
        index[axis] = tail
        own_tail = own[tuple(index)]
        return jnp.concatenate(
            [jnp.stack(rows, axis=axis), own_head, own_tail, jnp.stack(after, axis=axis)], axis=axis
        )

    md_win = window(modal_disp, md_below, md_above, 3)
    ld_win = window(loads, ld_below, ld_above, 3)
    mod_win = window(modulus, mod_below, mod_above, 1)
    logical = jnp.concatenate(
        [
            jnp.arange(-8, edge_rows, dtype=jnp.int32),
            jnp.arange(depth - edge_rows, depth + 8, dtype=jnp.int32),
        ]
    )

    def valid(reach):
        keep = (logical >= 0) & (logical < depth)
        keep = keep | (low_on & (logical >= -reach) & (logical < 0))
        keep = keep | (up_on & (logical >= depth) & (logical < depth + reach))
        return jnp.broadcast_to(keep.astype(jnp.float32)[:, None], (logical.shape[0], width))

    masks = jnp.stack([valid(2), valid(1)], axis=0)
    disp_win, res_win = chain(md_win, ld_win, mod_win, masks)

    reach = 3
    sub_row = lax.broadcasted_iota(jnp.int32, (8, 1), 0)

    def merge(local, win):
        top = jnp.where(sub_row < reach, win[:, :, :, 8:16], local[:, :, :, 0:8])
        bottom = jnp.where(sub_row >= 8 - reach, win[:, :, :, 16:24], local[:, :, :, depth - 8 : depth])
        return jnp.concatenate([top, local[:, :, :, 8 : depth - 8], bottom], axis=3)

    displacement = merge(disp_local, disp_win)
    residual = merge(res_local, res_win)
    return (
        jnp.transpose(displacement, (0, 1, 3, 2, 4)),
        jnp.transpose(residual, (0, 1, 3, 2, 4)),
    )


def col_grp_index():
    return lax.axis_index("col") * GROUP + lax.axis_index("grp")


def solution(mesh):
    devices = mesh.devices.reshape(-1)
    grid = Mesh(devices.reshape(devices.size // GROUP, GROUP), ("col", "grp"))
    slab = ("col", "grp")
    in_specs = (
        P(None, None, slab, None, None),
        P(None, None, slab, None, None),
        P(slab, None, None),
        P(),
        P(),
        P(),
        P(),
        P(),
    )
    out_specs = (P(None, None, slab, None, None), P(None, None, slab, None, None))
    return jax.shard_map(
        on_device, mesh=grid, in_specs=in_specs, out_specs=out_specs, check_vma=False
    )
```

```python
import jax
import jax.numpy as jnp
from jax import lax
from jax.experimental import pallas as pl
from jax.experimental.pallas import tpu as pltpu
from jax.sharding import Mesh, PartitionSpec as P

MATERIALS = 8
GROUP = 8

GAMMA = 0.2
BETA = 0.5
EDGE_WEIGHTS = (0.0, 1.0, 0.5, 0.25)
OFFSETS = [
    (a, b, c) for a in (-1, 0, 1) for b in (-1, 0, 1) for c in (-1, 0, 1) if (a, b, c) != (0, 0, 0)
]


def shift_cells(array, axis, step):
    if step == 0:
        return array
    length = array.shape[axis]
    zero = jnp.zeros_like(lax.slice_in_dim(array, 0, 1, axis=axis))
    if step > 0:
        return jnp.concatenate([lax.slice_in_dim(array, 1, length, axis=axis), zero], axis=axis)
    return jnp.concatenate([zero, lax.slice_in_dim(array, 0, length - 1, axis=axis)], axis=axis)


def mod_neighbour(mod_ext, off_x, off_y, off_z, depth):
    rows = lax.slice_in_dim(mod_ext, 1 + off_x, 1 + off_x + depth, axis=1)
    return shift_cells(shift_cells(rows, 0, off_y), 2, off_z)


def edges_of(mod_ext, depth):
    centre = mod_neighbour(mod_ext, 0, 0, 0, depth)
    edges = []
    for offset in OFFSETS:
        norm_sq = offset[0] * offset[0] + offset[1] * offset[1] + offset[2] * offset[2]
        edges.append(
            EDGE_WEIGHTS[norm_sq]
            * 0.5
            * (centre + mod_neighbour(mod_ext, offset[0], offset[1], offset[2], depth))
        )
    return centre, edges


def diagonal_of(centre, edges):
    comps = [GAMMA * centre, GAMMA * centre, GAMMA * centre]
    for offset, edge in zip(OFFSETS, edges):
        norm_sq = offset[0] * offset[0] + offset[1] * offset[1] + offset[2] * offset[2]
        for comp in range(3):
            comps[comp] = comps[comp] + edge * (1.0 + BETA * offset[comp] * offset[comp] / norm_sq)
    return jnp.stack(comps, axis=0)


def edges_body(mod_ref, edge_ref, centre_ref, diag_ref):
    rows_y, depth, width = mod_ref.shape
    chunks = depth // 8
    sub = lax.broadcasted_iota(jnp.int32, (8, width), 0)
    lane = lax.broadcasted_iota(jnp.int32, (8, width), 1)
    zero = jnp.zeros((8, width), jnp.float32)

    def body(it, carry):
        r = pl.multiple_of(it * 8, 8)
        centre = [mod_ref[y, pl.ds(r, 8), :] for y in range(rows_y)]
        prev = [
            jnp.where(it == 0, zero, mod_ref[y, pl.ds(jnp.maximum(r - 8, 0), 8), :])
            for y in range(rows_y)
        ]
        nxt = [
            jnp.where(it == chunks - 1, zero, mod_ref[y, pl.ds(jnp.minimum(r + 8, depth - 8), 8), :])
            for y in range(rows_y)
        ]
        comps = [[GAMMA * centre[y] for y in range(rows_y)] for c in range(3)]
        index = 0
        for off_x in (-1, 0, 1):
            if off_x == 0:
                shifted_x = centre
            elif off_x < 0:
                shifted_x = [
                    jnp.where(sub == 0, pltpu.roll(prev[y], 1, 0), pltpu.roll(centre[y], 1, 0))
                    for y in range(rows_y)
                ]
            else:
                shifted_x = [
                    jnp.where(sub == 7, pltpu.roll(nxt[y], 7, 0), pltpu.roll(centre[y], 7, 0))
                    for y in range(rows_y)
                ]
            shifted = {0: shifted_x}
            shifted[-1] = [jnp.where(lane == 0, jnp.float32(0.0), pltpu.roll(v, 1, 1)) for v in shifted_x]
            shifted[1] = [
                jnp.where(lane == width - 1, jnp.float32(0.0), pltpu.roll(v, width - 1, 1))
                for v in shifted_x
            ]
            for off_y in (-1, 0, 1):
                for off_z in (-1, 0, 1):
                    if (off_x, off_y, off_z) == (0, 0, 0):
                        continue
                    offset = (off_x, off_y, off_z)
                    norm_sq = off_x * off_x + off_y * off_y + off_z * off_z
                    for y in range(rows_y):
                        source = y + off_y
                        if 0 <= source < rows_y:
                            other = shifted[off_z][source]
                        else:
                            other = zero
                        edge = EDGE_WEIGHTS[norm_sq] * 0.5 * (centre[y] + other)
                        edge_ref[index, y, pl.ds(r, 8), :] = edge
                        for c in range(3):
                            comps[c][y] = comps[c][y] + edge * (
                                1.0 + BETA * offset[c] * offset[c] / norm_sq
                            )
                    index += 1
        for y in range(rows_y):
            centre_ref[y, pl.ds(r, 8), :] = centre[y]
            for c in range(3):
                diag_ref[c, y, pl.ds(r, 8), :] = comps[c][y]
        return carry

    lax.fori_loop(0, chunks, body, 0)


def stencil_body(field_ref, edge_ref, cm_ref, out_ref):
    samples, _, rows_y, depth, width = field_ref.shape
    chunks = depth // 8
    sub = lax.broadcasted_iota(jnp.int32, (8, width), 0)
    lane = lax.broadcasted_iota(jnp.int32, (8, width), 1)
    zero = jnp.zeros((8, width), jnp.float32)

    def body(it, carry):
        s = it // chunks
        part = it % chunks
        r = pl.multiple_of(part * 8, 8)

        def rows(c, y, off):
            if off == 0:
                return field_ref[s, c, y, pl.ds(r, 8), :]
            if off < 0:
                return jnp.where(
                    part == 0, zero, field_ref[s, c, y, pl.ds(jnp.maximum(r - 8, 0), 8), :]
                )
            return jnp.where(
                part == chunks - 1,
                zero,
                field_ref[s, c, y, pl.ds(jnp.minimum(r + 8, depth - 8), 8), :],
            )

        centre = [[rows(c, y, 0) for y in range(rows_y)] for c in range(3)]
        acc = [
            [GAMMA * cm_ref[y, pl.ds(r, 8), :] * centre[c][y] for y in range(rows_y)]
            for c in range(3)
        ]
        index = 0
        for off_x in (-1, 0, 1):
            if off_x == 0:
                shifted_x = centre
            elif off_x < 0:
                shifted_x = [
                    [
                        jnp.where(
                            sub == 0,
                            pltpu.roll(rows(c, y, -1), 1, 0),
                            pltpu.roll(centre[c][y], 1, 0),
                        )
                        for y in range(rows_y)
                    ]
                    for c in range(3)
                ]
            else:
                shifted_x = [
                    [
                        jnp.where(
                            sub == 7,
                            pltpu.roll(rows(c, y, 1), 7, 0),
                            pltpu.roll(centre[c][y], 7, 0),
                        )
                        for y in range(rows_y)
                    ]
                    for c in range(3)
                ]
            shifted = {0: shifted_x}
            shifted[-1] = [
                [jnp.where(lane == 0, jnp.float32(0.0), pltpu.roll(v, 1, 1)) for v in per_c]
                for per_c in shifted_x
            ]
            shifted[1] = [
                [
                    jnp.where(lane == width - 1, jnp.float32(0.0), pltpu.roll(v, width - 1, 1))
                    for v in per_c
                ]
                for per_c in shifted_x
            ]
            for off_y in (-1, 0, 1):
                for off_z in (-1, 0, 1):
                    if (off_x, off_y, off_z) == (0, 0, 0):
                        continue
                    offset = (off_x, off_y, off_z)
                    norm_sq = off_x * off_x + off_y * off_y + off_z * off_z
                    for y in range(rows_y):
                        edge = edge_ref[index, y, pl.ds(r, 8), :]
                        source = y + off_y
                        if 0 <= source < rows_y:
                            delta = [centre[c][y] - shifted[off_z][c][source] for c in range(3)]
                        else:
                            delta = [centre[c][y] for c in range(3)]
                        project = None
                        for c in range(3):
                            if offset[c] > 0:
                                project = delta[c] if project is None else project + delta[c]
                            elif offset[c] < 0:
                                project = -delta[c] if project is None else project - delta[c]
                        if norm_sq == 2:
                            project = project * 0.5
                        elif norm_sq == 3:
                            project = project * (1.0 / 3.0)
                        for c in range(3):
                            if offset[c] != 0:
                                acc[c][y] = acc[c][y] + edge * (delta[c] + BETA * offset[c] * project)
                            else:
                                acc[c][y] = acc[c][y] + edge * delta[c]
                    index += 1
        for c in range(3):
            for y in range(rows_y):
                out_ref[s, c, y, pl.ds(r, 8), :] = acc[c][y]
        return carry

    lax.fori_loop(0, samples * chunks, body, 0)


def chain_kernel(
    scal_ref, moduli_ref, mask_ref, md_ref, ld_ref, ids_ref, disp_ref, res_ref,
    mod_s, edge_s, cm_s, jac_s, k_s, a_s, step0_s, step1_s,
):
    samples, _, rows_y, depth, width = md_ref.shape
    theta = scal_ref[0]
    c1 = scal_ref[1]
    c2 = scal_ref[2]
    keep_mod = mask_ref[2] > 0.0
    for y in range(rows_y):
        ids = ids_ref[y]
        modulus = jnp.zeros(ids.shape, jnp.float32)
        for index in range(MATERIALS):
            modulus = modulus + jnp.where(ids == float(index), moduli_ref[index], jnp.float32(0.0))
        mod_s[y] = jnp.where(keep_mod, modulus, jnp.float32(0.0))
    edges_body(mod_s, edge_s, cm_s, jac_s)
    stencil_body(md_ref, edge_s, cm_s, k_s)
    keep0 = mask_ref[0] > 0.0
    keep1 = mask_ref[1] > 0.0

    def first(it, carry):
        s = it // 3
        c = it % 3
        for y in range(rows_y):
            start = ld_ref[s, c, y] - k_s[s, c, y]
            a_s[s, c, y] = start
            step0_s[s, c, y] = jnp.where(keep0, start / (theta * jac_s[c, y]), jnp.float32(0.0))
        return carry

    lax.fori_loop(0, samples * 3, first, 0)
    stencil_body(step0_s, edge_s, cm_s, k_s)

    def second(it, carry):
        s = it // 3
        c = it % 3
        for y in range(rows_y):
            residual1 = a_s[s, c, y] - k_s[s, c, y]
            a_s[s, c, y] = residual1
            step0 = step0_s[s, c, y]
            step1 = jnp.where(
                keep1, c1 * step0 + c2 * residual1 / jac_s[c, y], jnp.float32(0.0)
            )
            step1_s[s, c, y] = step1
            disp_ref[s, c, y] = md_ref[s, c, y] + step0 + step1
        return carry

    lax.fori_loop(0, samples * 3, second, 0)
    stencil_body(step1_s, edge_s, cm_s, k_s)

    def third(it, carry):
        s = it // 3
        c = it % 3
        for y in range(rows_y):
            res_ref[s, c, y] = a_s[s, c, y] - k_s[s, c, y]
        return carry

    lax.fori_loop(0, samples * 3, third, 0)


def run_chain(scalars, moduli, masks, md, ld, ids):
    samples, _, rows_y, depth, width = md.shape
    vmem = pl.BlockSpec(memory_space=pltpu.VMEM)
    smem = pl.BlockSpec(memory_space=pltpu.SMEM)
    field = jax.ShapeDtypeStruct(md.shape, jnp.float32)
    size = md.size
    return pl.pallas_call(
        chain_kernel,
        out_shape=(field, field),
        in_specs=[smem, smem, vmem, vmem, vmem, vmem],
        out_specs=(vmem, vmem),
        scratch_shapes=[
            pltpu.VMEM((rows_y, depth, width), jnp.float32),
            pltpu.VMEM((len(OFFSETS), rows_y, depth, width), jnp.float32),
            pltpu.VMEM((rows_y, depth, width), jnp.float32),
            pltpu.VMEM((3, rows_y, depth, width), jnp.float32),
        ]
        + [pltpu.VMEM(md.shape, jnp.float32)] * 4,
        compiler_params=pltpu.CompilerParams(vmem_limit_bytes=48 * 1024 * 1024),
        cost_estimate=pl.CostEstimate(
            flops=3 * 26 * 20 * size, bytes_accessed=4 * 5 * size, transcendentals=0
        ),
    )(scalars, moduli, masks, md, ld, ids)


def lookup_modulus(material, moduli):
    modulus = jnp.zeros(material.shape, jnp.float32)
    for index in range(MATERIALS):
        modulus = modulus + jnp.where(material == float(index), moduli[index], jnp.float32(0.0))
    return modulus


def neighbour_devices(part_device, partners):
    count = part_device.shape[0]
    ids = jnp.arange(count, dtype=jnp.int32)
    hit = part_device[None, :] == ids[:, None]
    place = jnp.sum(jnp.where(hit, ids[None, :], 0), axis=1)
    upper = place % 2 == 0
    up_dev = jnp.where(upper, partners[0], partners[1])
    low_dev = jnp.where(upper, partners[1], partners[0])
    return up_dev, low_dev


def exchange(first, last, up_dev, low_dev):
    col = lax.axis_index("col")
    grp = lax.axis_index("grp")
    me = col * GROUP + grp
    cols = up_dev.shape[0] // GROUP
    rows = first.shape[0]
    pack = jnp.concatenate([first, last], axis=0)[None]
    held = lax.all_gather(pack, "grp", axis=0, tiled=True)
    pick = (jnp.arange(GROUP, dtype=jnp.int32) == grp)[None, :]
    t_up = jnp.sum(jnp.where(pick, up_dev.reshape(cols, GROUP), 0), axis=1)
    t_low = jnp.sum(jnp.where(pick, low_dev.reshape(cols, GROUP), 0), axis=1)
    up_at = jnp.where(t_up // GROUP == col, t_up % GROUP, -1)[:, None]
    low_at = jnp.where(t_low // GROUP == col, t_low % GROUP, -1)[:, None]
    up_at = up_at[:, :, None]
    low_at = low_at[:, :, None]
    from_up = jnp.zeros((cols,) + first.shape, jnp.float32)
    from_low = jnp.zeros((cols,) + first.shape, jnp.float32)
    for k in range(GROUP):
        from_up = jnp.where(up_at == k, held[k, :rows][None], from_up)
        from_low = jnp.where(low_at == k, held[k, rows:][None], from_low)
    rows = first.shape[0]
    slots = jnp.concatenate([from_up, from_low], axis=1)
    got = lax.all_to_all(slots, "col", 0, 0, tiled=True)
    my_up = up_dev[me]
    my_low = low_dev[me]
    above = lax.dynamic_index_in_dim(got, my_up // GROUP, axis=0, keepdims=False)[:rows]
    below = lax.dynamic_index_in_dim(got, my_low // GROUP, axis=0, keepdims=False)[rows:]
    above = jnp.where(my_up != me, above, jnp.float32(0.0))
    below = jnp.where(my_low != me, below, jnp.float32(0.0))
    return below, above


def on_device(loads, modal_disp, material, moduli, part_device, partners, low_bound, high_bound):
    up_dev, low_dev = neighbour_devices(part_device, partners)
    samples, _, depth, rows_y, width = loads.shape
    ids_orig = material.astype(jnp.float32)
    plane = (samples, 3, rows_y, width)
    plane_size = samples * 3 * rows_y * width
    mod_size = rows_y * width

    def pack(md_rows, load_rows):
        parts = [modal_disp[:, :, r].reshape(-1) for r in md_rows]
        parts += [loads[:, :, r].reshape(-1) for r in load_rows]
        parts += [ids_orig[r].reshape(-1) for r in md_rows]
        flat = jnp.concatenate(parts)
        return flat.reshape(flat.shape[0] // width, width)

    first = pack((0, 1, 2), (0, 1))
    last = pack((depth - 3, depth - 2, depth - 1), (depth - 2, depth - 1))
    below, above = exchange(first, last, up_dev, low_dev)
    below = below.reshape(-1)
    above = above.reshape(-1)

    def planes_of(got, count, start, size, shape):
        return [got[start + i * size : start + (i + 1) * size].reshape(shape) for i in range(count)]

    md_below = planes_of(below, 3, 0, plane_size, plane)
    md_above = planes_of(above, 3, 0, plane_size, plane)
    ld_below = planes_of(below, 2, 3 * plane_size, plane_size, plane)
    ld_above = planes_of(above, 2, 3 * plane_size, plane_size, plane)
    ids_below = planes_of(below, 3, 5 * plane_size, mod_size, (rows_y, width))
    ids_above = planes_of(above, 3, 5 * plane_size, mod_size, (rows_y, width))

    loads = jnp.transpose(loads, (0, 1, 3, 2, 4))
    modal_disp = jnp.transpose(modal_disp, (0, 1, 3, 2, 4))
    ids = jnp.transpose(ids_orig, (1, 0, 2))

    mine = jnp.arange(up_dev.shape[0], dtype=jnp.int32) == col_grp_index()
    low_on = jnp.sum(jnp.where(mine, low_dev, 0)) != col_grp_index()
    up_on = jnp.sum(jnp.where(mine, up_dev, 0)) != col_grp_index()

    theta = (high_bound[0] + low_bound[0]) / 2.0
    half = (high_bound[0] - low_bound[0]) / 2.0
    sigma = theta / half
    rho0 = 1.0 / sigma
    rho1 = 1.0 / (2.0 * sigma - rho0)
    scalars = jnp.stack([theta, rho1 * rho0, 2.0 * rho1 / half]).astype(jnp.float32)

    def chain(md, ld, material_ids, masks):
        return run_chain(scalars, moduli, masks, md, ld, material_ids)

    disp_local, res_local = chain(modal_disp, loads, ids, jnp.ones((3, depth, width), jnp.float32))
    out_local = (
        jnp.transpose(disp_local, (0, 1, 3, 2, 4)),
        jnp.transpose(res_local, (0, 1, 3, 2, 4)),
    )

    edge_rows = 8
    head = slice(0, edge_rows)
    tail = slice(depth - edge_rows, depth)

    def window(own, lower, upper, axis):
        zero = jnp.zeros_like(lower[0])
        rows = [zero] * (8 - len(lower)) + list(lower)
        after = list(upper) + [zero] * (8 - len(upper))
        index = [slice(None)] * own.ndim
        index[axis] = head
        own_head = own[tuple(index)]
        index[axis] = tail
        own_tail = own[tuple(index)]
        return jnp.concatenate(
            [jnp.stack(rows, axis=axis), own_head, own_tail, jnp.stack(after, axis=axis)], axis=axis
        )

    md_win = window(modal_disp, md_below, md_above, 3)
    ld_win = window(loads, ld_below, ld_above, 3)
    ids_win = window(ids, ids_below, ids_above, 1)
    logical = jnp.concatenate(
        [
            jnp.arange(-8, edge_rows, dtype=jnp.int32),
            jnp.arange(depth - edge_rows, depth + 8, dtype=jnp.int32),
        ]
    )

    def valid(reach):
        keep = (logical >= 0) & (logical < depth)
        keep = keep | (low_on & (logical >= -reach) & (logical < 0))
        keep = keep | (up_on & (logical >= depth) & (logical < depth + reach))
        return jnp.broadcast_to(keep.astype(jnp.float32)[:, None], (logical.shape[0], width))

    masks = jnp.stack([valid(2), valid(1), valid(3)], axis=0)
    disp_win, res_win = chain(md_win, ld_win, ids_win, masks)

    reach = 3

    def patch(out, win):
        top = jnp.transpose(win[:, :, :, 8 : 8 + reach], (0, 1, 3, 2, 4))
        bottom = jnp.transpose(win[:, :, :, 8 + 2 * edge_rows - reach : 8 + 2 * edge_rows], (0, 1, 3, 2, 4))
        out = lax.dynamic_update_slice_in_dim(out, top, 0, axis=2)
        return lax.dynamic_update_slice_in_dim(out, bottom, depth - reach, axis=2)

    return (patch(out_local[0], disp_win), patch(out_local[1], res_win))


def col_grp_index():
    return lax.axis_index("col") * GROUP + lax.axis_index("grp")


def solution(mesh):
    devices = mesh.devices.reshape(-1)
    grid = Mesh(devices.reshape(devices.size // GROUP, GROUP), ("col", "grp"))
    slab = ("col", "grp")
    in_specs = (
        P(None, None, slab, None, None),
        P(None, None, slab, None, None),
        P(slab, None, None),
        P(),
        P(),
        P(),
        P(),
        P(),
    )
    out_specs = (P(None, None, slab, None, None), P(None, None, slab, None, None))
    return jax.shard_map(
        on_device, mesh=grid, in_specs=in_specs, out_specs=out_specs, check_vma=False
    )
```

```python
import jax
import jax.numpy as jnp
from jax import lax
from jax.experimental import pallas as pl
from jax.experimental.pallas import tpu as pltpu
from jax.sharding import Mesh, PartitionSpec as P

MATERIALS = 8
GROUP = 8

GAMMA = 0.2
BETA = 0.5
EDGE_WEIGHTS = (0.0, 1.0, 0.5, 0.25)
OFFSETS = [
    (a, b, c) for a in (-1, 0, 1) for b in (-1, 0, 1) for c in (-1, 0, 1) if (a, b, c) != (0, 0, 0)
]


def shift_cells(array, axis, step):
    if step == 0:
        return array
    length = array.shape[axis]
    zero = jnp.zeros_like(lax.slice_in_dim(array, 0, 1, axis=axis))
    if step > 0:
        return jnp.concatenate([lax.slice_in_dim(array, 1, length, axis=axis), zero], axis=axis)
    return jnp.concatenate([zero, lax.slice_in_dim(array, 0, length - 1, axis=axis)], axis=axis)


def mod_neighbour(mod_ext, off_x, off_y, off_z, depth):
    rows = lax.slice_in_dim(mod_ext, 1 + off_x, 1 + off_x + depth, axis=1)
    return shift_cells(shift_cells(rows, 0, off_y), 2, off_z)


def edges_of(mod_ext, depth):
    centre = mod_neighbour(mod_ext, 0, 0, 0, depth)
    edges = []
    for offset in OFFSETS:
        norm_sq = offset[0] * offset[0] + offset[1] * offset[1] + offset[2] * offset[2]
        edges.append(
            EDGE_WEIGHTS[norm_sq]
            * 0.5
            * (centre + mod_neighbour(mod_ext, offset[0], offset[1], offset[2], depth))
        )
    return centre, edges


def diagonal_of(centre, edges):
    comps = [GAMMA * centre, GAMMA * centre, GAMMA * centre]
    for offset, edge in zip(OFFSETS, edges):
        norm_sq = offset[0] * offset[0] + offset[1] * offset[1] + offset[2] * offset[2]
        for comp in range(3):
            comps[comp] = comps[comp] + edge * (1.0 + BETA * offset[comp] * offset[comp] / norm_sq)
    return jnp.stack(comps, axis=0)


def edges_body(mod_ref, edge_ref, centre_ref, diag_ref):
    rows_y, depth, width = mod_ref.shape
    chunks = depth // 8
    sub = lax.broadcasted_iota(jnp.int32, (8, width), 0)
    lane = lax.broadcasted_iota(jnp.int32, (8, width), 1)
    zero = jnp.zeros((8, width), jnp.float32)

    def body(it, carry):
        r = pl.multiple_of(it * 8, 8)
        centre = [mod_ref[y, pl.ds(r, 8), :] for y in range(rows_y)]
        prev = [
            jnp.where(it == 0, zero, mod_ref[y, pl.ds(jnp.maximum(r - 8, 0), 8), :])
            for y in range(rows_y)
        ]
        nxt = [
            jnp.where(it == chunks - 1, zero, mod_ref[y, pl.ds(jnp.minimum(r + 8, depth - 8), 8), :])
            for y in range(rows_y)
        ]
        comps = [[GAMMA * centre[y] for y in range(rows_y)] for c in range(3)]
        index = 0
        for off_x in (-1, 0, 1):
            if off_x == 0:
                shifted_x = centre
            elif off_x < 0:
                shifted_x = [
                    jnp.where(sub == 0, pltpu.roll(prev[y], 1, 0), pltpu.roll(centre[y], 1, 0))
                    for y in range(rows_y)
                ]
            else:
                shifted_x = [
                    jnp.where(sub == 7, pltpu.roll(nxt[y], 7, 0), pltpu.roll(centre[y], 7, 0))
                    for y in range(rows_y)
                ]
            shifted = {0: shifted_x}
            shifted[-1] = [jnp.where(lane == 0, jnp.float32(0.0), pltpu.roll(v, 1, 1)) for v in shifted_x]
            shifted[1] = [
                jnp.where(lane == width - 1, jnp.float32(0.0), pltpu.roll(v, width - 1, 1))
                for v in shifted_x
            ]
            for off_y in (-1, 0, 1):
                for off_z in (-1, 0, 1):
                    if (off_x, off_y, off_z) == (0, 0, 0):
                        continue
                    offset = (off_x, off_y, off_z)
                    norm_sq = off_x * off_x + off_y * off_y + off_z * off_z
                    for y in range(rows_y):
                        source = y + off_y
                        if 0 <= source < rows_y:
                            other = shifted[off_z][source]
                        else:
                            other = zero
                        edge = EDGE_WEIGHTS[norm_sq] * 0.5 * (centre[y] + other)
                        edge_ref[index, y, pl.ds(r, 8), :] = edge
                        for c in range(3):
                            comps[c][y] = comps[c][y] + edge * (
                                1.0 + BETA * offset[c] * offset[c] / norm_sq
                            )
                    index += 1
        for y in range(rows_y):
            centre_ref[y, pl.ds(r, 8), :] = centre[y]
            for c in range(3):
                diag_ref[c, y, pl.ds(r, 8), :] = comps[c][y]
        return carry

    lax.fori_loop(0, chunks, body, 0)


def stencil_body(field_ref, edge_ref, cm_ref, out_ref):
    samples, _, rows_y, depth, width = field_ref.shape
    chunks = depth // 8
    sub = lax.broadcasted_iota(jnp.int32, (8, width), 0)
    lane = lax.broadcasted_iota(jnp.int32, (8, width), 1)
    zero = jnp.zeros((8, width), jnp.float32)

    def body(it, carry):
        s = it // chunks
        part = it % chunks
        r = pl.multiple_of(part * 8, 8)

        def rows(c, y, off):
            if off == 0:
                return field_ref[s, c, y, pl.ds(r, 8), :]
            if off < 0:
                return jnp.where(
                    part == 0, zero, field_ref[s, c, y, pl.ds(jnp.maximum(r - 8, 0), 8), :]
                )
            return jnp.where(
                part == chunks - 1,
                zero,
                field_ref[s, c, y, pl.ds(jnp.minimum(r + 8, depth - 8), 8), :],
            )

        centre = [[rows(c, y, 0) for y in range(rows_y)] for c in range(3)]
        acc = [
            [GAMMA * cm_ref[y, pl.ds(r, 8), :] * centre[c][y] for y in range(rows_y)]
            for c in range(3)
        ]
        index = 0
        for off_x in (-1, 0, 1):
            if off_x == 0:
                shifted_x = centre
            elif off_x < 0:
                shifted_x = [
                    [
                        jnp.where(
                            sub == 0,
                            pltpu.roll(rows(c, y, -1), 1, 0),
                            pltpu.roll(centre[c][y], 1, 0),
                        )
                        for y in range(rows_y)
                    ]
                    for c in range(3)
                ]
            else:
                shifted_x = [
                    [
                        jnp.where(
                            sub == 7,
                            pltpu.roll(rows(c, y, 1), 7, 0),
                            pltpu.roll(centre[c][y], 7, 0),
                        )
                        for y in range(rows_y)
                    ]
                    for c in range(3)
                ]
            shifted = {0: shifted_x}
            shifted[-1] = [
                [jnp.where(lane == 0, jnp.float32(0.0), pltpu.roll(v, 1, 1)) for v in per_c]
                for per_c in shifted_x
            ]
            shifted[1] = [
                [
                    jnp.where(lane == width - 1, jnp.float32(0.0), pltpu.roll(v, width - 1, 1))
                    for v in per_c
                ]
                for per_c in shifted_x
            ]
            for off_y in (-1, 0, 1):
                for off_z in (-1, 0, 1):
                    if (off_x, off_y, off_z) == (0, 0, 0):
                        continue
                    offset = (off_x, off_y, off_z)
                    norm_sq = off_x * off_x + off_y * off_y + off_z * off_z
                    for y in range(rows_y):
                        edge = edge_ref[index, y, pl.ds(r, 8), :]
                        source = y + off_y
                        if 0 <= source < rows_y:
                            delta = [centre[c][y] - shifted[off_z][c][source] for c in range(3)]
                        else:
                            delta = [centre[c][y] for c in range(3)]
                        project = None
                        for c in range(3):
                            if offset[c] > 0:
                                project = delta[c] if project is None else project + delta[c]
                            elif offset[c] < 0:
                                project = -delta[c] if project is None else project - delta[c]
                        if norm_sq == 2:
                            project = project * 0.5
                        elif norm_sq == 3:
                            project = project * (1.0 / 3.0)
                        for c in range(3):
                            if offset[c] != 0:
                                acc[c][y] = acc[c][y] + edge * (delta[c] + BETA * offset[c] * project)
                            else:
                                acc[c][y] = acc[c][y] + edge * delta[c]
                    index += 1
        for c in range(3):
            for y in range(rows_y):
                out_ref[s, c, y, pl.ds(r, 8), :] = acc[c][y]
        return carry

    lax.fori_loop(0, samples * chunks, body, 0)


def chain_kernel(
    scal_ref, moduli_ref, mask_ref, md_ref, ld_ref, ids_ref, disp_ref, res_ref,
    mod_s, edge_s, cm_s, jac_s, k_s, a_s, step0_s, step1_s,
):
    samples, _, rows_y, depth, width = md_ref.shape
    theta = scal_ref[0]
    c1 = scal_ref[1]
    c2 = scal_ref[2]
    keep_mod = mask_ref[2] > 0.0
    for y in range(rows_y):
        ids = ids_ref[y]
        modulus = jnp.zeros(ids.shape, jnp.float32)
        for index in range(MATERIALS):
            modulus = modulus + jnp.where(ids == float(index), moduli_ref[index], jnp.float32(0.0))
        mod_s[y] = jnp.where(keep_mod, modulus, jnp.float32(0.0))
    edges_body(mod_s, edge_s, cm_s, jac_s)
    stencil_body(md_ref, edge_s, cm_s, k_s)
    keep0 = mask_ref[0] > 0.0
    keep1 = mask_ref[1] > 0.0

    def first(it, carry):
        s = it // 3
        c = it % 3
        for y in range(rows_y):
            start = ld_ref[s, c, y] - k_s[s, c, y]
            a_s[s, c, y] = start
            step0_s[s, c, y] = jnp.where(keep0, start / (theta * jac_s[c, y]), jnp.float32(0.0))
        return carry

    lax.fori_loop(0, samples * 3, first, 0)
    stencil_body(step0_s, edge_s, cm_s, k_s)

    def second(it, carry):
        s = it // 3
        c = it % 3
        for y in range(rows_y):
            residual1 = a_s[s, c, y] - k_s[s, c, y]
            a_s[s, c, y] = residual1
            step0 = step0_s[s, c, y]
            step1 = jnp.where(
                keep1, c1 * step0 + c2 * residual1 / jac_s[c, y], jnp.float32(0.0)
            )
            step1_s[s, c, y] = step1
            disp_ref[s, c, y] = md_ref[s, c, y] + step0 + step1
        return carry

    lax.fori_loop(0, samples * 3, second, 0)
    stencil_body(step1_s, edge_s, cm_s, k_s)

    def third(it, carry):
        s = it // 3
        c = it % 3
        for y in range(rows_y):
            res_ref[s, c, y] = a_s[s, c, y] - k_s[s, c, y]
        return carry

    lax.fori_loop(0, samples * 3, third, 0)


def run_chain(scalars, moduli, masks, md, ld, ids):
    samples, _, rows_y, depth, width = md.shape
    vmem = pl.BlockSpec(memory_space=pltpu.VMEM)
    smem = pl.BlockSpec(memory_space=pltpu.SMEM)
    field = jax.ShapeDtypeStruct(md.shape, jnp.float32)
    size = md.size
    return pl.pallas_call(
        chain_kernel,
        out_shape=(field, field),
        in_specs=[smem, smem, vmem, vmem, vmem, vmem],
        out_specs=(vmem, vmem),
        scratch_shapes=[
            pltpu.VMEM((rows_y, depth, width), jnp.float32),
            pltpu.VMEM((len(OFFSETS), rows_y, depth, width), jnp.float32),
            pltpu.VMEM((rows_y, depth, width), jnp.float32),
            pltpu.VMEM((3, rows_y, depth, width), jnp.float32),
        ]
        + [pltpu.VMEM(md.shape, jnp.float32)] * 4,
        compiler_params=pltpu.CompilerParams(vmem_limit_bytes=48 * 1024 * 1024),
        cost_estimate=pl.CostEstimate(
            flops=3 * 26 * 20 * size, bytes_accessed=4 * 5 * size, transcendentals=0
        ),
    )(scalars, moduli, masks, md, ld, ids)


def lookup_modulus(material, moduli):
    modulus = jnp.zeros(material.shape, jnp.float32)
    for index in range(MATERIALS):
        modulus = modulus + jnp.where(material == float(index), moduli[index], jnp.float32(0.0))
    return modulus


def neighbour_devices(part_device, partners):
    count = part_device.shape[0]
    ids = jnp.arange(count, dtype=jnp.int32)
    hit = part_device[None, :] == ids[:, None]
    place = jnp.sum(jnp.where(hit, ids[None, :], 0), axis=1)
    upper = place % 2 == 0
    up_dev = jnp.where(upper, partners[0], partners[1])
    low_dev = jnp.where(upper, partners[1], partners[0])
    return up_dev, low_dev


def exchange(first, last, up_dev, low_dev):
    col = lax.axis_index("col")
    grp = lax.axis_index("grp")
    me = col * GROUP + grp
    cols = up_dev.shape[0] // GROUP
    rows = first.shape[0]
    pack = jnp.concatenate([first, last], axis=0)[None]
    held = lax.all_gather(pack, "grp", axis=0, tiled=True)
    pick = (jnp.arange(GROUP, dtype=jnp.int32) == grp)[None, :]
    t_up = jnp.sum(jnp.where(pick, up_dev.reshape(cols, GROUP), 0), axis=1)
    t_low = jnp.sum(jnp.where(pick, low_dev.reshape(cols, GROUP), 0), axis=1)
    up_at = jnp.where(t_up // GROUP == col, t_up % GROUP, -1)[:, None, None]
    low_at = jnp.where(t_low // GROUP == col, t_low % GROUP, -1)[:, None, None]
    row = lax.broadcasted_iota(jnp.int32, (1, 2 * rows, 1), 1)
    source = jnp.where(row < rows, up_at, low_at)
    slots = jnp.zeros((cols, 2 * rows) + first.shape[1:], jnp.float32)
    for k in range(GROUP):
        slots = jnp.where(source == k, held[k][None], slots)
    got = lax.all_to_all(slots, "col", 0, 0, tiled=True)
    my_up = up_dev[me]
    my_low = low_dev[me]
    above = lax.dynamic_index_in_dim(got, my_up // GROUP, axis=0, keepdims=False)[:rows]
    below = lax.dynamic_index_in_dim(got, my_low // GROUP, axis=0, keepdims=False)[rows:]
    above = jnp.where(my_up != me, above, jnp.float32(0.0))
    below = jnp.where(my_low != me, below, jnp.float32(0.0))
    return below, above


def on_device(loads, modal_disp, material, moduli, part_device, partners, low_bound, high_bound):
    up_dev, low_dev = neighbour_devices(part_device, partners)
    samples, _, depth, rows_y, width = loads.shape
    ids_orig = material.astype(jnp.float32)
    plane = (samples, 3, rows_y, width)
    plane_size = samples * 3 * rows_y * width
    mod_size = rows_y * width

    def pack(md_rows, load_rows):
        parts = [modal_disp[:, :, r].reshape(-1) for r in md_rows]
        parts += [loads[:, :, r].reshape(-1) for r in load_rows]
        parts += [ids_orig[r].reshape(-1) for r in md_rows]
        flat = jnp.concatenate(parts)
        return flat.reshape(flat.shape[0] // width, width)

    first = pack((0, 1, 2), (0, 1))
    last = pack((depth - 3, depth - 2, depth - 1), (depth - 2, depth - 1))
    below, above = exchange(first, last, up_dev, low_dev)
    below = below.reshape(-1)
    above = above.reshape(-1)

    def planes_of(got, count, start, size, shape):
        return [got[start + i * size : start + (i + 1) * size].reshape(shape) for i in range(count)]

    md_below = planes_of(below, 3, 0, plane_size, plane)
    md_above = planes_of(above, 3, 0, plane_size, plane)
    ld_below = planes_of(below, 2, 3 * plane_size, plane_size, plane)
    ld_above = planes_of(above, 2, 3 * plane_size, plane_size, plane)
    ids_below = planes_of(below, 3, 5 * plane_size, mod_size, (rows_y, width))
    ids_above = planes_of(above, 3, 5 * plane_size, mod_size, (rows_y, width))

    loads = jnp.transpose(loads, (0, 1, 3, 2, 4))
    modal_disp = jnp.transpose(modal_disp, (0, 1, 3, 2, 4))
    ids = jnp.transpose(ids_orig, (1, 0, 2))

    mine = jnp.arange(up_dev.shape[0], dtype=jnp.int32) == col_grp_index()
    low_on = jnp.sum(jnp.where(mine, low_dev, 0)) != col_grp_index()
    up_on = jnp.sum(jnp.where(mine, up_dev, 0)) != col_grp_index()

    theta = (high_bound[0] + low_bound[0]) / 2.0
    half = (high_bound[0] - low_bound[0]) / 2.0
    sigma = theta / half
    rho0 = 1.0 / sigma
    rho1 = 1.0 / (2.0 * sigma - rho0)
    scalars = jnp.stack([theta, rho1 * rho0, 2.0 * rho1 / half]).astype(jnp.float32)

    def chain(md, ld, material_ids, masks):
        return run_chain(scalars, moduli, masks, md, ld, material_ids)

    disp_local, res_local = chain(modal_disp, loads, ids, jnp.ones((3, depth, width), jnp.float32))
    out_local = (
        jnp.transpose(disp_local, (0, 1, 3, 2, 4)),
        jnp.transpose(res_local, (0, 1, 3, 2, 4)),
    )

    reach = 3
    margin = 2 * reach
    pad_rows = (-(2 * reach + 2 * margin)) % 8

    def window(own, lower, upper, axis):
        index = [slice(None)] * own.ndim
        index[axis] = slice(0, margin)
        own_head = own[tuple(index)]
        index[axis] = slice(depth - margin, depth)
        own_tail = own[tuple(index)]
        zero_shape = list(own.shape)
        zero_shape[axis] = pad_rows
        return jnp.concatenate(
            [
                jnp.stack(list(lower), axis=axis),
                own_head,
                own_tail,
                jnp.stack(list(upper), axis=axis),
                jnp.zeros(zero_shape, jnp.float32),
            ],
            axis=axis,
        )

    md_win = window(modal_disp, md_below, md_above, 3)
    ld_zero = jnp.zeros(plane, jnp.float32)
    ld_win = window(loads, [ld_zero] + ld_below, ld_above + [ld_zero], 3)
    ids_win = window(ids, ids_below, ids_above, 1)
    logical = jnp.concatenate(
        [
            jnp.arange(-reach, margin, dtype=jnp.int32),
            jnp.arange(depth - margin, depth + reach, dtype=jnp.int32),
            jnp.full((pad_rows,), depth + 8, dtype=jnp.int32),
        ]
    )

    def valid(reach):
        keep = (logical >= 0) & (logical < depth)
        keep = keep | (low_on & (logical >= -reach) & (logical < 0))
        keep = keep | (up_on & (logical >= depth) & (logical < depth + reach))
        return jnp.broadcast_to(keep.astype(jnp.float32)[:, None], (logical.shape[0], width))

    masks = jnp.stack([valid(2), valid(1), valid(3)], axis=0)
    disp_win, res_win = chain(md_win, ld_win, ids_win, masks)

    def patch(out, win):
        top = jnp.transpose(win[:, :, :, reach : 2 * reach], (0, 1, 3, 2, 4))
        bottom = jnp.transpose(win[:, :, :, reach + 2 * margin - reach : reach + 2 * margin], (0, 1, 3, 2, 4))
        out = lax.dynamic_update_slice_in_dim(out, top, 0, axis=2)
        return lax.dynamic_update_slice_in_dim(out, bottom, depth - reach, axis=2)

    return (patch(out_local[0], disp_win), patch(out_local[1], res_win))


def col_grp_index():
    return lax.axis_index("col") * GROUP + lax.axis_index("grp")


def solution(mesh):
    devices = mesh.devices.reshape(-1)
    grid = Mesh(devices.reshape(devices.size // GROUP, GROUP), ("col", "grp"))
    slab = ("col", "grp")
    in_specs = (
        P(None, None, slab, None, None),
        P(None, None, slab, None, None),
        P(slab, None, None),
        P(),
        P(),
        P(),
        P(),
        P(),
    )
    out_specs = (P(None, None, slab, None, None), P(None, None, slab, None, None))
    return jax.shard_map(
        on_device, mesh=grid, in_specs=in_specs, out_specs=out_specs, check_vma=False
    )
```

```python
import jax
import jax.numpy as jnp
from jax import lax
from jax.experimental import pallas as pl
from jax.experimental.pallas import tpu as pltpu
from jax.sharding import Mesh, PartitionSpec as P

MATERIALS = 8
GROUP = 8

GAMMA = 0.2
BETA = 0.5
EDGE_WEIGHTS = (0.0, 1.0, 0.5, 0.25)
OFFSETS = [
    (a, b, c) for a in (-1, 0, 1) for b in (-1, 0, 1) for c in (-1, 0, 1) if (a, b, c) != (0, 0, 0)
]


def shift_cells(array, axis, step):
    if step == 0:
        return array
    length = array.shape[axis]
    zero = jnp.zeros_like(lax.slice_in_dim(array, 0, 1, axis=axis))
    if step > 0:
        return jnp.concatenate([lax.slice_in_dim(array, 1, length, axis=axis), zero], axis=axis)
    return jnp.concatenate([zero, lax.slice_in_dim(array, 0, length - 1, axis=axis)], axis=axis)


def mod_neighbour(mod_ext, off_x, off_y, off_z, depth):
    rows = lax.slice_in_dim(mod_ext, 1 + off_x, 1 + off_x + depth, axis=1)
    return shift_cells(shift_cells(rows, 0, off_y), 2, off_z)


def edges_of(mod_ext, depth):
    centre = mod_neighbour(mod_ext, 0, 0, 0, depth)
    edges = []
    for offset in OFFSETS:
        norm_sq = offset[0] * offset[0] + offset[1] * offset[1] + offset[2] * offset[2]
        edges.append(
            EDGE_WEIGHTS[norm_sq]
            * 0.5
            * (centre + mod_neighbour(mod_ext, offset[0], offset[1], offset[2], depth))
        )
    return centre, edges


def diagonal_of(centre, edges):
    comps = [GAMMA * centre, GAMMA * centre, GAMMA * centre]
    for offset, edge in zip(OFFSETS, edges):
        norm_sq = offset[0] * offset[0] + offset[1] * offset[1] + offset[2] * offset[2]
        for comp in range(3):
            comps[comp] = comps[comp] + edge * (1.0 + BETA * offset[comp] * offset[comp] / norm_sq)
    return jnp.stack(comps, axis=0)


def edges_body(mod_ref, edge_ref, centre_ref, diag_ref):
    rows_y, depth, width = mod_ref.shape
    chunks = depth // 8
    sub = lax.broadcasted_iota(jnp.int32, (8, width), 0)
    lane = lax.broadcasted_iota(jnp.int32, (8, width), 1)
    zero = jnp.zeros((8, width), jnp.float32)

    def body(it, carry):
        r = pl.multiple_of(it * 8, 8)
        centre = [mod_ref[y, pl.ds(r, 8), :] for y in range(rows_y)]
        prev = [
            jnp.where(it == 0, zero, mod_ref[y, pl.ds(jnp.maximum(r - 8, 0), 8), :])
            for y in range(rows_y)
        ]
        nxt = [
            jnp.where(it == chunks - 1, zero, mod_ref[y, pl.ds(jnp.minimum(r + 8, depth - 8), 8), :])
            for y in range(rows_y)
        ]
        comps = [[GAMMA * centre[y] for y in range(rows_y)] for c in range(3)]
        index = 0
        for off_x in (-1, 0, 1):
            if off_x == 0:
                shifted_x = centre
            elif off_x < 0:
                shifted_x = [
                    jnp.where(sub == 0, pltpu.roll(prev[y], 1, 0), pltpu.roll(centre[y], 1, 0))
                    for y in range(rows_y)
                ]
            else:
                shifted_x = [
                    jnp.where(sub == 7, pltpu.roll(nxt[y], 7, 0), pltpu.roll(centre[y], 7, 0))
                    for y in range(rows_y)
                ]
            shifted = {0: shifted_x}
            shifted[-1] = [jnp.where(lane == 0, jnp.float32(0.0), pltpu.roll(v, 1, 1)) for v in shifted_x]
            shifted[1] = [
                jnp.where(lane == width - 1, jnp.float32(0.0), pltpu.roll(v, width - 1, 1))
                for v in shifted_x
            ]
            for off_y in (-1, 0, 1):
                for off_z in (-1, 0, 1):
                    if (off_x, off_y, off_z) == (0, 0, 0):
                        continue
                    offset = (off_x, off_y, off_z)
                    norm_sq = off_x * off_x + off_y * off_y + off_z * off_z
                    for y in range(rows_y):
                        source = y + off_y
                        if 0 <= source < rows_y:
                            other = shifted[off_z][source]
                        else:
                            other = zero
                        edge = EDGE_WEIGHTS[norm_sq] * 0.5 * (centre[y] + other)
                        edge_ref[index, y, pl.ds(r, 8), :] = edge
                        for c in range(3):
                            comps[c][y] = comps[c][y] + edge * (
                                1.0 + BETA * offset[c] * offset[c] / norm_sq
                            )
                    index += 1
        for y in range(rows_y):
            centre_ref[y, pl.ds(r, 8), :] = centre[y]
            for c in range(3):
                diag_ref[c, y, pl.ds(r, 8), :] = comps[c][y]
        return carry

    lax.fori_loop(0, chunks, body, 0)


def stencil_body(field_ref, edge_ref, cm_ref, out_ref):
    samples, _, rows_y, depth, width = field_ref.shape
    chunks = depth // 8
    sub = lax.broadcasted_iota(jnp.int32, (8, width), 0)
    lane = lax.broadcasted_iota(jnp.int32, (8, width), 1)
    zero = jnp.zeros((8, width), jnp.float32)

    def body(it, carry):
        s = it // chunks
        part = it % chunks
        r = pl.multiple_of(part * 8, 8)

        def rows(c, y, off):
            if off == 0:
                return field_ref[s, c, y, pl.ds(r, 8), :]
            if off < 0:
                return jnp.where(
                    part == 0, zero, field_ref[s, c, y, pl.ds(jnp.maximum(r - 8, 0), 8), :]
                )
            return jnp.where(
                part == chunks - 1,
                zero,
                field_ref[s, c, y, pl.ds(jnp.minimum(r + 8, depth - 8), 8), :],
            )

        centre = [[rows(c, y, 0) for y in range(rows_y)] for c in range(3)]
        acc = [
            [GAMMA * cm_ref[y, pl.ds(r, 8), :] * centre[c][y] for y in range(rows_y)]
            for c in range(3)
        ]
        index = 0
        for off_x in (-1, 0, 1):
            if off_x == 0:
                shifted_x = centre
            elif off_x < 0:
                shifted_x = [
                    [
                        jnp.where(
                            sub == 0,
                            pltpu.roll(rows(c, y, -1), 1, 0),
                            pltpu.roll(centre[c][y], 1, 0),
                        )
                        for y in range(rows_y)
                    ]
                    for c in range(3)
                ]
            else:
                shifted_x = [
                    [
                        jnp.where(
                            sub == 7,
                            pltpu.roll(rows(c, y, 1), 7, 0),
                            pltpu.roll(centre[c][y], 7, 0),
                        )
                        for y in range(rows_y)
                    ]
                    for c in range(3)
                ]
            shifted = {0: shifted_x}
            shifted[-1] = [
                [jnp.where(lane == 0, jnp.float32(0.0), pltpu.roll(v, 1, 1)) for v in per_c]
                for per_c in shifted_x
            ]
            shifted[1] = [
                [
                    jnp.where(lane == width - 1, jnp.float32(0.0), pltpu.roll(v, width - 1, 1))
                    for v in per_c
                ]
                for per_c in shifted_x
            ]
            for off_y in (-1, 0, 1):
                for off_z in (-1, 0, 1):
                    if (off_x, off_y, off_z) == (0, 0, 0):
                        continue
                    offset = (off_x, off_y, off_z)
                    norm_sq = off_x * off_x + off_y * off_y + off_z * off_z
                    for y in range(rows_y):
                        edge = edge_ref[index, y, pl.ds(r, 8), :]
                        source = y + off_y
                        if 0 <= source < rows_y:
                            delta = [centre[c][y] - shifted[off_z][c][source] for c in range(3)]
                        else:
                            delta = [centre[c][y] for c in range(3)]
                        project = None
                        for c in range(3):
                            if offset[c] > 0:
                                project = delta[c] if project is None else project + delta[c]
                            elif offset[c] < 0:
                                project = -delta[c] if project is None else project - delta[c]
                        if norm_sq == 2:
                            project = project * 0.5
                        elif norm_sq == 3:
                            project = project * (1.0 / 3.0)
                        for c in range(3):
                            if offset[c] != 0:
                                acc[c][y] = acc[c][y] + edge * (delta[c] + BETA * offset[c] * project)
                            else:
                                acc[c][y] = acc[c][y] + edge * delta[c]
                    index += 1
        for c in range(3):
            for y in range(rows_y):
                out_ref[s, c, y, pl.ds(r, 8), :] = acc[c][y]
        return carry

    lax.fori_loop(0, samples * chunks, body, 0)


def chain_kernel(
    scal_ref, moduli_ref, mask_ref, md_ref, ld_ref, ids_ref, disp_ref, res_ref,
    mod_s, edge_s, cm_s, jac_s, k_s, a_s, step0_s, step1_s,
):
    samples, _, rows_y, depth, width = md_ref.shape
    theta = scal_ref[0]
    c1 = scal_ref[1]
    c2 = scal_ref[2]
    keep_mod = mask_ref[2] > 0.0
    for y in range(rows_y):
        ids = ids_ref[y]
        modulus = jnp.zeros(ids.shape, jnp.float32)
        for index in range(MATERIALS):
            modulus = modulus + jnp.where(ids == float(index), moduli_ref[index], jnp.float32(0.0))
        mod_s[y] = jnp.where(keep_mod, modulus, jnp.float32(0.0))
    edges_body(mod_s, edge_s, cm_s, jac_s)
    stencil_body(md_ref, edge_s, cm_s, k_s)
    keep0 = mask_ref[0] > 0.0
    keep1 = mask_ref[1] > 0.0

    def first(it, carry):
        s = it // 3
        c = it % 3
        for y in range(rows_y):
            start = ld_ref[s, c, y] - k_s[s, c, y]
            a_s[s, c, y] = start
            step0_s[s, c, y] = jnp.where(keep0, start / (theta * jac_s[c, y]), jnp.float32(0.0))
        return carry

    lax.fori_loop(0, samples * 3, first, 0)
    stencil_body(step0_s, edge_s, cm_s, k_s)

    def second(it, carry):
        s = it // 3
        c = it % 3
        for y in range(rows_y):
            residual1 = a_s[s, c, y] - k_s[s, c, y]
            a_s[s, c, y] = residual1
            step0 = step0_s[s, c, y]
            step1 = jnp.where(
                keep1, c1 * step0 + c2 * residual1 / jac_s[c, y], jnp.float32(0.0)
            )
            step1_s[s, c, y] = step1
            disp_ref[s, c, y] = md_ref[s, c, y] + step0 + step1
        return carry

    lax.fori_loop(0, samples * 3, second, 0)
    stencil_body(step1_s, edge_s, cm_s, k_s)

    def third(it, carry):
        s = it // 3
        c = it % 3
        for y in range(rows_y):
            res_ref[s, c, y] = a_s[s, c, y] - k_s[s, c, y]
        return carry

    lax.fori_loop(0, samples * 3, third, 0)


def run_chain(scalars, moduli, masks, md, ld, ids):
    samples, _, rows_y, depth, width = md.shape
    vmem = pl.BlockSpec(memory_space=pltpu.VMEM)
    smem = pl.BlockSpec(memory_space=pltpu.SMEM)
    field = jax.ShapeDtypeStruct(md.shape, jnp.float32)
    size = md.size
    return pl.pallas_call(
        chain_kernel,
        out_shape=(field, field),
        in_specs=[smem, smem, vmem, vmem, vmem, vmem],
        out_specs=(vmem, vmem),
        scratch_shapes=[
            pltpu.VMEM((rows_y, depth, width), jnp.float32),
            pltpu.VMEM((len(OFFSETS), rows_y, depth, width), jnp.float32),
            pltpu.VMEM((rows_y, depth, width), jnp.float32),
            pltpu.VMEM((3, rows_y, depth, width), jnp.float32),
        ]
        + [pltpu.VMEM(md.shape, jnp.float32)] * 4,
        compiler_params=pltpu.CompilerParams(vmem_limit_bytes=48 * 1024 * 1024),
        cost_estimate=pl.CostEstimate(
            flops=3 * 26 * 20 * size, bytes_accessed=4 * 5 * size, transcendentals=0
        ),
    )(scalars, moduli, masks, md, ld, ids)


def lookup_modulus(material, moduli):
    modulus = jnp.zeros(material.shape, jnp.float32)
    for index in range(MATERIALS):
        modulus = modulus + jnp.where(material == float(index), moduli[index], jnp.float32(0.0))
    return modulus


def neighbour_devices(part_device, partners):
    count = part_device.shape[0]
    ids = jnp.arange(count, dtype=jnp.int32)
    hit = part_device[None, :] == ids[:, None]
    place = jnp.sum(jnp.where(hit, ids[None, :], 0), axis=1)
    upper = place % 2 == 0
    up_dev = jnp.where(upper, partners[0], partners[1])
    low_dev = jnp.where(upper, partners[1], partners[0])
    return up_dev, low_dev


def exchange(first, last, up_dev, low_dev):
    col = lax.axis_index("col")
    grp = lax.axis_index("grp")
    me = col * GROUP + grp
    cols = up_dev.shape[0] // GROUP
    rows = first.shape[0]
    pack = jnp.concatenate([first, last], axis=0)[None]
    held = lax.all_gather(pack, "grp", axis=0, tiled=True)
    pick = (jnp.arange(GROUP, dtype=jnp.int32) == grp)[None, :]
    t_up = jnp.sum(jnp.where(pick, up_dev.reshape(cols, GROUP), 0), axis=1)
    t_low = jnp.sum(jnp.where(pick, low_dev.reshape(cols, GROUP), 0), axis=1)
    up_at = jnp.where(t_up // GROUP == col, t_up % GROUP, -1)[:, None, None]
    low_at = jnp.where(t_low // GROUP == col, t_low % GROUP, -1)[:, None, None]
    from_up = jnp.zeros((cols,) + first.shape, jnp.float32)
    from_low = jnp.zeros((cols,) + first.shape, jnp.float32)
    for k in range(GROUP):
        from_up = jnp.where(up_at == k, held[k, :rows][None], from_up)
        from_low = jnp.where(low_at == k, held[k, rows:][None], from_low)
    slots = jnp.concatenate([from_up, from_low], axis=1)
    got = lax.all_to_all(slots, "col", 0, 0, tiled=True)
    my_up = up_dev[me]
    my_low = low_dev[me]
    above = lax.dynamic_index_in_dim(got, my_up // GROUP, axis=0, keepdims=False)[:rows]
    below = lax.dynamic_index_in_dim(got, my_low // GROUP, axis=0, keepdims=False)[rows:]
    above = jnp.where(my_up != me, above, jnp.float32(0.0))
    below = jnp.where(my_low != me, below, jnp.float32(0.0))
    return below, above


def on_device(loads, modal_disp, material, moduli, part_device, partners, low_bound, high_bound):
    up_dev, low_dev = neighbour_devices(part_device, partners)
    samples, _, depth, rows_y, width = loads.shape
    ids_orig = material.astype(jnp.float32)
    plane = (samples, 3, rows_y, width)
    plane_size = samples * 3 * rows_y * width
    mod_size = rows_y * width

    def pack(md_rows, load_rows):
        parts = [modal_disp[:, :, r].reshape(-1) for r in md_rows]
        parts += [loads[:, :, r].reshape(-1) for r in load_rows]
        parts += [ids_orig[r].reshape(-1) for r in md_rows]
        flat = jnp.concatenate(parts)
        return flat.reshape(flat.shape[0] // width, width)

    first = pack((0, 1, 2), (0, 1))
    last = pack((depth - 3, depth - 2, depth - 1), (depth - 2, depth - 1))
    below, above = exchange(first, last, up_dev, low_dev)
    below = below.reshape(-1)
    above = above.reshape(-1)

    def planes_of(got, count, start, size, shape):
        return [got[start + i * size : start + (i + 1) * size].reshape(shape) for i in range(count)]

    md_below = planes_of(below, 3, 0, plane_size, plane)
    md_above = planes_of(above, 3, 0, plane_size, plane)
    ld_below = planes_of(below, 2, 3 * plane_size, plane_size, plane)
    ld_above = planes_of(above, 2, 3 * plane_size, plane_size, plane)
    ids_below = planes_of(below, 3, 5 * plane_size, mod_size, (rows_y, width))
    ids_above = planes_of(above, 3, 5 * plane_size, mod_size, (rows_y, width))

    loads = jnp.transpose(loads, (0, 1, 3, 2, 4))
    modal_disp = jnp.transpose(modal_disp, (0, 1, 3, 2, 4))
    ids = jnp.transpose(ids_orig, (1, 0, 2))

    mine = jnp.arange(up_dev.shape[0], dtype=jnp.int32) == col_grp_index()
    low_on = jnp.sum(jnp.where(mine, low_dev, 0)) != col_grp_index()
    up_on = jnp.sum(jnp.where(mine, up_dev, 0)) != col_grp_index()

    theta = (high_bound[0] + low_bound[0]) / 2.0
    half = (high_bound[0] - low_bound[0]) / 2.0
    sigma = theta / half
    rho0 = 1.0 / sigma
    rho1 = 1.0 / (2.0 * sigma - rho0)
    scalars = jnp.stack([theta, rho1 * rho0, 2.0 * rho1 / half]).astype(jnp.float32)

    def chain(md, ld, material_ids, masks):
        return run_chain(scalars, moduli, masks, md, ld, material_ids)

    disp_local, res_local = chain(modal_disp, loads, ids, jnp.ones((3, depth, width), jnp.float32))
    out_local = (
        jnp.transpose(disp_local, (0, 1, 3, 2, 4)),
        jnp.transpose(res_local, (0, 1, 3, 2, 4)),
    )

    reach = 3
    margin = 2 * reach
    pad_rows = (-(2 * reach + 2 * margin)) % 8

    def window(own, lower, upper, axis):
        index = [slice(None)] * own.ndim
        index[axis] = slice(0, margin)
        own_head = own[tuple(index)]
        index[axis] = slice(depth - margin, depth)
        own_tail = own[tuple(index)]
        zero_shape = list(own.shape)
        zero_shape[axis] = pad_rows
        return jnp.concatenate(
            [
                jnp.stack(list(lower), axis=axis),
                own_head,
                own_tail,
                jnp.stack(list(upper), axis=axis),
                jnp.zeros(zero_shape, jnp.float32),
            ],
            axis=axis,
        )

    md_win = window(modal_disp, md_below, md_above, 3)
    ld_zero = jnp.zeros(plane, jnp.float32)
    ld_win = window(loads, [ld_zero] + ld_below, ld_above + [ld_zero], 3)
    ids_win = window(ids, ids_below, ids_above, 1)
    logical = jnp.concatenate(
        [
            jnp.arange(-reach, margin, dtype=jnp.int32),
            jnp.arange(depth - margin, depth + reach, dtype=jnp.int32),
            jnp.full((pad_rows,), depth + 8, dtype=jnp.int32),
        ]
    )

    def valid(reach):
        keep = (logical >= 0) & (logical < depth)
        keep = keep | (low_on & (logical >= -reach) & (logical < 0))
        keep = keep | (up_on & (logical >= depth) & (logical < depth + reach))
        return jnp.broadcast_to(keep.astype(jnp.float32)[:, None], (logical.shape[0], width))

    masks = jnp.stack([valid(2), valid(1), valid(3)], axis=0)
    disp_win, res_win = chain(md_win, ld_win, ids_win, masks)

    def patch(out, win):
        top = jnp.transpose(win[:, :, :, reach : 2 * reach], (0, 1, 3, 2, 4))
        bottom = jnp.transpose(win[:, :, :, reach + 2 * margin - reach : reach + 2 * margin], (0, 1, 3, 2, 4))
        out = lax.dynamic_update_slice_in_dim(out, top, 0, axis=2)
        return lax.dynamic_update_slice_in_dim(out, bottom, depth - reach, axis=2)

    return (patch(out_local[0], disp_win), patch(out_local[1], res_win))


def col_grp_index():
    return lax.axis_index("col") * GROUP + lax.axis_index("grp")


def solution(mesh):
    devices = mesh.devices.reshape(-1)
    grid = Mesh(devices.reshape(devices.size // GROUP, GROUP), ("col", "grp"))
    slab = ("col", "grp")
    in_specs = (
        P(None, None, slab, None, None),
        P(None, None, slab, None, None),
        P(slab, None, None),
        P(),
        P(),
        P(),
        P(),
        P(),
    )
    out_specs = (P(None, None, slab, None, None), P(None, None, slab, None, None))
    return jax.shard_map(
        on_device, mesh=grid, in_specs=in_specs, out_specs=out_specs, check_vma=False
    )
```

```python
import jax
import jax.numpy as jnp
from jax import lax
from jax.experimental import pallas as pl
from jax.experimental.pallas import tpu as pltpu
from jax.sharding import Mesh, PartitionSpec as P

MATERIALS = 8
GROUP = 8

GAMMA = 0.2
BETA = 0.5
EDGE_WEIGHTS = (0.0, 1.0, 0.5, 0.25)
OFFSETS = [
    (a, b, c) for a in (-1, 0, 1) for b in (-1, 0, 1) for c in (-1, 0, 1) if (a, b, c) != (0, 0, 0)
]


def shift_cells(array, axis, step):
    if step == 0:
        return array
    length = array.shape[axis]
    zero = jnp.zeros_like(lax.slice_in_dim(array, 0, 1, axis=axis))
    if step > 0:
        return jnp.concatenate([lax.slice_in_dim(array, 1, length, axis=axis), zero], axis=axis)
    return jnp.concatenate([zero, lax.slice_in_dim(array, 0, length - 1, axis=axis)], axis=axis)


def mod_neighbour(mod_ext, off_x, off_y, off_z, depth):
    rows = lax.slice_in_dim(mod_ext, 1 + off_x, 1 + off_x + depth, axis=1)
    return shift_cells(shift_cells(rows, 0, off_y), 2, off_z)


def edges_of(mod_ext, depth):
    centre = mod_neighbour(mod_ext, 0, 0, 0, depth)
    edges = []
    for offset in OFFSETS:
        norm_sq = offset[0] * offset[0] + offset[1] * offset[1] + offset[2] * offset[2]
        edges.append(
            EDGE_WEIGHTS[norm_sq]
            * 0.5
            * (centre + mod_neighbour(mod_ext, offset[0], offset[1], offset[2], depth))
        )
    return centre, edges


def diagonal_of(centre, edges):
    comps = [GAMMA * centre, GAMMA * centre, GAMMA * centre]
    for offset, edge in zip(OFFSETS, edges):
        norm_sq = offset[0] * offset[0] + offset[1] * offset[1] + offset[2] * offset[2]
        for comp in range(3):
            comps[comp] = comps[comp] + edge * (1.0 + BETA * offset[comp] * offset[comp] / norm_sq)
    return jnp.stack(comps, axis=0)


def edges_body(mod_ref, edge_ref, centre_ref, diag_ref):
    rows_y, depth, width = mod_ref.shape
    chunks = depth // 8
    sub = lax.broadcasted_iota(jnp.int32, (8, width), 0)
    lane = lax.broadcasted_iota(jnp.int32, (8, width), 1)
    zero = jnp.zeros((8, width), jnp.float32)

    def body(it, carry):
        r = pl.multiple_of(it * 8, 8)
        centre = [mod_ref[y, pl.ds(r, 8), :] for y in range(rows_y)]
        prev = [
            jnp.where(it == 0, zero, mod_ref[y, pl.ds(jnp.maximum(r - 8, 0), 8), :])
            for y in range(rows_y)
        ]
        nxt = [
            jnp.where(it == chunks - 1, zero, mod_ref[y, pl.ds(jnp.minimum(r + 8, depth - 8), 8), :])
            for y in range(rows_y)
        ]
        comps = [[GAMMA * centre[y] for y in range(rows_y)] for c in range(3)]
        index = 0
        for off_x in (-1, 0, 1):
            if off_x == 0:
                shifted_x = centre
            elif off_x < 0:
                shifted_x = [
                    jnp.where(sub == 0, pltpu.roll(prev[y], 1, 0), pltpu.roll(centre[y], 1, 0))
                    for y in range(rows_y)
                ]
            else:
                shifted_x = [
                    jnp.where(sub == 7, pltpu.roll(nxt[y], 7, 0), pltpu.roll(centre[y], 7, 0))
                    for y in range(rows_y)
                ]
            shifted = {0: shifted_x}
            shifted[-1] = [jnp.where(lane == 0, jnp.float32(0.0), pltpu.roll(v, 1, 1)) for v in shifted_x]
            shifted[1] = [
                jnp.where(lane == width - 1, jnp.float32(0.0), pltpu.roll(v, width - 1, 1))
                for v in shifted_x
            ]
            for off_y in (-1, 0, 1):
                for off_z in (-1, 0, 1):
                    if (off_x, off_y, off_z) == (0, 0, 0):
                        continue
                    offset = (off_x, off_y, off_z)
                    norm_sq = off_x * off_x + off_y * off_y + off_z * off_z
                    for y in range(rows_y):
                        source = y + off_y
                        if 0 <= source < rows_y:
                            other = shifted[off_z][source]
                        else:
                            other = zero
                        edge = EDGE_WEIGHTS[norm_sq] * 0.5 * (centre[y] + other)
                        edge_ref[index, y, pl.ds(r, 8), :] = edge
                        for c in range(3):
                            comps[c][y] = comps[c][y] + edge * (
                                1.0 + BETA * offset[c] * offset[c] / norm_sq
                            )
                    index += 1
        for y in range(rows_y):
            centre_ref[y, pl.ds(r, 8), :] = centre[y]
            for c in range(3):
                diag_ref[c, y, pl.ds(r, 8), :] = comps[c][y]
        return carry

    lax.fori_loop(0, chunks, body, 0)


def stencil_body(field_ref, edge_ref, cm_ref, out_ref):
    samples, _, rows_y, depth, width = field_ref.shape
    chunks = depth // 8
    sub = lax.broadcasted_iota(jnp.int32, (8, width), 0)
    lane = lax.broadcasted_iota(jnp.int32, (8, width), 1)
    zero = jnp.zeros((8, width), jnp.float32)

    def body(it, carry):
        s = it // chunks
        part = it % chunks
        r = pl.multiple_of(part * 8, 8)

        def rows(c, y, off):
            if off == 0:
                return field_ref[s, c, y, pl.ds(r, 8), :]
            if off < 0:
                return jnp.where(
                    part == 0, zero, field_ref[s, c, y, pl.ds(jnp.maximum(r - 8, 0), 8), :]
                )
            return jnp.where(
                part == chunks - 1,
                zero,
                field_ref[s, c, y, pl.ds(jnp.minimum(r + 8, depth - 8), 8), :],
            )

        centre = [[rows(c, y, 0) for y in range(rows_y)] for c in range(3)]
        acc = [
            [GAMMA * cm_ref[y, pl.ds(r, 8), :] * centre[c][y] for y in range(rows_y)]
            for c in range(3)
        ]
        index = 0
        for off_x in (-1, 0, 1):
            if off_x == 0:
                shifted_x = centre
            elif off_x < 0:
                shifted_x = [
                    [
                        jnp.where(
                            sub == 0,
                            pltpu.roll(rows(c, y, -1), 1, 0),
                            pltpu.roll(centre[c][y], 1, 0),
                        )
                        for y in range(rows_y)
                    ]
                    for c in range(3)
                ]
            else:
                shifted_x = [
                    [
                        jnp.where(
                            sub == 7,
                            pltpu.roll(rows(c, y, 1), 7, 0),
                            pltpu.roll(centre[c][y], 7, 0),
                        )
                        for y in range(rows_y)
                    ]
                    for c in range(3)
                ]
            shifted = {0: shifted_x}
            shifted[-1] = [
                [jnp.where(lane == 0, jnp.float32(0.0), pltpu.roll(v, 1, 1)) for v in per_c]
                for per_c in shifted_x
            ]
            shifted[1] = [
                [
                    jnp.where(lane == width - 1, jnp.float32(0.0), pltpu.roll(v, width - 1, 1))
                    for v in per_c
                ]
                for per_c in shifted_x
            ]
            for off_y in (-1, 0, 1):
                for off_z in (-1, 0, 1):
                    if (off_x, off_y, off_z) == (0, 0, 0):
                        continue
                    offset = (off_x, off_y, off_z)
                    norm_sq = off_x * off_x + off_y * off_y + off_z * off_z
                    for y in range(rows_y):
                        edge = edge_ref[index, y, pl.ds(r, 8), :]
                        source = y + off_y
                        if 0 <= source < rows_y:
                            delta = [centre[c][y] - shifted[off_z][c][source] for c in range(3)]
                        else:
                            delta = [centre[c][y] for c in range(3)]
                        project = None
                        for c in range(3):
                            if offset[c] > 0:
                                project = delta[c] if project is None else project + delta[c]
                            elif offset[c] < 0:
                                project = -delta[c] if project is None else project - delta[c]
                        if norm_sq == 2:
                            project = project * 0.5
                        elif norm_sq == 3:
                            project = project * (1.0 / 3.0)
                        for c in range(3):
                            if offset[c] != 0:
                                acc[c][y] = acc[c][y] + edge * (delta[c] + BETA * offset[c] * project)
                            else:
                                acc[c][y] = acc[c][y] + edge * delta[c]
                    index += 1
        for c in range(3):
            for y in range(rows_y):
                out_ref[s, c, y, pl.ds(r, 8), :] = acc[c][y]
        return carry

    lax.fori_loop(0, samples * chunks, body, 0)


def chain_kernel(
    scal_ref, moduli_ref, mask_ref, md_ref, ld_ref, ids_ref, disp_ref, res_ref,
    mod_s, edge_s, cm_s, jac_s, k_s, a_s, step0_s, step1_s,
):
    samples, _, rows_y, depth, width = md_ref.shape
    theta = scal_ref[0]
    c1 = scal_ref[1]
    c2 = scal_ref[2]
    keep_mod = mask_ref[2] > 0.0
    for y in range(rows_y):
        ids = ids_ref[y]
        modulus = jnp.zeros(ids.shape, jnp.float32)
        for index in range(MATERIALS):
            modulus = modulus + jnp.where(ids == float(index), moduli_ref[index], jnp.float32(0.0))
        mod_s[y] = jnp.where(keep_mod, modulus, jnp.float32(0.0))
    edges_body(mod_s, edge_s, cm_s, jac_s)
    stencil_body(md_ref, edge_s, cm_s, k_s)
    keep0 = mask_ref[0] > 0.0
    keep1 = mask_ref[1] > 0.0

    def first(it, carry):
        s = it // 3
        c = it % 3
        for y in range(rows_y):
            start = ld_ref[s, c, y] - k_s[s, c, y]
            a_s[s, c, y] = start
            step0_s[s, c, y] = jnp.where(keep0, start / (theta * jac_s[c, y]), jnp.float32(0.0))
        return carry

    lax.fori_loop(0, samples * 3, first, 0)
    stencil_body(step0_s, edge_s, cm_s, k_s)

    def second(it, carry):
        s = it // 3
        c = it % 3
        for y in range(rows_y):
            residual1 = a_s[s, c, y] - k_s[s, c, y]
            a_s[s, c, y] = residual1
            step0 = step0_s[s, c, y]
            step1 = jnp.where(
                keep1, c1 * step0 + c2 * residual1 / jac_s[c, y], jnp.float32(0.0)
            )
            step1_s[s, c, y] = step1
            disp_ref[s, c, y] = md_ref[s, c, y] + step0 + step1
        return carry

    lax.fori_loop(0, samples * 3, second, 0)
    stencil_body(step1_s, edge_s, cm_s, k_s)

    def third(it, carry):
        s = it // 3
        c = it % 3
        for y in range(rows_y):
            res_ref[s, c, y] = a_s[s, c, y] - k_s[s, c, y]
        return carry

    lax.fori_loop(0, samples * 3, third, 0)


def run_chain(scalars, moduli, masks, md, ld, ids):
    samples, _, rows_y, depth, width = md.shape
    vmem = pl.BlockSpec(memory_space=pltpu.VMEM)
    smem = pl.BlockSpec(memory_space=pltpu.SMEM)
    field = jax.ShapeDtypeStruct(md.shape, jnp.float32)
    size = md.size
    return pl.pallas_call(
        chain_kernel,
        out_shape=(field, field),
        in_specs=[smem, smem, vmem, vmem, vmem, vmem],
        out_specs=(vmem, vmem),
        scratch_shapes=[
            pltpu.VMEM((rows_y, depth, width), jnp.float32),
            pltpu.VMEM((len(OFFSETS), rows_y, depth, width), jnp.float32),
            pltpu.VMEM((rows_y, depth, width), jnp.float32),
            pltpu.VMEM((3, rows_y, depth, width), jnp.float32),
        ]
        + [pltpu.VMEM(md.shape, jnp.float32)] * 4,
        compiler_params=pltpu.CompilerParams(vmem_limit_bytes=48 * 1024 * 1024),
        cost_estimate=pl.CostEstimate(
            flops=3 * 26 * 20 * size, bytes_accessed=4 * 5 * size, transcendentals=0
        ),
    )(scalars, moduli, masks, md, ld, ids)


def lookup_modulus(material, moduli):
    modulus = jnp.zeros(material.shape, jnp.float32)
    for index in range(MATERIALS):
        modulus = modulus + jnp.where(material == float(index), moduli[index], jnp.float32(0.0))
    return modulus


def neighbour_devices(part_device, partners):
    count = part_device.shape[0]
    ids = jnp.arange(count, dtype=jnp.int32)
    hit = part_device[None, :] == ids[:, None]
    place = jnp.sum(jnp.where(hit, ids[None, :], 0), axis=1)
    upper = place % 2 == 0
    up_dev = jnp.where(upper, partners[0], partners[1])
    low_dev = jnp.where(upper, partners[1], partners[0])
    return up_dev, low_dev


def exchange(first, last, up_dev, low_dev):
    col = lax.axis_index("col")
    grp = lax.axis_index("grp")
    me = col * GROUP + grp
    cols = up_dev.shape[0] // GROUP
    rows = first.shape[0]
    pack = jnp.concatenate([first, last], axis=0)[None]
    held = lax.all_gather(pack, "grp", axis=0, tiled=True)
    pick = (jnp.arange(GROUP, dtype=jnp.int32) == grp)[None, :]
    t_up = jnp.sum(jnp.where(pick, up_dev.reshape(cols, GROUP), 0), axis=1)
    t_low = jnp.sum(jnp.where(pick, low_dev.reshape(cols, GROUP), 0), axis=1)
    up_at = jnp.where(t_up // GROUP == col, t_up % GROUP, -1)[:, None, None]
    low_at = jnp.where(t_low // GROUP == col, t_low % GROUP, -1)[:, None, None]
    from_up = jnp.zeros((cols,) + first.shape, jnp.float32)
    from_low = jnp.zeros((cols,) + first.shape, jnp.float32)
    for k in range(GROUP):
        from_up = jnp.where(up_at == k, held[k, :rows][None], from_up)
        from_low = jnp.where(low_at == k, held[k, rows:][None], from_low)
    slots = jnp.concatenate([from_up, from_low], axis=1)
    got = lax.all_to_all(slots, "col", 0, 0, tiled=True)
    my_up = up_dev[me]
    my_low = low_dev[me]
    above = lax.dynamic_index_in_dim(got, my_up // GROUP, axis=0, keepdims=False)[:rows]
    below = lax.dynamic_index_in_dim(got, my_low // GROUP, axis=0, keepdims=False)[rows:]
    above = jnp.where(my_up != me, above, jnp.float32(0.0))
    below = jnp.where(my_low != me, below, jnp.float32(0.0))
    return below, above


def on_device(loads, modal_disp, material, moduli, part_device, partners, low_bound, high_bound):
    up_dev, low_dev = neighbour_devices(part_device, partners)
    samples, _, depth, rows_y, width = loads.shape
    ids_orig = material.astype(jnp.float32)
    plane = (samples, 3, rows_y, width)
    plane_size = samples * 3 * rows_y * width
    mod_size = rows_y * width

    def pack(md_rows, load_rows):
        parts = [modal_disp[:, :, r].reshape(-1) for r in md_rows]
        parts += [loads[:, :, r].reshape(-1) for r in load_rows]
        parts += [ids_orig[r].reshape(-1) for r in md_rows]
        flat = jnp.concatenate(parts)
        return flat.reshape(flat.shape[0] // width, width)

    first = pack((0, 1, 2), (0, 1))
    last = pack((depth - 3, depth - 2, depth - 1), (depth - 2, depth - 1))
    below, above = exchange(first, last, up_dev, low_dev)
    below = below.reshape(-1)
    above = above.reshape(-1)

    def planes_of(got, count, start, size, shape):
        return [got[start + i * size : start + (i + 1) * size].reshape(shape) for i in range(count)]

    md_below = planes_of(below, 3, 0, plane_size, plane)
    md_above = planes_of(above, 3, 0, plane_size, plane)
    ld_below = planes_of(below, 2, 3 * plane_size, plane_size, plane)
    ld_above = planes_of(above, 2, 3 * plane_size, plane_size, plane)
    ids_below = planes_of(below, 3, 5 * plane_size, mod_size, (rows_y, width))
    ids_above = planes_of(above, 3, 5 * plane_size, mod_size, (rows_y, width))

    loads = jnp.transpose(loads, (0, 1, 3, 2, 4))
    modal_disp = jnp.transpose(modal_disp, (0, 1, 3, 2, 4))
    ids = jnp.transpose(ids_orig, (1, 0, 2))

    mine = jnp.arange(up_dev.shape[0], dtype=jnp.int32) == col_grp_index()
    low_on = jnp.sum(jnp.where(mine, low_dev, 0)) != col_grp_index()
    up_on = jnp.sum(jnp.where(mine, up_dev, 0)) != col_grp_index()

    theta = (high_bound[0] + low_bound[0]) / 2.0
    half = (high_bound[0] - low_bound[0]) / 2.0
    sigma = theta / half
    rho0 = 1.0 / sigma
    rho1 = 1.0 / (2.0 * sigma - rho0)
    scalars = jnp.stack([theta, rho1 * rho0, 2.0 * rho1 / half]).astype(jnp.float32)

    def chain(md, ld, material_ids, masks):
        return run_chain(scalars, moduli, masks, md, ld, material_ids)

    disp_local, res_local = chain(modal_disp, loads, ids, jnp.ones((3, depth, width), jnp.float32))

    reach = 3
    margin = 2 * reach
    pad_rows = (-(2 * reach + 2 * margin)) % 8

    def window(own, lower, upper, axis):
        index = [slice(None)] * own.ndim
        index[axis] = slice(0, margin)
        own_head = own[tuple(index)]
        index[axis] = slice(depth - margin, depth)
        own_tail = own[tuple(index)]
        zero_shape = list(own.shape)
        zero_shape[axis] = pad_rows
        return jnp.concatenate(
            [
                jnp.stack(list(lower), axis=axis),
                own_head,
                own_tail,
                jnp.stack(list(upper), axis=axis),
                jnp.zeros(zero_shape, jnp.float32),
            ],
            axis=axis,
        )

    md_win = window(modal_disp, md_below, md_above, 3)
    ld_zero = jnp.zeros(plane, jnp.float32)
    ld_win = window(loads, [ld_zero] + ld_below, ld_above + [ld_zero], 3)
    ids_win = window(ids, ids_below, ids_above, 1)
    logical = jnp.concatenate(
        [
            jnp.arange(-reach, margin, dtype=jnp.int32),
            jnp.arange(depth - margin, depth + reach, dtype=jnp.int32),
            jnp.full((pad_rows,), depth + 8, dtype=jnp.int32),
        ]
    )

    def valid(reach):
        keep = (logical >= 0) & (logical < depth)
        keep = keep | (low_on & (logical >= -reach) & (logical < 0))
        keep = keep | (up_on & (logical >= depth) & (logical < depth + reach))
        return jnp.broadcast_to(keep.astype(jnp.float32)[:, None], (logical.shape[0], width))

    masks = jnp.stack([valid(2), valid(1), valid(3)], axis=0)
    disp_win, res_win = chain(md_win, ld_win, ids_win, masks)

    def patch(out, win):
        out = lax.dynamic_update_slice_in_dim(out, win[:, :, :, reach : 2 * reach], 0, axis=3)
        out = lax.dynamic_update_slice_in_dim(
            out, win[:, :, :, reach + 2 * margin - reach : reach + 2 * margin], depth - reach, axis=3
        )
        return jnp.transpose(out, (0, 1, 3, 2, 4))

    return (patch(disp_local, disp_win), patch(res_local, res_win))


def col_grp_index():
    return lax.axis_index("col") * GROUP + lax.axis_index("grp")


def solution(mesh):
    devices = mesh.devices.reshape(-1)
    grid = Mesh(devices.reshape(devices.size // GROUP, GROUP), ("col", "grp"))
    slab = ("col", "grp")
    in_specs = (
        P(None, None, slab, None, None),
        P(None, None, slab, None, None),
        P(slab, None, None),
        P(),
        P(),
        P(),
        P(),
        P(),
    )
    out_specs = (P(None, None, slab, None, None), P(None, None, slab, None, None))
    return jax.shard_map(
        on_device, mesh=grid, in_specs=in_specs, out_specs=out_specs, check_vma=False
    )
```

```python
import jax
import jax.numpy as jnp
from jax import lax
from jax.experimental import pallas as pl
from jax.experimental.pallas import tpu as pltpu
from jax.sharding import Mesh, PartitionSpec as P

MATERIALS = 8
GROUP = 8

GAMMA = 0.2
BETA = 0.5
EDGE_WEIGHTS = (0.0, 1.0, 0.5, 0.25)
OFFSETS = [
    (a, b, c) for a in (-1, 0, 1) for b in (-1, 0, 1) for c in (-1, 0, 1) if (a, b, c) != (0, 0, 0)
]


def shift_cells(array, axis, step):
    if step == 0:
        return array
    length = array.shape[axis]
    zero = jnp.zeros_like(lax.slice_in_dim(array, 0, 1, axis=axis))
    if step > 0:
        return jnp.concatenate([lax.slice_in_dim(array, 1, length, axis=axis), zero], axis=axis)
    return jnp.concatenate([zero, lax.slice_in_dim(array, 0, length - 1, axis=axis)], axis=axis)


def mod_neighbour(mod_ext, off_x, off_y, off_z, depth):
    rows = lax.slice_in_dim(mod_ext, 1 + off_x, 1 + off_x + depth, axis=1)
    return shift_cells(shift_cells(rows, 0, off_y), 2, off_z)


def edges_of(mod_ext, depth):
    centre = mod_neighbour(mod_ext, 0, 0, 0, depth)
    edges = []
    for offset in OFFSETS:
        norm_sq = offset[0] * offset[0] + offset[1] * offset[1] + offset[2] * offset[2]
        edges.append(
            EDGE_WEIGHTS[norm_sq]
            * 0.5
            * (centre + mod_neighbour(mod_ext, offset[0], offset[1], offset[2], depth))
        )
    return centre, edges


def diagonal_of(centre, edges):
    comps = [GAMMA * centre, GAMMA * centre, GAMMA * centre]
    for offset, edge in zip(OFFSETS, edges):
        norm_sq = offset[0] * offset[0] + offset[1] * offset[1] + offset[2] * offset[2]
        for comp in range(3):
            comps[comp] = comps[comp] + edge * (1.0 + BETA * offset[comp] * offset[comp] / norm_sq)
    return jnp.stack(comps, axis=0)


def edges_body(mod_ref, edge_ref, centre_ref, diag_ref):
    rows_y, depth, width = mod_ref.shape
    chunks = depth // 8
    sub = lax.broadcasted_iota(jnp.int32, (8, width), 0)
    lane = lax.broadcasted_iota(jnp.int32, (8, width), 1)
    zero = jnp.zeros((8, width), jnp.float32)

    def body(it, carry):
        r = pl.multiple_of(it * 8, 8)
        centre = [mod_ref[y, pl.ds(r, 8), :] for y in range(rows_y)]
        prev = [
            jnp.where(it == 0, zero, mod_ref[y, pl.ds(jnp.maximum(r - 8, 0), 8), :])
            for y in range(rows_y)
        ]
        nxt = [
            jnp.where(it == chunks - 1, zero, mod_ref[y, pl.ds(jnp.minimum(r + 8, depth - 8), 8), :])
            for y in range(rows_y)
        ]
        comps = [[GAMMA * centre[y] for y in range(rows_y)] for c in range(3)]
        index = 0
        for off_x in (-1, 0, 1):
            if off_x == 0:
                shifted_x = centre
            elif off_x < 0:
                shifted_x = [
                    jnp.where(sub == 0, pltpu.roll(prev[y], 1, 0), pltpu.roll(centre[y], 1, 0))
                    for y in range(rows_y)
                ]
            else:
                shifted_x = [
                    jnp.where(sub == 7, pltpu.roll(nxt[y], 7, 0), pltpu.roll(centre[y], 7, 0))
                    for y in range(rows_y)
                ]
            shifted = {0: shifted_x}
            shifted[-1] = [jnp.where(lane == 0, jnp.float32(0.0), pltpu.roll(v, 1, 1)) for v in shifted_x]
            shifted[1] = [
                jnp.where(lane == width - 1, jnp.float32(0.0), pltpu.roll(v, width - 1, 1))
                for v in shifted_x
            ]
            for off_y in (-1, 0, 1):
                for off_z in (-1, 0, 1):
                    if (off_x, off_y, off_z) == (0, 0, 0):
                        continue
                    offset = (off_x, off_y, off_z)
                    norm_sq = off_x * off_x + off_y * off_y + off_z * off_z
                    for y in range(rows_y):
                        source = y + off_y
                        if 0 <= source < rows_y:
                            other = shifted[off_z][source]
                        else:
                            other = zero
                        edge = EDGE_WEIGHTS[norm_sq] * 0.5 * (centre[y] + other)
                        edge_ref[index, y, pl.ds(r, 8), :] = edge
                        for c in range(3):
                            comps[c][y] = comps[c][y] + edge * (
                                1.0 + BETA * offset[c] * offset[c] / norm_sq
                            )
                    index += 1
        for y in range(rows_y):
            centre_ref[y, pl.ds(r, 8), :] = centre[y]
            for c in range(3):
                diag_ref[c, y, pl.ds(r, 8), :] = comps[c][y]
        return carry

    lax.fori_loop(0, chunks, body, 0)


def stencil_body(field_ref, edge_ref, cm_ref, out_ref):
    samples, _, rows_y, depth, width = field_ref.shape
    chunks = depth // 8
    sub = lax.broadcasted_iota(jnp.int32, (8, width), 0)
    lane = lax.broadcasted_iota(jnp.int32, (8, width), 1)
    zero = jnp.zeros((8, width), jnp.float32)

    def body(it, carry):
        s = it // chunks
        part = it % chunks
        r = pl.multiple_of(part * 8, 8)

        def rows(c, y, off):
            if off == 0:
                return field_ref[s, c, y, pl.ds(r, 8), :]
            if off < 0:
                return jnp.where(
                    part == 0, zero, field_ref[s, c, y, pl.ds(jnp.maximum(r - 8, 0), 8), :]
                )
            return jnp.where(
                part == chunks - 1,
                zero,
                field_ref[s, c, y, pl.ds(jnp.minimum(r + 8, depth - 8), 8), :],
            )

        centre = [[rows(c, y, 0) for y in range(rows_y)] for c in range(3)]
        acc = [
            [GAMMA * cm_ref[y, pl.ds(r, 8), :] * centre[c][y] for y in range(rows_y)]
            for c in range(3)
        ]
        index = 0
        for off_x in (-1, 0, 1):
            if off_x == 0:
                shifted_x = centre
            elif off_x < 0:
                shifted_x = [
                    [
                        jnp.where(
                            sub == 0,
                            pltpu.roll(rows(c, y, -1), 1, 0),
                            pltpu.roll(centre[c][y], 1, 0),
                        )
                        for y in range(rows_y)
                    ]
                    for c in range(3)
                ]
            else:
                shifted_x = [
                    [
                        jnp.where(
                            sub == 7,
                            pltpu.roll(rows(c, y, 1), 7, 0),
                            pltpu.roll(centre[c][y], 7, 0),
                        )
                        for y in range(rows_y)
                    ]
                    for c in range(3)
                ]
            shifted = {0: shifted_x}
            shifted[-1] = [
                [jnp.where(lane == 0, jnp.float32(0.0), pltpu.roll(v, 1, 1)) for v in per_c]
                for per_c in shifted_x
            ]
            shifted[1] = [
                [
                    jnp.where(lane == width - 1, jnp.float32(0.0), pltpu.roll(v, width - 1, 1))
                    for v in per_c
                ]
                for per_c in shifted_x
            ]
            for off_y in (-1, 0, 1):
                for off_z in (-1, 0, 1):
                    if (off_x, off_y, off_z) == (0, 0, 0):
                        continue
                    offset = (off_x, off_y, off_z)
                    norm_sq = off_x * off_x + off_y * off_y + off_z * off_z
                    for y in range(rows_y):
                        edge = edge_ref[index, y, pl.ds(r, 8), :]
                        source = y + off_y
                        if 0 <= source < rows_y:
                            delta = [centre[c][y] - shifted[off_z][c][source] for c in range(3)]
                        else:
                            delta = [centre[c][y] for c in range(3)]
                        project = None
                        for c in range(3):
                            if offset[c] > 0:
                                project = delta[c] if project is None else project + delta[c]
                            elif offset[c] < 0:
                                project = -delta[c] if project is None else project - delta[c]
                        if norm_sq == 2:
                            project = project * 0.5
                        elif norm_sq == 3:
                            project = project * (1.0 / 3.0)
                        for c in range(3):
                            if offset[c] != 0:
                                acc[c][y] = acc[c][y] + edge * (delta[c] + BETA * offset[c] * project)
                            else:
                                acc[c][y] = acc[c][y] + edge * delta[c]
                    index += 1
        for c in range(3):
            for y in range(rows_y):
                out_ref[s, c, y, pl.ds(r, 8), :] = acc[c][y]
        return carry

    lax.fori_loop(0, samples * chunks, body, 0)


def chain_kernel(
    scal_ref, moduli_ref, mask_ref, md_ref, ld_ref, ids_ref, disp_ref, res_ref,
    mod_s, edge_s, cm_s, jac_s, k_s, a_s, step0_s, step1_s,
):
    samples, _, rows_y, depth, width = md_ref.shape
    theta = scal_ref[0]
    c1 = scal_ref[1]
    c2 = scal_ref[2]
    keep_mod = mask_ref[2] > 0.0
    for y in range(rows_y):
        ids = ids_ref[y]
        modulus = jnp.zeros(ids.shape, jnp.float32)
        for index in range(MATERIALS):
            modulus = modulus + jnp.where(ids == float(index), moduli_ref[index], jnp.float32(0.0))
        mod_s[y] = jnp.where(keep_mod, modulus, jnp.float32(0.0))
    edges_body(mod_s, edge_s, cm_s, jac_s)
    stencil_body(md_ref, edge_s, cm_s, k_s)
    keep0 = mask_ref[0] > 0.0
    keep1 = mask_ref[1] > 0.0

    def first(it, carry):
        s = it // 3
        c = it % 3
        for y in range(rows_y):
            start = ld_ref[s, c, y] - k_s[s, c, y]
            a_s[s, c, y] = start
            step0_s[s, c, y] = jnp.where(keep0, start / (theta * jac_s[c, y]), jnp.float32(0.0))
        return carry

    lax.fori_loop(0, samples * 3, first, 0)
    stencil_body(step0_s, edge_s, cm_s, k_s)

    def second(it, carry):
        s = it // 3
        c = it % 3
        for y in range(rows_y):
            residual1 = a_s[s, c, y] - k_s[s, c, y]
            a_s[s, c, y] = residual1
            step0 = step0_s[s, c, y]
            step1 = jnp.where(
                keep1, c1 * step0 + c2 * residual1 / jac_s[c, y], jnp.float32(0.0)
            )
            step1_s[s, c, y] = step1
            disp_ref[s, c, y] = md_ref[s, c, y] + step0 + step1
        return carry

    lax.fori_loop(0, samples * 3, second, 0)
    stencil_body(step1_s, edge_s, cm_s, k_s)

    def third(it, carry):
        s = it // 3
        c = it % 3
        for y in range(rows_y):
            res_ref[s, c, y] = a_s[s, c, y] - k_s[s, c, y]
        return carry

    lax.fori_loop(0, samples * 3, third, 0)


def run_chain(scalars, moduli, masks, md, ld, ids, fuse=False):
    samples, _, rows_y, depth, width = md.shape
    vmem = pl.BlockSpec(memory_space=pltpu.VMEM)
    smem = pl.BlockSpec(memory_space=pltpu.SMEM)
    field = jax.ShapeDtypeStruct(md.shape, jnp.float32)
    size = md.size
    return pl.pallas_call(
        chain_kernel,
        out_shape=(field, field),
        in_specs=[smem, smem, vmem, vmem, vmem, vmem],
        out_specs=(vmem, vmem),
        scratch_shapes=[
            pltpu.VMEM((rows_y, depth, width), jnp.float32),
            pltpu.VMEM((len(OFFSETS), rows_y, depth, width), jnp.float32),
            pltpu.VMEM((rows_y, depth, width), jnp.float32),
            pltpu.VMEM((3, rows_y, depth, width), jnp.float32),
        ]
        + [pltpu.VMEM(md.shape, jnp.float32)] * 4,
        compiler_params=pltpu.CompilerParams(
            vmem_limit_bytes=48 * 1024 * 1024,
            allow_input_fusion=[False, False, fuse, fuse, fuse, fuse],
        ),
        cost_estimate=pl.CostEstimate(
            flops=3 * 26 * 20 * size, bytes_accessed=4 * 5 * size, transcendentals=0
        ),
    )(scalars, moduli, masks, md, ld, ids)


def lookup_modulus(material, moduli):
    modulus = jnp.zeros(material.shape, jnp.float32)
    for index in range(MATERIALS):
        modulus = modulus + jnp.where(material == float(index), moduli[index], jnp.float32(0.0))
    return modulus


def neighbour_devices(part_device, partners):
    count = part_device.shape[0]
    ids = jnp.arange(count, dtype=jnp.int32)
    hit = part_device[None, :] == ids[:, None]
    place = jnp.sum(jnp.where(hit, ids[None, :], 0), axis=1)
    upper = place % 2 == 0
    up_dev = jnp.where(upper, partners[0], partners[1])
    low_dev = jnp.where(upper, partners[1], partners[0])
    return up_dev, low_dev


def exchange(first, last, up_dev, low_dev):
    col = lax.axis_index("col")
    grp = lax.axis_index("grp")
    me = col * GROUP + grp
    cols = up_dev.shape[0] // GROUP
    rows = first.shape[0]
    pack = jnp.concatenate([first, last], axis=0)[None]
    held = lax.all_gather(pack, "grp", axis=0, tiled=True)
    pick = (jnp.arange(GROUP, dtype=jnp.int32) == grp)[None, :]
    t_up = jnp.sum(jnp.where(pick, up_dev.reshape(cols, GROUP), 0), axis=1)
    t_low = jnp.sum(jnp.where(pick, low_dev.reshape(cols, GROUP), 0), axis=1)
    up_at = jnp.where(t_up // GROUP == col, t_up % GROUP, -1)[:, None, None]
    low_at = jnp.where(t_low // GROUP == col, t_low % GROUP, -1)[:, None, None]
    from_up = jnp.zeros((cols,) + first.shape, jnp.float32)
    from_low = jnp.zeros((cols,) + first.shape, jnp.float32)
    for k in range(GROUP):
        from_up = jnp.where(up_at == k, held[k, :rows][None], from_up)
        from_low = jnp.where(low_at == k, held[k, rows:][None], from_low)
    slots = jnp.concatenate([from_up, from_low], axis=1)
    got = lax.all_to_all(slots, "col", 0, 0, tiled=True)
    my_up = up_dev[me]
    my_low = low_dev[me]
    above = lax.dynamic_index_in_dim(got, my_up // GROUP, axis=0, keepdims=False)[:rows]
    below = lax.dynamic_index_in_dim(got, my_low // GROUP, axis=0, keepdims=False)[rows:]
    above = jnp.where(my_up != me, above, jnp.float32(0.0))
    below = jnp.where(my_low != me, below, jnp.float32(0.0))
    return below, above


def on_device(loads, modal_disp, material, moduli, part_device, partners, low_bound, high_bound):
    up_dev, low_dev = neighbour_devices(part_device, partners)
    samples, _, depth, rows_y, width = loads.shape
    ids_orig = material.astype(jnp.float32)
    plane = (samples, 3, rows_y, width)
    plane_size = samples * 3 * rows_y * width
    mod_size = rows_y * width

    def pack(md_rows, load_rows):
        parts = [modal_disp[:, :, r].reshape(-1) for r in md_rows]
        parts += [loads[:, :, r].reshape(-1) for r in load_rows]
        parts += [ids_orig[r].reshape(-1) for r in md_rows]
        flat = jnp.concatenate(parts)
        return flat.reshape(flat.shape[0] // width, width)

    first = pack((0, 1, 2), (0, 1))
    last = pack((depth - 3, depth - 2, depth - 1), (depth - 2, depth - 1))
    below, above = exchange(first, last, up_dev, low_dev)
    below = below.reshape(-1)
    above = above.reshape(-1)

    def planes_of(got, count, start, size, shape):
        return [got[start + i * size : start + (i + 1) * size].reshape(shape) for i in range(count)]

    md_below = planes_of(below, 3, 0, plane_size, plane)
    md_above = planes_of(above, 3, 0, plane_size, plane)
    ld_below = planes_of(below, 2, 3 * plane_size, plane_size, plane)
    ld_above = planes_of(above, 2, 3 * plane_size, plane_size, plane)
    ids_below = planes_of(below, 3, 5 * plane_size, mod_size, (rows_y, width))
    ids_above = planes_of(above, 3, 5 * plane_size, mod_size, (rows_y, width))

    loads = jnp.transpose(loads, (0, 1, 3, 2, 4))
    modal_disp = jnp.transpose(modal_disp, (0, 1, 3, 2, 4))
    ids = jnp.transpose(ids_orig, (1, 0, 2))

    mine = jnp.arange(up_dev.shape[0], dtype=jnp.int32) == col_grp_index()
    low_on = jnp.sum(jnp.where(mine, low_dev, 0)) != col_grp_index()
    up_on = jnp.sum(jnp.where(mine, up_dev, 0)) != col_grp_index()

    theta = (high_bound[0] + low_bound[0]) / 2.0
    half = (high_bound[0] - low_bound[0]) / 2.0
    sigma = theta / half
    rho0 = 1.0 / sigma
    rho1 = 1.0 / (2.0 * sigma - rho0)
    scalars = jnp.stack([theta, rho1 * rho0, 2.0 * rho1 / half]).astype(jnp.float32)

    def chain(md, ld, material_ids, masks, fuse=False):
        return run_chain(scalars, moduli, masks, md, ld, material_ids, fuse)

    disp_local, res_local = chain(modal_disp, loads, ids, jnp.ones((3, depth, width), jnp.float32))

    reach = 3
    margin = 2 * reach
    pad_rows = (-(2 * reach + 2 * margin)) % 8

    def window(own, lower, upper, axis):
        index = [slice(None)] * own.ndim
        index[axis] = slice(0, margin)
        own_head = own[tuple(index)]
        index[axis] = slice(depth - margin, depth)
        own_tail = own[tuple(index)]
        zero_shape = list(own.shape)
        zero_shape[axis] = pad_rows
        return jnp.concatenate(
            [
                jnp.stack(list(lower), axis=axis),
                own_head,
                own_tail,
                jnp.stack(list(upper), axis=axis),
                jnp.zeros(zero_shape, jnp.float32),
            ],
            axis=axis,
        )

    md_win = window(modal_disp, md_below, md_above, 3)
    ld_zero = jnp.zeros(plane, jnp.float32)
    ld_win = window(loads, [ld_zero] + ld_below, ld_above + [ld_zero], 3)
    ids_win = window(ids, ids_below, ids_above, 1)
    logical = jnp.concatenate(
        [
            jnp.arange(-reach, margin, dtype=jnp.int32),
            jnp.arange(depth - margin, depth + reach, dtype=jnp.int32),
            jnp.full((pad_rows,), depth + 8, dtype=jnp.int32),
        ]
    )

    def valid(reach):
        keep = (logical >= 0) & (logical < depth)
        keep = keep | (low_on & (logical >= -reach) & (logical < 0))
        keep = keep | (up_on & (logical >= depth) & (logical < depth + reach))
        return jnp.broadcast_to(keep.astype(jnp.float32)[:, None], (logical.shape[0], width))

    masks = jnp.stack([valid(2), valid(1), valid(3)], axis=0)
    disp_win, res_win = chain(md_win, ld_win, ids_win, masks, True)

    def patch(out, win):
        out = lax.dynamic_update_slice_in_dim(out, win[:, :, :, reach : 2 * reach], 0, axis=3)
        out = lax.dynamic_update_slice_in_dim(
            out, win[:, :, :, reach + 2 * margin - reach : reach + 2 * margin], depth - reach, axis=3
        )
        return jnp.transpose(out, (0, 1, 3, 2, 4))

    return (patch(disp_local, disp_win), patch(res_local, res_win))


def col_grp_index():
    return lax.axis_index("col") * GROUP + lax.axis_index("grp")


def solution(mesh):
    devices = mesh.devices.reshape(-1)
    grid = Mesh(devices.reshape(devices.size // GROUP, GROUP), ("col", "grp"))
    slab = ("col", "grp")
    in_specs = (
        P(None, None, slab, None, None),
        P(None, None, slab, None, None),
        P(slab, None, None),
        P(),
        P(),
        P(),
        P(),
        P(),
    )
    out_specs = (P(None, None, slab, None, None), P(None, None, slab, None, None))
    return jax.shard_map(
        on_device, mesh=grid, in_specs=in_specs, out_specs=out_specs, check_vma=False
    )
```

```python
import jax
import jax.numpy as jnp
from jax import lax
from jax.experimental import pallas as pl
from jax.experimental.pallas import tpu as pltpu
from jax.sharding import Mesh, PartitionSpec as P

MATERIALS = 8
GROUP = 8

GAMMA = 0.2
BETA = 0.5
EDGE_WEIGHTS = (0.0, 1.0, 0.5, 0.25)
OFFSETS = [
    (a, b, c) for a in (-1, 0, 1) for b in (-1, 0, 1) for c in (-1, 0, 1) if (a, b, c) != (0, 0, 0)
]


def shift_cells(array, axis, step):
    if step == 0:
        return array
    length = array.shape[axis]
    zero = jnp.zeros_like(lax.slice_in_dim(array, 0, 1, axis=axis))
    if step > 0:
        return jnp.concatenate([lax.slice_in_dim(array, 1, length, axis=axis), zero], axis=axis)
    return jnp.concatenate([zero, lax.slice_in_dim(array, 0, length - 1, axis=axis)], axis=axis)


def mod_neighbour(mod_ext, off_x, off_y, off_z, depth):
    rows = lax.slice_in_dim(mod_ext, 1 + off_x, 1 + off_x + depth, axis=1)
    return shift_cells(shift_cells(rows, 0, off_y), 2, off_z)


def edges_of(mod_ext, depth):
    centre = mod_neighbour(mod_ext, 0, 0, 0, depth)
    edges = []
    for offset in OFFSETS:
        norm_sq = offset[0] * offset[0] + offset[1] * offset[1] + offset[2] * offset[2]
        edges.append(
            EDGE_WEIGHTS[norm_sq]
            * 0.5
            * (centre + mod_neighbour(mod_ext, offset[0], offset[1], offset[2], depth))
        )
    return centre, edges


def diagonal_of(centre, edges):
    comps = [GAMMA * centre, GAMMA * centre, GAMMA * centre]
    for offset, edge in zip(OFFSETS, edges):
        norm_sq = offset[0] * offset[0] + offset[1] * offset[1] + offset[2] * offset[2]
        for comp in range(3):
            comps[comp] = comps[comp] + edge * (1.0 + BETA * offset[comp] * offset[comp] / norm_sq)
    return jnp.stack(comps, axis=0)


def edges_body(mod_ref, edge_ref, centre_ref, diag_ref):
    rows_y, depth, width = mod_ref.shape
    chunks = depth // 8
    sub = lax.broadcasted_iota(jnp.int32, (8, width), 0)
    lane = lax.broadcasted_iota(jnp.int32, (8, width), 1)
    zero = jnp.zeros((8, width), jnp.float32)

    def body(it, carry):
        r = pl.multiple_of(it * 8, 8)
        centre = [mod_ref[y, pl.ds(r, 8), :] for y in range(rows_y)]
        prev = [
            jnp.where(it == 0, zero, mod_ref[y, pl.ds(jnp.maximum(r - 8, 0), 8), :])
            for y in range(rows_y)
        ]
        nxt = [
            jnp.where(it == chunks - 1, zero, mod_ref[y, pl.ds(jnp.minimum(r + 8, depth - 8), 8), :])
            for y in range(rows_y)
        ]
        comps = [[GAMMA * centre[y] for y in range(rows_y)] for c in range(3)]
        index = 0
        for off_x in (-1, 0, 1):
            if off_x == 0:
                shifted_x = centre
            elif off_x < 0:
                shifted_x = [
                    jnp.where(sub == 0, pltpu.roll(prev[y], 1, 0), pltpu.roll(centre[y], 1, 0))
                    for y in range(rows_y)
                ]
            else:
                shifted_x = [
                    jnp.where(sub == 7, pltpu.roll(nxt[y], 7, 0), pltpu.roll(centre[y], 7, 0))
                    for y in range(rows_y)
                ]
            shifted = {0: shifted_x}
            shifted[-1] = [jnp.where(lane == 0, jnp.float32(0.0), pltpu.roll(v, 1, 1)) for v in shifted_x]
            shifted[1] = [
                jnp.where(lane == width - 1, jnp.float32(0.0), pltpu.roll(v, width - 1, 1))
                for v in shifted_x
            ]
            for off_y in (-1, 0, 1):
                for off_z in (-1, 0, 1):
                    if (off_x, off_y, off_z) == (0, 0, 0):
                        continue
                    offset = (off_x, off_y, off_z)
                    norm_sq = off_x * off_x + off_y * off_y + off_z * off_z
                    for y in range(rows_y):
                        source = y + off_y
                        if 0 <= source < rows_y:
                            other = shifted[off_z][source]
                        else:
                            other = zero
                        edge = EDGE_WEIGHTS[norm_sq] * 0.5 * (centre[y] + other)
                        edge_ref[index, y, pl.ds(r, 8), :] = edge
                        for c in range(3):
                            comps[c][y] = comps[c][y] + edge * (
                                1.0 + BETA * offset[c] * offset[c] / norm_sq
                            )
                    index += 1
        for y in range(rows_y):
            centre_ref[y, pl.ds(r, 8), :] = centre[y]
            for c in range(3):
                diag_ref[c, y, pl.ds(r, 8), :] = comps[c][y]
        return carry

    lax.fori_loop(0, chunks, body, 0)


def stencil_body(field_ref, edge_ref, cm_ref, out_ref):
    samples, _, rows_y, depth, width = field_ref.shape
    chunks = depth // 8
    sub = lax.broadcasted_iota(jnp.int32, (8, width), 0)
    lane = lax.broadcasted_iota(jnp.int32, (8, width), 1)
    zero = jnp.zeros((8, width), jnp.float32)

    def body(it, carry):
        s = it // chunks
        part = it % chunks
        r = pl.multiple_of(part * 8, 8)

        def rows(c, y, off):
            if off == 0:
                return field_ref[s, c, y, pl.ds(r, 8), :]
            if off < 0:
                return jnp.where(
                    part == 0, zero, field_ref[s, c, y, pl.ds(jnp.maximum(r - 8, 0), 8), :]
                )
            return jnp.where(
                part == chunks - 1,
                zero,
                field_ref[s, c, y, pl.ds(jnp.minimum(r + 8, depth - 8), 8), :],
            )

        centre = [[rows(c, y, 0) for y in range(rows_y)] for c in range(3)]
        acc = [
            [GAMMA * cm_ref[y, pl.ds(r, 8), :] * centre[c][y] for y in range(rows_y)]
            for c in range(3)
        ]
        index = 0
        for off_x in (-1, 0, 1):
            if off_x == 0:
                shifted_x = centre
            elif off_x < 0:
                shifted_x = [
                    [
                        jnp.where(
                            sub == 0,
                            pltpu.roll(rows(c, y, -1), 1, 0),
                            pltpu.roll(centre[c][y], 1, 0),
                        )
                        for y in range(rows_y)
                    ]
                    for c in range(3)
                ]
            else:
                shifted_x = [
                    [
                        jnp.where(
                            sub == 7,
                            pltpu.roll(rows(c, y, 1), 7, 0),
                            pltpu.roll(centre[c][y], 7, 0),
                        )
                        for y in range(rows_y)
                    ]
                    for c in range(3)
                ]
            shifted = {0: shifted_x}
            shifted[-1] = [
                [jnp.where(lane == 0, jnp.float32(0.0), pltpu.roll(v, 1, 1)) for v in per_c]
                for per_c in shifted_x
            ]
            shifted[1] = [
                [
                    jnp.where(lane == width - 1, jnp.float32(0.0), pltpu.roll(v, width - 1, 1))
                    for v in per_c
                ]
                for per_c in shifted_x
            ]
            for off_y in (-1, 0, 1):
                for off_z in (-1, 0, 1):
                    if (off_x, off_y, off_z) == (0, 0, 0):
                        continue
                    offset = (off_x, off_y, off_z)
                    norm_sq = off_x * off_x + off_y * off_y + off_z * off_z
                    for y in range(rows_y):
                        edge = edge_ref[index, y, pl.ds(r, 8), :]
                        source = y + off_y
                        if 0 <= source < rows_y:
                            delta = [centre[c][y] - shifted[off_z][c][source] for c in range(3)]
                        else:
                            delta = [centre[c][y] for c in range(3)]
                        project = None
                        for c in range(3):
                            if offset[c] > 0:
                                project = delta[c] if project is None else project + delta[c]
                            elif offset[c] < 0:
                                project = -delta[c] if project is None else project - delta[c]
                        if norm_sq == 2:
                            project = project * 0.5
                        elif norm_sq == 3:
                            project = project * (1.0 / 3.0)
                        for c in range(3):
                            if offset[c] != 0:
                                acc[c][y] = acc[c][y] + edge * (delta[c] + BETA * offset[c] * project)
                            else:
                                acc[c][y] = acc[c][y] + edge * delta[c]
                    index += 1
        for c in range(3):
            for y in range(rows_y):
                out_ref[s, c, y, pl.ds(r, 8), :] = acc[c][y]
        return carry

    lax.fori_loop(0, samples * chunks, body, 0)


def chain_kernel(
    scal_ref, moduli_ref, mask_ref, md_ref, ld_ref, ids_ref, disp_ref, res_ref,
    mod_s, edge_s, cm_s, jac_s, k_s, a_s, step0_s, step1_s,
):
    samples, _, rows_y, depth, width = md_ref.shape
    theta = scal_ref[0]
    c1 = scal_ref[1]
    c2 = scal_ref[2]
    keep_mod = mask_ref[2] > 0.0
    for y in range(rows_y):
        ids = ids_ref[y]
        modulus = jnp.zeros(ids.shape, jnp.float32)
        for index in range(MATERIALS):
            modulus = modulus + jnp.where(ids == float(index), moduli_ref[index], jnp.float32(0.0))
        mod_s[y] = jnp.where(keep_mod, modulus, jnp.float32(0.0))
    edges_body(mod_s, edge_s, cm_s, jac_s)
    stencil_body(md_ref, edge_s, cm_s, k_s)
    keep0 = mask_ref[0] > 0.0
    keep1 = mask_ref[1] > 0.0

    def first(it, carry):
        s = it // 3
        c = it % 3
        for y in range(rows_y):
            start = ld_ref[s, c, y] - k_s[s, c, y]
            a_s[s, c, y] = start
            step0_s[s, c, y] = jnp.where(keep0, start / (theta * jac_s[c, y]), jnp.float32(0.0))
        return carry

    lax.fori_loop(0, samples * 3, first, 0)
    stencil_body(step0_s, edge_s, cm_s, k_s)

    def second(it, carry):
        s = it // 3
        c = it % 3
        for y in range(rows_y):
            residual1 = a_s[s, c, y] - k_s[s, c, y]
            a_s[s, c, y] = residual1
            step0 = step0_s[s, c, y]
            step1 = jnp.where(
                keep1, c1 * step0 + c2 * residual1 / jac_s[c, y], jnp.float32(0.0)
            )
            step1_s[s, c, y] = step1
            disp_ref[s, c, y] = md_ref[s, c, y] + step0 + step1
        return carry

    lax.fori_loop(0, samples * 3, second, 0)
    stencil_body(step1_s, edge_s, cm_s, k_s)

    def third(it, carry):
        s = it // 3
        c = it % 3
        for y in range(rows_y):
            res_ref[s, c, y] = a_s[s, c, y] - k_s[s, c, y]
        return carry

    lax.fori_loop(0, samples * 3, third, 0)


def run_chain(scalars, moduli, masks, md, ld, ids):
    samples, _, rows_y, depth, width = md.shape
    vmem = pl.BlockSpec(memory_space=pltpu.VMEM)
    smem = pl.BlockSpec(memory_space=pltpu.SMEM)
    field = jax.ShapeDtypeStruct(md.shape, jnp.float32)
    size = md.size
    return pl.pallas_call(
        chain_kernel,
        out_shape=(field, field),
        in_specs=[smem, smem, vmem, vmem, vmem, vmem],
        out_specs=(vmem, vmem),
        scratch_shapes=[
            pltpu.VMEM((rows_y, depth, width), jnp.float32),
            pltpu.VMEM((len(OFFSETS), rows_y, depth, width), jnp.float32),
            pltpu.VMEM((rows_y, depth, width), jnp.float32),
            pltpu.VMEM((3, rows_y, depth, width), jnp.float32),
        ]
        + [pltpu.VMEM(md.shape, jnp.float32)] * 4,
        compiler_params=pltpu.CompilerParams(vmem_limit_bytes=48 * 1024 * 1024),
        cost_estimate=pl.CostEstimate(
            flops=3 * 26 * 20 * size, bytes_accessed=4 * 5 * size, transcendentals=0
        ),
    )(scalars, moduli, masks, md, ld, ids)


def lookup_modulus(material, moduli):
    modulus = jnp.zeros(material.shape, jnp.float32)
    for index in range(MATERIALS):
        modulus = modulus + jnp.where(material == float(index), moduli[index], jnp.float32(0.0))
    return modulus


def neighbour_devices(part_device, partners):
    count = part_device.shape[0]
    ids = jnp.arange(count, dtype=jnp.int32)
    hit = part_device[None, :] == ids[:, None]
    place = jnp.sum(jnp.where(hit, ids[None, :], 0), axis=1)
    upper = place % 2 == 0
    up_dev = jnp.where(upper, partners[0], partners[1])
    low_dev = jnp.where(upper, partners[1], partners[0])
    return up_dev, low_dev


def exchange(first, last, up_dev, low_dev):
    col = lax.axis_index("col")
    grp = lax.axis_index("grp")
    me = col * GROUP + grp
    cols = up_dev.shape[0] // GROUP
    rows = first.shape[0]
    pack = jnp.concatenate([first, last], axis=0)[None]
    held = lax.all_gather(pack, "grp", axis=0, tiled=True)
    pick = (jnp.arange(GROUP, dtype=jnp.int32) == grp)[None, :]
    t_up = jnp.sum(jnp.where(pick, up_dev.reshape(cols, GROUP), 0), axis=1)
    t_low = jnp.sum(jnp.where(pick, low_dev.reshape(cols, GROUP), 0), axis=1)
    up_at = jnp.where(t_up // GROUP == col, t_up % GROUP, -1)[:, None, None]
    low_at = jnp.where(t_low // GROUP == col, t_low % GROUP, -1)[:, None, None]
    slot_shape = (cols, 2 * rows) + first.shape[1:]
    from_up = jnp.zeros(slot_shape, jnp.float32)
    from_low = jnp.zeros(slot_shape, jnp.float32)
    for k in range(GROUP):
        from_up = jnp.where(up_at == k, held[k][None], from_up)
        from_low = jnp.where(low_at == k, held[k][None], from_low)
    half_row = lax.broadcasted_iota(jnp.int32, slot_shape, 1)
    slots = jnp.where(half_row < rows, from_up, from_low)
    got = lax.all_to_all(slots, "col", 0, 0, tiled=True)
    my_up = up_dev[me]
    my_low = low_dev[me]
    above = lax.dynamic_index_in_dim(got, my_up // GROUP, axis=0, keepdims=False)[:rows]
    below = lax.dynamic_index_in_dim(got, my_low // GROUP, axis=0, keepdims=False)[rows:]
    above = jnp.where(my_up != me, above, jnp.float32(0.0))
    below = jnp.where(my_low != me, below, jnp.float32(0.0))
    return below, above


def on_device(loads, modal_disp, material, moduli, part_device, partners, low_bound, high_bound):
    up_dev, low_dev = neighbour_devices(part_device, partners)
    samples, _, depth, rows_y, width = loads.shape
    ids_orig = material.astype(jnp.float32)
    plane = (samples, 3, rows_y, width)
    plane_size = samples * 3 * rows_y * width
    mod_size = rows_y * width

    def pack(md_rows, load_rows):
        parts = [modal_disp[:, :, r].reshape(-1) for r in md_rows]
        parts += [loads[:, :, r].reshape(-1) for r in load_rows]
        parts += [ids_orig[r].reshape(-1) for r in md_rows]
        flat = jnp.concatenate(parts)
        return flat.reshape(flat.shape[0] // width, width)

    first = pack((0, 1, 2), (0, 1))
    last = pack((depth - 3, depth - 2, depth - 1), (depth - 2, depth - 1))
    below, above = exchange(first, last, up_dev, low_dev)
    below = below.reshape(-1)
    above = above.reshape(-1)

    def planes_of(got, count, start, size, shape):
        return [got[start + i * size : start + (i + 1) * size].reshape(shape) for i in range(count)]

    md_below = planes_of(below, 3, 0, plane_size, plane)
    md_above = planes_of(above, 3, 0, plane_size, plane)
    ld_below = planes_of(below, 2, 3 * plane_size, plane_size, plane)
    ld_above = planes_of(above, 2, 3 * plane_size, plane_size, plane)
    ids_below = planes_of(below, 3, 5 * plane_size, mod_size, (rows_y, width))
    ids_above = planes_of(above, 3, 5 * plane_size, mod_size, (rows_y, width))

    loads = jnp.transpose(loads, (0, 1, 3, 2, 4))
    modal_disp = jnp.transpose(modal_disp, (0, 1, 3, 2, 4))
    ids = jnp.transpose(ids_orig, (1, 0, 2))

    mine = jnp.arange(up_dev.shape[0], dtype=jnp.int32) == col_grp_index()
    low_on = jnp.sum(jnp.where(mine, low_dev, 0)) != col_grp_index()
    up_on = jnp.sum(jnp.where(mine, up_dev, 0)) != col_grp_index()

    theta = (high_bound[0] + low_bound[0]) / 2.0
    half = (high_bound[0] - low_bound[0]) / 2.0
    sigma = theta / half
    rho0 = 1.0 / sigma
    rho1 = 1.0 / (2.0 * sigma - rho0)
    scalars = jnp.stack([theta, rho1 * rho0, 2.0 * rho1 / half]).astype(jnp.float32)

    def chain(md, ld, material_ids, masks):
        return run_chain(scalars, moduli, masks, md, ld, material_ids)

    disp_local, res_local = chain(modal_disp, loads, ids, jnp.ones((3, depth, width), jnp.float32))

    reach = 3
    margin = 2 * reach
    pad_rows = (-(2 * reach + 2 * margin)) % 8

    def window(own, lower, upper, axis):
        index = [slice(None)] * own.ndim
        index[axis] = slice(0, margin)
        own_head = own[tuple(index)]
        index[axis] = slice(depth - margin, depth)
        own_tail = own[tuple(index)]
        zero_shape = list(own.shape)
        zero_shape[axis] = pad_rows
        return jnp.concatenate(
            [
                jnp.stack(list(lower), axis=axis),
                own_head,
                own_tail,
                jnp.stack(list(upper), axis=axis),
                jnp.zeros(zero_shape, jnp.float32),
            ],
            axis=axis,
        )

    md_win = window(modal_disp, md_below, md_above, 3)
    ld_zero = jnp.zeros(plane, jnp.float32)
    ld_win = window(loads, [ld_zero] + ld_below, ld_above + [ld_zero], 3)
    ids_win = window(ids, ids_below, ids_above, 1)
    logical = jnp.concatenate(
        [
            jnp.arange(-reach, margin, dtype=jnp.int32),
            jnp.arange(depth - margin, depth + reach, dtype=jnp.int32),
            jnp.full((pad_rows,), depth + 8, dtype=jnp.int32),
        ]
    )

    def valid(reach):
        keep = (logical >= 0) & (logical < depth)
        keep = keep | (low_on & (logical >= -reach) & (logical < 0))
        keep = keep | (up_on & (logical >= depth) & (logical < depth + reach))
        return jnp.broadcast_to(keep.astype(jnp.float32)[:, None], (logical.shape[0], width))

    masks = jnp.stack([valid(2), valid(1), valid(3)], axis=0)
    disp_win, res_win = chain(md_win, ld_win, ids_win, masks)

    def patch(out, win):
        out = lax.dynamic_update_slice_in_dim(out, win[:, :, :, reach : 2 * reach], 0, axis=3)
        out = lax.dynamic_update_slice_in_dim(
            out, win[:, :, :, reach + 2 * margin - reach : reach + 2 * margin], depth - reach, axis=3
        )
        return jnp.transpose(out, (0, 1, 3, 2, 4))

    return (patch(disp_local, disp_win), patch(res_local, res_win))


def col_grp_index():
    return lax.axis_index("col") * GROUP + lax.axis_index("grp")


def solution(mesh):
    devices = mesh.devices.reshape(-1)
    grid = Mesh(devices.reshape(devices.size // GROUP, GROUP), ("col", "grp"))
    slab = ("col", "grp")
    in_specs = (
        P(None, None, slab, None, None),
        P(None, None, slab, None, None),
        P(slab, None, None),
        P(),
        P(),
        P(),
        P(),
        P(),
    )
    out_specs = (P(None, None, slab, None, None), P(None, None, slab, None, None))
    return jax.shard_map(
        on_device, mesh=grid, in_specs=in_specs, out_specs=out_specs, check_vma=False
    )
```
